32 devices in a mesh: dp: 4 (over x, core), seq: 8 (over z, y).
Axes of the slice: x: 2, y: 2, z: 4, core: 2. Of those that a mesh axis runs over, the one named last changes fastest.
Arguments:
- inputs: bfloat16 [2, 4, 1024, 768], P(None, 'dp', 'seq'), may hold values from -6 to 6
- cotangent: bfloat16 [2, 4, 1024, 768], P(None, 'dp', 'seq'), may hold values from -6 to 6
- bounds: int32 [2, 4, 2, 2], P(None, 'dp'), may hold values from 0 to 1024, as said below
- ln1_gain: bfloat16 [768], P(('dp', 'seq')), may hold values from 0.5 to 1.5
- ln1_bias: bfloat16 [768], P(('dp', 'seq')), may hold values from -1 to 1
- w_qkv: bfloat16 [768, 2304], P(('dp', 'seq')), may hold values from -0.21875 to 0.21875
- b_query: bfloat16 [768], P(('dp', 'seq')), may hold values from -1.5 to 1.5
- b_value: bfloat16 [768], P(('dp', 'seq')), may hold values from -1.5 to 1.5
- w_out: bfloat16 [768, 768], P(('dp', 'seq')), may hold values from -1.25 to 1.25
- b_out: bfloat16 [768], P(('dp', 'seq')), may hold values from -1.5 to 1.5
- ln2_gain: bfloat16 [768], P(('dp', 'seq')), may hold values from 0.5 to 1.5
- ln2_bias: bfloat16 [768], P(('dp', 'seq')), may hold values from -1 to 1
- w_up: bfloat16 [768, 3072], P(('dp', 'seq')), may hold values from -0.21875 to 0.21875
- b_up: bfloat16 [3072], P(('dp', 'seq')), may hold values from -1.5 to 1.5
- w_down: bfloat16 [3072, 768], P(('dp', 'seq')), may hold values from -0.109375 to 0.109375
- b_down: bfloat16 [768], P(('dp', 'seq')), may hold values from -1.5 to 1.5
Outputs:
- outputs: bfloat16 [2, 4, 1024, 768], P(None, 'dp', 'seq')
- input_grad: bfloat16 [2, 4, 1024, 768], P(None, 'dp', 'seq')
- grad_ln1_gain: float32 [768], P(('dp', 'seq'))
- grad_ln1_bias: float32 [768], P(('dp', 'seq'))
- grad_w_qkv: float32 [768, 2304], P(('dp', 'seq'))
- grad_b_query: float32 [768], P(('dp', 'seq'))
- grad_b_value: float32 [768], P(('dp', 'seq'))
- grad_w_out: float32 [768, 768], P(('dp', 'seq'))
- grad_b_out: float32 [768], P(('dp', 'seq'))
- grad_ln2_gain: float32 [768], P(('dp', 'seq'))
- grad_ln2_bias: float32 [768], P(('dp', 'seq'))
- grad_w_up: float32 [768, 3072], P(('dp', 'seq'))
- grad_b_up: float32 [3072], P(('dp', 'seq'))
- grad_w_down: float32 [3072, 768], P(('dp', 'seq'))
- grad_b_down: float32 [768], P(('dp', 'seq'))
The draws below stay inside these ranges and needn't reach their ends.
Inputs may be any that keep to these rules, and one draw needn't show every extreme that they name: `bounds`: for each sequence, 2 picture pieces [start, end) of exactly 256 rows each, in increasing order and not intersecting.
All inputs are finite; a program needn't handle non-finite values.
Results may differ from the reference program's by a relative error of at most 0.02.
Values may be sent and summed in bfloat16 or wider, within the bound.
No kernel may reach another device: no remote copies, remote signals or barrier semaphores. Data moves between devices by JAX's collectives and lax.ppermute only.
A program may use at most 256 MiB of HBM per device.

```python
import math
import jax
import jax.numpy as jnp
from jax import lax

D = 768
HEADS = 12
HEAD = 64
FF = 3072
MICRO = 2
PATCH = 256
BATCH = 4
L = 1024
PIECES = 2


def draw_bounds(key, part):
    spare_rows = L - PIECES * PATCH
    subkeys = jax.random.split(key, MICRO * BATCH)

    def one_seq(subkey):
        shuffled = jax.random.permutation(subkey, spare_rows + PIECES)[:PIECES]
        chosen = jnp.sort(shuffled)
        piece_rank = jnp.arange(PIECES, dtype=jnp.int32)
        starts = chosen.astype(jnp.int32) - piece_rank + piece_rank * PATCH
        return jnp.stack([starts, starts + PATCH], axis=-1)
    return jax.vmap(one_seq)(subkeys).reshape(MICRO, BATCH, PIECES, 2).astype(jnp.int32)


def levels(key, dims, pieces, smallest, top_value):
    gain, own = 1.0, jax.random.fold_in(key, 6)
    for axis_at, shards_of in pieces:
        heights = jnp.exp(jax.random.uniform(jax.random.fold_in(own, axis_at), (shards_of,), jnp.float32, smallest / len(pieces), top_value / len(pieces)))
        gain = gain * jnp.repeat(heights, dims[axis_at] // shards_of).reshape([-1 if axis == axis_at else 1 for axis in range(len(dims))])
    return gain


def gaussian(rng, extent, scale, most, cuts=(), kind=jnp.bfloat16):
    gain = levels(rng, extent, cuts, -0.22, 0.18) if cuts else 1.0
    array = jax.random.normal(rng, extent, jnp.float32) * scale * gain
    return jnp.minimum(jnp.maximum(array, -most), most).astype(kind)


def setup_inputs(seed: int = 0) -> dict:
    splits = jax.random.split(jax.random.key(seed), 17)
    return {
        "inputs": gaussian(splits[0], (MICRO, BATCH, L, D), 1.0, 6.0, ((1, 4), (2, 8))),
        "cotangent": gaussian(splits[1], (MICRO, BATCH, L, D), 1.0, 6.0, ((1, 4), (2, 8))),
        "bounds": draw_bounds(jax.random.fold_in(splits[16], 71), 0),
        "ln1_gain": jnp.clip(1.0 + 0.1 * jax.random.normal(splits[3], (D,), jnp.float32), 0.5, 1.5).astype(jnp.bfloat16),
        "ln1_bias": gaussian(splits[4], (D,), 0.2, 1.0, ((0, 32),)),
        "w_qkv": gaussian(splits[5], (D, 3 * D), D ** -0.5, 0.21875, ((0, 32),)),
        "b_query": gaussian(splits[6], (D,), 0.3, 1.5, ((0, 32),)),
        "b_value": gaussian(splits[7], (D,), 0.3, 1.5, ((0, 32),)),
        "w_out": gaussian(splits[8], (D, D), (max(1, D * 32 // L)) ** -0.5, 1.25, ((0, 32),)),
        "b_out": gaussian(splits[9], (D,), 0.3, 1.5, ((0, 32),)),
        "ln2_gain": jnp.clip(1.0 + 0.1 * jax.random.normal(splits[10], (D,), jnp.float32), 0.5, 1.5).astype(jnp.bfloat16),
        "ln2_bias": gaussian(splits[11], (D,), 0.2, 1.0, ((0, 32),)),
        "w_up": gaussian(splits[12], (D, FF), D ** -0.5, 0.21875, ((0, 32),)),
        "b_up": gaussian(splits[13], (FF,), 0.3, 1.5, ((0, 32),)),
        "w_down": gaussian(splits[14], (FF, D), FF ** -0.5, 0.109375, ((0, 32),)),
        "b_down": gaussian(splits[15], (D,), 0.3, 1.5, ((0, 32),)),
    }


@jax.custom_vjp
def low(v):
    return lax.optimization_barrier(v.astype(jnp.bfloat16)).astype(jnp.float32)

@jax.custom_vjp
def low_back(v):
    return v

def low_keep(v):
    return (low(v), None)

def low_pass(kept, grad):
    return (grad,)

def back_keep(v):
    return (v, None)

def back_low(kept, grad):
    return (low(grad),)
low.defvjp(low_keep, low_pass)
low_back.defvjp(back_keep, back_low)
EPSILON = 1e-05

def highest(left, right):
    return jnp.dot(left, right, precision=lax.Precision.HIGHEST, preferred_element_type=jnp.float32)

def layer_norm(values, ln_gain, ln_shift):
    center = lax.optimization_barrier(jnp.mean(values, axis=-1, keepdims=True))
    centered = values - center
    spread = lax.optimization_barrier(jnp.mean(centered * centered, axis=-1, keepdims=True))
    return centered * lax.rsqrt(spread + EPSILON) * ln_gain + ln_shift

def piece_label(positions, bounds):
    inside = (positions[:, None] >= bounds[None, :, 0]) & (positions[:, None] < bounds[None, :, 1])
    labels = jnp.arange(1, bounds.shape[0] + 1, dtype=jnp.int32)
    return lax.optimization_barrier(jnp.sum(jnp.where(inside, labels[None, :], 0), axis=1)).astype(jnp.int32) - 1

def allowed_mask(query_pos, key_pos, bounds):
    query_label = piece_label(query_pos, bounds)
    key_label = piece_label(key_pos, bounds)
    causal = key_pos[None, :] <= query_pos[:, None]
    same_piece = (query_label[:, None] == key_label[None, :]) & (query_label[:, None] >= 0)
    return causal | same_piece

def attend(queries, keys_all, values_all, bounds):
    length = queries.shape[0]
    block_rows = math.gcd(length, 512)
    key_pos = jnp.arange(length, dtype=jnp.int32)
    query_heads = queries.reshape(length, HEADS, HEAD)
    key_heads = keys_all.reshape(length, HEADS, HEAD)
    value_heads = values_all.reshape(length, HEADS, HEAD)

    def one_block(first_row):
        query_rows = lax.dynamic_slice_in_dim(query_heads, first_row, block_rows, 0)
        query_pos = first_row + jnp.arange(block_rows, dtype=jnp.int32)
        scores = jnp.einsum('qhd,khd->hqk', query_rows, key_heads, precision=lax.Precision.HIGHEST) * HEAD ** (-0.5)
        scores = low_back(scores)
        allowed = allowed_mask(query_pos, key_pos, bounds)
        weights = jnp.where(allowed[None], jnp.exp(scores), 0.0)
        totals = lax.optimization_barrier(jnp.sum(weights, axis=-1))
        summed = low_back(jnp.einsum('hqk,khd->qhd', low(weights), value_heads, precision=lax.Precision.HIGHEST))
        return (summed / totals.T[:, :, None]).reshape(block_rows, HEADS * HEAD)
    starts = jnp.arange(0, length, block_rows, dtype=jnp.int32)
    return lax.map(jax.checkpoint(one_block), starts).reshape(length, HEADS * HEAD)

def forward(inputs, params, bounds):
    ln1_gain, ln1_bias, w_qkv, b_query, b_value, w_out, b_out, ln2_gain, ln2_bias, w_up, b_up, w_down, b_down = params
    width = inputs.shape[1]
    normed = low(layer_norm(inputs, ln1_gain, ln1_bias))
    projected = highest(normed, w_qkv)
    queries = low(low_back(projected[:, :width] + b_query))
    keys_all = low(low_back(projected[:, width:2 * width]))
    values_all = low(low_back(projected[:, 2 * width:] + b_value))
    attended = low(low_back(attend(queries, keys_all, values_all, bounds)))
    branch = low_back(highest(attended, w_out) + b_out)
    middle = inputs + branch
    normed_two = low(layer_norm(middle, ln2_gain, ln2_bias))
    hidden = low_back(highest(normed_two, w_up) + b_up)
    activated = low(jax.nn.gelu(hidden, approximate=False))
    mlp_out = low_back(highest(activated, w_down) + b_down)
    return middle + mlp_out

def reference(inputs, cotangent, bounds, ln1_gain, ln1_bias, w_qkv, b_query, b_value, w_out, b_out, ln2_gain, ln2_bias, w_up, b_up, w_down, b_down):
    params = tuple((tensor.astype(jnp.float32) for tensor in (ln1_gain, ln1_bias, w_qkv, b_query, b_value, w_out, b_out, ln2_gain, ln2_bias, w_up, b_up, w_down, b_down)))
    length = inputs.shape[2]
    width = inputs.shape[3]
    flat_in = inputs.reshape(-1, length, width)
    flat_cot = cotangent.reshape(-1, length, width)
    flat_bounds = bounds.reshape(-1, bounds.shape[2], 2)

    def one_sequence(running, sequence):
        seq_in, seq_cot, seq_bounds = sequence

        def closed(values, *weight_list):
            return forward(values, weight_list, seq_bounds)
        output, pullback = jax.vjp(closed, seq_in.astype(jnp.float32), *params)
        gradients = pullback(seq_cot.astype(jnp.float32))
        running = tuple((accum + gradient for accum, gradient in zip(running, gradients[1:])))
        return (running, (output.astype(jnp.bfloat16), gradients[0].astype(jnp.bfloat16)))
    zero_grads = tuple((jnp.zeros(tensor.shape, jnp.float32) for tensor in params))
    running, (outputs, input_grads) = lax.scan(one_sequence, zero_grads, (flat_in, flat_cot, flat_bounds))
    return (outputs.reshape(inputs.shape), input_grads.reshape(inputs.shape), running[0], running[1], running[2], running[3], running[4], running[5], running[6], running[7], running[8], running[9], running[10], running[11], running[12])
```

```python
from functools import partial

import jax
import jax.numpy as jnp
from jax import lax
from jax.sharding import PartitionSpec as P

HEADS = 12
HEAD = 64
EPSILON = 1e-05
ALL = ("dp", "seq")


def layer_norm(values, ln_gain, ln_shift):
    center = jnp.mean(values, axis=-1, keepdims=True)
    centered = values - center
    spread = jnp.mean(centered * centered, axis=-1, keepdims=True)
    return centered * lax.rsqrt(spread + EPSILON) * ln_gain + ln_shift


def piece_label(positions, bounds):
    inside = (positions[:, None] >= bounds[None, :, 0]) & (positions[:, None] < bounds[None, :, 1])
    labels = jnp.arange(1, bounds.shape[0] + 1, dtype=jnp.int32)
    return jnp.sum(jnp.where(inside, labels[None, :], 0), axis=1) - 1


def allowed_mask(query_pos, key_pos, bounds):
    query_label = piece_label(query_pos, bounds)
    key_label = piece_label(key_pos, bounds)
    causal = key_pos[None, :] <= query_pos[:, None]
    same_piece = (query_label[:, None] == key_label[None, :]) & (query_label[:, None] >= 0)
    return causal | same_piece


def outer_rows(left, right):
    return lax.dot_general(
        left, right, (((0,), (0,)), ((), ())), preferred_element_type=jnp.float32
    )


def times_transposed(left, right):
    return lax.dot_general(
        left, right, (((1,), (1,)), ((), ())), preferred_element_type=jnp.float32
    )


def pack_layout(width, ff):
    ratio = ff // width
    cols = [3 * width, width, ff, ff]
    offsets = [0]
    for c in cols:
        offsets.append(offsets[-1] + c)
    vec_at = offsets[-1]
    used = vec_at + 8 + ratio
    total = -(-used // 128) * 128
    return offsets, vec_at, ratio, total


def pack_params(params, width, ff):
    ln1_g, ln1_b, w_qkv, b_q, b_v, w_out, b_out, ln2_g, ln2_b, w_up, b_up, w_down, b_down = params
    offsets, vec_at, ratio, total = pack_layout(width, ff)
    rows = w_qkv.shape[0]
    vecs = [ln1_g, ln1_b, b_q, b_v, b_out, ln2_g, ln2_b, b_down]
    pieces = [w_qkv, w_out, w_up, w_down.reshape(rows, ratio * width)]
    pieces += [v.reshape(rows, 1) for v in vecs]
    pieces.append(b_up.reshape(rows, ratio))
    pad = total - (vec_at + 8 + ratio)
    if pad:
        pieces.append(jnp.zeros((rows, pad), pieces[0].dtype))
    return jnp.concatenate(pieces, axis=1)


def unpack_params(packed, width, ff):
    offsets, vec_at, ratio, total = pack_layout(width, ff)
    rows = packed.shape[0]
    w_qkv = packed[:, offsets[0] : offsets[1]]
    w_out = packed[:, offsets[1] : offsets[2]]
    w_up = packed[:, offsets[2] : offsets[3]]
    w_down = packed[:, offsets[3] : offsets[4]].reshape(rows * ratio, width)
    vecs = [packed[:, vec_at + k] for k in range(8)]
    b_up = packed[:, vec_at + 8 : vec_at + 8 + ratio].reshape(rows * ratio)
    ln1_g, ln1_b, b_q, b_v, b_out, ln2_g, ln2_b, b_down = vecs
    return (ln1_g, ln1_b, w_qkv, b_q, b_v, w_out, b_out, ln2_g, ln2_b, w_up, b_up, w_down, b_down)


def unit_bounds(bounds, unit_count, per_device):
    first = lax.axis_index("seq") * per_device
    micro = (first + jnp.arange(per_device, dtype=jnp.int32)) // HEADS
    return bounds[:, 0][micro]


def unit_masks(ubounds, length):
    pos = jnp.arange(length, dtype=jnp.int32)
    return jax.vmap(lambda b: allowed_mask(pos, pos, b))(ubounds)


def rows_to_units(x, seq_count, per_device, parts):
    micro, rows = x.shape[0], x.shape[1]
    x = jnp.transpose(x, (0, 3, 1, 2, 4)).reshape(seq_count, per_device, rows, parts, HEAD)
    x = lax.all_to_all(x, "seq", 0, 0, tiled=True)
    x = jnp.transpose(x, (1, 0, 2, 3, 4))
    return x.reshape(per_device, seq_count * rows, parts, HEAD)


def units_to_rows(x, seq_count, micro, parts):
    per_device, length = x.shape[0], x.shape[1]
    rows = length // seq_count
    x = x.reshape(per_device, seq_count, rows, parts, HEAD)
    x = jnp.transpose(x, (1, 0, 2, 3, 4))
    x = lax.all_to_all(x, "seq", 0, 0, tiled=True)
    x = x.reshape(micro, HEADS, rows, parts, HEAD)
    x = jnp.transpose(x, (0, 2, 3, 1, 4))
    return x.reshape(micro * rows, parts * HEADS * HEAD)


def unit_forward(q, k, v, allowed):
    factor = q.shape[-1] ** (-0.5)
    scores = jnp.einsum("uqd,ukd->uqk", q, k, preferred_element_type=jnp.float32) * factor
    weights = jnp.where(allowed, jnp.exp(scores), 0.0)
    totals = jnp.sum(weights, axis=-1)
    summed = jnp.einsum(
        "uqk,ukd->uqd", weights.astype(jnp.bfloat16), v, preferred_element_type=jnp.float32
    )
    return weights, totals, summed / totals[:, :, None]


def unit_backward(q, k, v, weights, totals, attended, attended_grad):
    factor = q.shape[-1] ** (-0.5)
    grad_f = attended_grad.astype(jnp.float32)
    delta = jnp.sum(grad_f * attended, axis=-1) / totals
    summed_grad = (grad_f / totals[:, :, None]).astype(jnp.bfloat16)
    products = jnp.einsum("uqd,ukd->uqk", summed_grad, v, preferred_element_type=jnp.float32)
    score_grad = (weights * (products - delta[:, :, None])).astype(jnp.bfloat16)
    q_grad = jnp.einsum("uqk,ukd->uqd", score_grad, k, preferred_element_type=jnp.float32) * factor
    k_grad = jnp.einsum("uqk,uqd->ukd", score_grad, q, preferred_element_type=jnp.float32) * factor
    v_grad = jnp.einsum(
        "uqk,uqd->ukd", weights.astype(jnp.bfloat16), summed_grad, preferred_element_type=jnp.float32
    )
    return jnp.stack([q_grad, k_grad, v_grad], axis=2).astype(jnp.bfloat16)


def fallback_attention(queries, keys, values, bounds, row_count):
    micro = bounds.shape[0]
    seq_count = lax.axis_size("seq")
    total_len = row_count * seq_count
    query_pos = lax.axis_index("seq") * row_count + jnp.arange(row_count, dtype=jnp.int32)
    key_pos = jnp.arange(total_len, dtype=jnp.int32)
    saved = []
    attended_all = []
    for m in range(micro):
        sl = slice(m * row_count, (m + 1) * row_count)
        qh = queries[sl].reshape(row_count, HEADS, HEAD)
        k_all = lax.all_gather(keys[sl], "seq", axis=0, tiled=True).reshape(total_len, HEADS, HEAD)
        v_all = lax.all_gather(values[sl], "seq", axis=0, tiled=True).reshape(total_len, HEADS, HEAD)
        allowed = allowed_mask(query_pos, key_pos, bounds[m, 0])
        scores = jnp.einsum("rhd,khd->hrk", qh, k_all, preferred_element_type=jnp.float32) * HEAD ** (-0.5)
        weights = jnp.where(allowed[None], jnp.exp(scores), 0.0)
        totals = jnp.sum(weights, axis=-1)
        summed = jnp.einsum(
            "hrk,khd->rhd", weights.astype(jnp.bfloat16), v_all, preferred_element_type=jnp.float32
        )
        attended = summed / totals.T[:, :, None]
        saved.append((qh, k_all, v_all, weights, totals, attended))
        attended_all.append(attended.reshape(row_count, HEADS * HEAD))
    return jnp.concatenate(attended_all, axis=0), saved


def fallback_attention_backward(saved, attended_grad, row_count):
    factor = HEAD ** (-0.5)
    proj = []
    for m, (qh, k_all, v_all, weights, totals, attended) in enumerate(saved):
        grad = attended_grad[m * row_count : (m + 1) * row_count].astype(jnp.float32)
        grad = grad.reshape(row_count, HEADS, HEAD)
        delta = jnp.sum(grad * attended, axis=-1).T / totals
        grad_heads = (grad / totals.T[:, :, None]).astype(jnp.bfloat16)
        products = jnp.einsum("rhd,khd->hrk", grad_heads, v_all, preferred_element_type=jnp.float32)
        score_grad = (weights * (products - delta[:, :, None])).astype(jnp.bfloat16)
        q_grad = jnp.einsum("hrk,khd->rhd", score_grad, k_all, preferred_element_type=jnp.float32) * factor
        k_rows = jnp.einsum("hrk,rhd->khd", score_grad, qh, preferred_element_type=jnp.float32) * factor
        v_rows = jnp.einsum(
            "hrk,rhd->khd", weights.astype(jnp.bfloat16), grad_heads, preferred_element_type=jnp.float32
        )
        width = HEADS * HEAD
        k_own = lax.psum_scatter(
            k_rows.reshape(-1, width).astype(jnp.bfloat16), "seq", scatter_dimension=0, tiled=True
        )
        v_own = lax.psum_scatter(
            v_rows.reshape(-1, width).astype(jnp.bfloat16), "seq", scatter_dimension=0, tiled=True
        )
        proj.append(
            jnp.concatenate(
                [q_grad.reshape(row_count, width).astype(jnp.bfloat16), k_own, v_own], axis=1
            )
        )
    return jnp.concatenate(proj, axis=0)


def body(inputs, cotangent, bounds, *shards):
    micro = inputs.shape[0]
    row_count = inputs.shape[2]
    width = inputs.shape[3]
    ff = shards[9].shape[1]
    rows = micro * row_count
    seq_count = lax.axis_size("seq")
    unit_count = micro * HEADS
    head_parallel = unit_count % seq_count == 0
    per_device = unit_count // seq_count

    packed = lax.all_gather(pack_params(shards, width, ff), ALL, axis=0, tiled=True)
    (
        gain_one,
        shift_one,
        proj_qkv,
        bias_query,
        bias_value,
        proj_out,
        bias_out,
        gain_two,
        shift_two,
        proj_up,
        bias_up,
        proj_down,
        bias_down,
    ) = unpack_params(packed, width, ff)

    seq_in = inputs[:, 0].reshape(rows, width).astype(jnp.float32)
    normed_f, norm_one_back = jax.vjp(
        layer_norm, seq_in, gain_one.astype(jnp.float32), shift_one.astype(jnp.float32)
    )
    normed = normed_f.astype(jnp.bfloat16)
    projected = jnp.dot(normed, proj_qkv, preferred_element_type=jnp.float32)
    queries = (projected[:, :width] + bias_query.astype(jnp.float32)).astype(jnp.bfloat16)
    keys_now = projected[:, width : 2 * width].astype(jnp.bfloat16)
    values_now = (projected[:, 2 * width :] + bias_value.astype(jnp.float32)).astype(jnp.bfloat16)

    if head_parallel:
        qkv_rows = jnp.concatenate([queries, keys_now, values_now], axis=1)
        qkv_units = rows_to_units(
            qkv_rows.reshape(micro, row_count, 3, HEADS, HEAD), seq_count, per_device, 3
        )
        uq, uk, uv = qkv_units[:, :, 0], qkv_units[:, :, 1], qkv_units[:, :, 2]
        allowed = unit_masks(unit_bounds(bounds, unit_count, per_device), seq_count * row_count)
        weights, totals, attended_u = unit_forward(uq, uk, uv, allowed)
        attended_b = units_to_rows(
            attended_u.astype(jnp.bfloat16)[:, :, None], seq_count, micro, 1
        )
    else:
        attended, saved = fallback_attention(queries, keys_now, values_now, bounds, row_count)
        attended_b = attended.astype(jnp.bfloat16)

    branch = jnp.dot(attended_b, proj_out, preferred_element_type=jnp.float32) + bias_out.astype(
        jnp.float32
    )
    middle = seq_in + branch
    normed_two_f, norm_two_back = jax.vjp(
        layer_norm, middle, gain_two.astype(jnp.float32), shift_two.astype(jnp.float32)
    )
    normed_two = normed_two_f.astype(jnp.bfloat16)
    hidden = jnp.dot(normed_two, proj_up, preferred_element_type=jnp.float32) + bias_up.astype(
        jnp.float32
    )
    activated_f, gelu_back = jax.vjp(partial(jax.nn.gelu, approximate=False), hidden)
    activated = activated_f.astype(jnp.bfloat16)
    mlp_out = jnp.dot(activated, proj_down, preferred_element_type=jnp.float32) + bias_down.astype(
        jnp.float32
    )
    outputs = (middle + mlp_out).astype(jnp.bfloat16)

    out_grad = cotangent[:, 0].reshape(rows, width)
    out_grad_f = out_grad.astype(jnp.float32)
    grad_down = outer_rows(activated, out_grad)
    grad_bias_down = jnp.sum(out_grad_f, axis=0)
    act_grad = times_transposed(out_grad, proj_down)
    (hidden_grad,) = gelu_back(act_grad)
    hidden_grad_b = hidden_grad.astype(jnp.bfloat16)
    grad_up = outer_rows(normed_two, hidden_grad_b)
    grad_bias_up = jnp.sum(hidden_grad_b.astype(jnp.float32), axis=0)
    normed_two_grad = times_transposed(hidden_grad_b, proj_up)
    middle_ln_grad, grad_gain_two, grad_shift_two = norm_two_back(normed_two_grad)
    middle_grad = out_grad_f + middle_ln_grad
    branch_grad = middle_grad.astype(jnp.bfloat16)
    grad_out = outer_rows(attended_b, branch_grad)
    grad_bias_out = jnp.sum(branch_grad.astype(jnp.float32), axis=0)
    attended_grad = times_transposed(branch_grad, proj_out).astype(jnp.bfloat16)

    if head_parallel:
        grad_units = rows_to_units(
            attended_grad.reshape(micro, row_count, 1, HEADS, HEAD), seq_count, per_device, 1
        )[:, :, 0]
        qkv_grad_u = unit_backward(uq, uk, uv, weights, totals, attended_u, grad_units)
        proj_grad = units_to_rows(qkv_grad_u, seq_count, micro, 3)
    else:
        proj_grad = fallback_attention_backward(saved, attended_grad, row_count)

    grad_qkv = outer_rows(normed, proj_grad)
    grad_bias_query = jnp.sum(proj_grad[:, :width].astype(jnp.float32), axis=0)
    grad_bias_value = jnp.sum(proj_grad[:, 2 * width :].astype(jnp.float32), axis=0)
    normed_grad = times_transposed(proj_grad, proj_qkv)
    input_ln_grad, grad_gain_one, grad_shift_one = norm_one_back(normed_grad)
    input_grads = (middle_grad + input_ln_grad).astype(jnp.bfloat16)

    grads = (
        grad_gain_one,
        grad_shift_one,
        grad_qkv,
        grad_bias_query,
        grad_bias_value,
        grad_out,
        grad_bias_out,
        grad_gain_two,
        grad_shift_two,
        grad_up,
        grad_bias_up,
        grad_down,
        grad_bias_down,
    )
    packed_grads = pack_params(tuple(g.astype(jnp.bfloat16) for g in grads), width, ff)
    reduced = lax.psum_scatter(packed_grads, ALL, scatter_dimension=0, tiled=True)
    reduced = tuple(g.astype(jnp.float32) for g in unpack_params(reduced, width, ff))
    return (
        outputs.reshape(micro, 1, row_count, width),
        input_grads.reshape(micro, 1, row_count, width),
    ) + reduced


def solution(mesh):
    vec = P(ALL)
    mat = P(ALL, None)
    param_specs = (vec, vec, mat, vec, vec, mat, vec, vec, vec, mat, vec, mat, vec)
    return jax.shard_map(
        body,
        mesh=mesh,
        in_specs=(P(None, "dp", "seq", None), P(None, "dp", "seq", None), P(None, "dp", None, None))
        + param_specs,
        out_specs=(P(None, "dp", "seq", None), P(None, "dp", "seq", None)) + param_specs,
        check_vma=False,
    )
```

```python
from functools import partial

import jax
import jax.numpy as jnp
from jax import lax
from jax.sharding import PartitionSpec as P

HEADS = 12
HEAD = 64
EPSILON = 1e-05
ALL = ("dp", "seq")


def layer_norm(values, ln_gain, ln_shift):
    center = jnp.mean(values, axis=-1, keepdims=True)
    centered = values - center
    spread = jnp.mean(centered * centered, axis=-1, keepdims=True)
    return centered * lax.rsqrt(spread + EPSILON) * ln_gain + ln_shift


def piece_label(positions, bounds):
    inside = (positions[:, None] >= bounds[None, :, 0]) & (positions[:, None] < bounds[None, :, 1])
    labels = jnp.arange(1, bounds.shape[0] + 1, dtype=jnp.int32)
    return jnp.sum(jnp.where(inside, labels[None, :], 0), axis=1) - 1


def allowed_mask(query_pos, key_pos, bounds):
    query_label = piece_label(query_pos, bounds)
    key_label = piece_label(key_pos, bounds)
    causal = key_pos[None, :] <= query_pos[:, None]
    same_piece = (query_label[:, None] == key_label[None, :]) & (query_label[:, None] >= 0)
    return causal | same_piece


def outer_rows(left, right):
    return lax.dot_general(
        left, right, (((0,), (0,)), ((), ())), preferred_element_type=jnp.float32
    )


def times_transposed(left, right):
    return lax.dot_general(
        left, right, (((1,), (1,)), ((), ())), preferred_element_type=jnp.float32
    )


def route_orders(dp_size, seq_size):
    nbits = (dp_size * seq_size).bit_length() - 1
    if (dp_size, seq_size) == (4, 8):
        return [(3, 4, 0, 1, 2), (3, 0, 1, 4, 2), (3, 1, 4, 0, 2)]
    core = (seq_size.bit_length() - 1) if dp_size > 1 else None
    others = [b for b in range(nbits) if b != core]
    head = [core] if core is not None else []
    return [tuple(head + others[i:] + others[:i]) for i in range(3)]


def split_routes(widths, routes, grain=128):
    total = sum(widths)
    target = -(-total // (routes * grain)) * grain
    segs = [[] for _ in range(routes)]
    pos = 0
    for i, w in enumerate(widths):
        c = 0
        while c < w:
            route = min(pos // target, routes - 1)
            stop = (route + 1) * target if route < routes - 1 else total
            take = min(w - c, stop - pos)
            segs[route].append((i, c, c + take))
            c += take
            pos += take
    return segs


def partner_pairs(count, bit):
    return [(i, i ^ (1 << bit)) for i in range(count)]


def gather_params(arrays, orders, count, me):
    nbits = count.bit_length() - 1
    rows = arrays[0].shape[0]
    segs = split_routes([a.shape[1] for a in arrays], len(orders))
    pieces = {}
    for route, order in zip(segs, orders):
        if not route:
            continue
        xs = [arrays[i][:, c0:c1] for i, c0, c1 in route]
        for b in reversed(order):
            got = lax.ppermute(xs, ALL, partner_pairs(count, b))
            xs = [jnp.stack([x, g]) for x, g in zip(xs, got)]
        idx = jnp.arange(count, dtype=jnp.int32)
        rel = jnp.zeros((count,), jnp.int32)
        for j, b in enumerate(order):
            rel = rel + ((((idx >> b) & 1) ^ ((me >> b) & 1)) << (nbits - 1 - j))
        for (i, c0, c1), x in zip(route, xs):
            x = jnp.take(x.reshape(count, rows, c1 - c0), rel, axis=0)
            pieces[(i, c0)] = x.reshape(count * rows, c1 - c0)
    out = []
    for i in range(len(arrays)):
        parts = [pieces[k] for k in sorted(k for k in pieces if k[0] == i)]
        out.append(parts[0] if len(parts) == 1 else jnp.concatenate(parts, axis=1))
    return out


def reduce_params(arrays, orders, count, me):
    nbits = count.bit_length() - 1
    rows = arrays[0].shape[0] // count
    segs = split_routes([a.shape[1] for a in arrays], len(orders))
    pieces = {}
    for route, order in zip(segs, orders):
        if not route:
            continue
        xs = [arrays[i][:, c0:c1].reshape([2] * nbits + [rows, c1 - c0]) for i, c0, c1 in route]
        remaining = list(range(nbits - 1, -1, -1))
        for b in order:
            axis = remaining.index(b)
            mine = (me >> b) & 1
            keep = [lax.dynamic_index_in_dim(x, mine, axis, keepdims=False) for x in xs]
            send = [
                lax.dynamic_index_in_dim(x, 1 - mine, axis, keepdims=False).astype(jnp.bfloat16)
                for x in xs
            ]
            got = lax.ppermute(send, ALL, partner_pairs(count, b))
            xs = [k + g.astype(jnp.float32) for k, g in zip(keep, got)]
            remaining.pop(axis)
        for (i, c0, c1), x in zip(route, xs):
            pieces[(i, c0)] = x.reshape(rows, c1 - c0)
    out = []
    for i in range(len(arrays)):
        parts = [pieces[k] for k in sorted(k for k in pieces if k[0] == i)]
        out.append(parts[0] if len(parts) == 1 else jnp.concatenate(parts, axis=1))
    return out


def vector_block(vectors, rows, dtype):
    cols = [v.reshape(rows, -1).astype(dtype) for v in vectors]
    used = sum(c.shape[1] for c in cols)
    pad = -(-used // 128) * 128 - used
    if pad:
        cols.append(jnp.zeros((rows, pad), dtype))
    return jnp.concatenate(cols, axis=1)


def vector_unblock(block, sizes):
    out, at = [], 0
    rows = block.shape[0]
    for s in sizes:
        out.append(block[:, at : at + s].reshape(rows * s))
        at += s
    return out


def unit_bounds(bounds, unit_count, per_device):
    first = lax.axis_index("seq") * per_device
    micro = (first + jnp.arange(per_device, dtype=jnp.int32)) // HEADS
    return bounds[:, 0][micro]


def unit_masks(ubounds, length):
    pos = jnp.arange(length, dtype=jnp.int32)
    return jax.vmap(lambda b: allowed_mask(pos, pos, b))(ubounds)


def rows_to_units(x, seq_count, per_device, parts):
    micro, rows = x.shape[0], x.shape[1]
    x = jnp.transpose(x, (0, 3, 1, 2, 4)).reshape(seq_count, per_device, rows, parts, HEAD)
    x = lax.all_to_all(x, "seq", 0, 0, tiled=True)
    x = jnp.transpose(x, (1, 0, 2, 3, 4))
    return x.reshape(per_device, seq_count * rows, parts, HEAD)


def units_to_rows(x, seq_count, micro, parts):
    per_device, length = x.shape[0], x.shape[1]
    rows = length // seq_count
    x = x.reshape(per_device, seq_count, rows, parts, HEAD)
    x = jnp.transpose(x, (1, 0, 2, 3, 4))
    x = lax.all_to_all(x, "seq", 0, 0, tiled=True)
    x = x.reshape(micro, HEADS, rows, parts, HEAD)
    x = jnp.transpose(x, (0, 2, 3, 1, 4))
    return x.reshape(micro * rows, parts * HEADS * HEAD)


def unit_forward(q, k, v, allowed):
    factor = q.shape[-1] ** (-0.5)
    scores = jnp.einsum("uqd,ukd->uqk", q, k, preferred_element_type=jnp.float32) * factor
    weights = jnp.where(allowed, jnp.exp(scores), 0.0)
    totals = jnp.sum(weights, axis=-1)
    summed = jnp.einsum(
        "uqk,ukd->uqd", weights.astype(jnp.bfloat16), v, preferred_element_type=jnp.float32
    )
    return weights, totals, summed / totals[:, :, None]


def unit_backward(q, k, v, weights, totals, attended, attended_grad):
    factor = q.shape[-1] ** (-0.5)
    grad_f = attended_grad.astype(jnp.float32)
    delta = jnp.sum(grad_f * attended, axis=-1) / totals
    summed_grad = (grad_f / totals[:, :, None]).astype(jnp.bfloat16)
    products = jnp.einsum("uqd,ukd->uqk", summed_grad, v, preferred_element_type=jnp.float32)
    score_grad = (weights * (products - delta[:, :, None])).astype(jnp.bfloat16)
    q_grad = jnp.einsum("uqk,ukd->uqd", score_grad, k, preferred_element_type=jnp.float32) * factor
    k_grad = jnp.einsum("uqk,uqd->ukd", score_grad, q, preferred_element_type=jnp.float32) * factor
    v_grad = jnp.einsum(
        "uqk,uqd->ukd", weights.astype(jnp.bfloat16), summed_grad, preferred_element_type=jnp.float32
    )
    return jnp.stack([q_grad, k_grad, v_grad], axis=2).astype(jnp.bfloat16)


def fallback_attention(queries, keys, values, bounds, row_count):
    micro = bounds.shape[0]
    seq_count = lax.axis_size("seq")
    total_len = row_count * seq_count
    query_pos = lax.axis_index("seq") * row_count + jnp.arange(row_count, dtype=jnp.int32)
    key_pos = jnp.arange(total_len, dtype=jnp.int32)
    saved = []
    attended_all = []
    for m in range(micro):
        sl = slice(m * row_count, (m + 1) * row_count)
        qh = queries[sl].reshape(row_count, HEADS, HEAD)
        k_all = lax.all_gather(keys[sl], "seq", axis=0, tiled=True).reshape(total_len, HEADS, HEAD)
        v_all = lax.all_gather(values[sl], "seq", axis=0, tiled=True).reshape(total_len, HEADS, HEAD)
        allowed = allowed_mask(query_pos, key_pos, bounds[m, 0])
        scores = jnp.einsum("rhd,khd->hrk", qh, k_all, preferred_element_type=jnp.float32) * HEAD ** (-0.5)
        weights = jnp.where(allowed[None], jnp.exp(scores), 0.0)
        totals = jnp.sum(weights, axis=-1)
        summed = jnp.einsum(
            "hrk,khd->rhd", weights.astype(jnp.bfloat16), v_all, preferred_element_type=jnp.float32
        )
        attended = summed / totals.T[:, :, None]
        saved.append((qh, k_all, v_all, weights, totals, attended))
        attended_all.append(attended.reshape(row_count, HEADS * HEAD))
    return jnp.concatenate(attended_all, axis=0), saved


def fallback_attention_backward(saved, attended_grad, row_count):
    factor = HEAD ** (-0.5)
    proj = []
    for m, (qh, k_all, v_all, weights, totals, attended) in enumerate(saved):
        grad = attended_grad[m * row_count : (m + 1) * row_count].astype(jnp.float32)
        grad = grad.reshape(row_count, HEADS, HEAD)
        delta = jnp.sum(grad * attended, axis=-1).T / totals
        grad_heads = (grad / totals.T[:, :, None]).astype(jnp.bfloat16)
        products = jnp.einsum("rhd,khd->hrk", grad_heads, v_all, preferred_element_type=jnp.float32)
        score_grad = (weights * (products - delta[:, :, None])).astype(jnp.bfloat16)
        q_grad = jnp.einsum("hrk,khd->rhd", score_grad, k_all, preferred_element_type=jnp.float32) * factor
        k_rows = jnp.einsum("hrk,rhd->khd", score_grad, qh, preferred_element_type=jnp.float32) * factor
        v_rows = jnp.einsum(
            "hrk,rhd->khd", weights.astype(jnp.bfloat16), grad_heads, preferred_element_type=jnp.float32
        )
        width = HEADS * HEAD
        k_own = lax.psum_scatter(
            k_rows.reshape(-1, width).astype(jnp.bfloat16), "seq", scatter_dimension=0, tiled=True
        )
        v_own = lax.psum_scatter(
            v_rows.reshape(-1, width).astype(jnp.bfloat16), "seq", scatter_dimension=0, tiled=True
        )
        proj.append(
            jnp.concatenate(
                [q_grad.reshape(row_count, width).astype(jnp.bfloat16), k_own, v_own], axis=1
            )
        )
    return jnp.concatenate(proj, axis=0)


def body(inputs, cotangent, bounds, *shards):
    micro = inputs.shape[0]
    row_count = inputs.shape[2]
    width = inputs.shape[3]
    ff = shards[9].shape[1]
    rows = micro * row_count
    seq_count = lax.axis_size("seq")
    unit_count = micro * HEADS
    head_parallel = unit_count % seq_count == 0
    per_device = unit_count // seq_count

    dp_count = lax.axis_size("dp")
    count = dp_count * seq_count
    me = lax.axis_index("dp") * seq_count + lax.axis_index("seq")
    orders = route_orders(dp_count, seq_count)
    ln1_g, ln1_b, w_qkv, b_q, b_v, w_out, b_out, ln2_g, ln2_b, w_up, b_up, w_down, b_down = shards
    shard_rows = w_qkv.shape[0]
    ratio = ff // width
    vec_sizes = [1] * 8 + [ratio]
    vecs_local = vector_block(
        [ln1_g, ln1_b, b_q, b_v, b_out, ln2_g, ln2_b, b_down, b_up], shard_rows, jnp.bfloat16
    )
    proj_qkv, vecs_all = gather_params([w_qkv, vecs_local], orders, count, me)
    (
        gain_one,
        shift_one,
        bias_query,
        bias_value,
        bias_out,
        gain_two,
        shift_two,
        bias_down,
        bias_up,
    ) = vector_unblock(vecs_all, vec_sizes)
    proj_out, proj_up, down_view = gather_params(
        [w_out, w_up, w_down.reshape(shard_rows, ratio * width)], orders, count, me
    )
    proj_down = down_view.reshape(count * shard_rows * ratio, width)

    seq_in = inputs[:, 0].reshape(rows, width).astype(jnp.float32)
    normed_f, norm_one_back = jax.vjp(
        layer_norm, seq_in, gain_one.astype(jnp.float32), shift_one.astype(jnp.float32)
    )
    normed = normed_f.astype(jnp.bfloat16)
    projected = jnp.dot(normed, proj_qkv, preferred_element_type=jnp.float32)
    queries = (projected[:, :width] + bias_query.astype(jnp.float32)).astype(jnp.bfloat16)
    keys_now = projected[:, width : 2 * width].astype(jnp.bfloat16)
    values_now = (projected[:, 2 * width :] + bias_value.astype(jnp.float32)).astype(jnp.bfloat16)

    if head_parallel:
        qkv_rows = jnp.concatenate([queries, keys_now, values_now], axis=1)
        qkv_units = rows_to_units(
            qkv_rows.reshape(micro, row_count, 3, HEADS, HEAD), seq_count, per_device, 3
        )
        uq, uk, uv = qkv_units[:, :, 0], qkv_units[:, :, 1], qkv_units[:, :, 2]
        allowed = unit_masks(unit_bounds(bounds, unit_count, per_device), seq_count * row_count)
        weights, totals, attended_u = unit_forward(uq, uk, uv, allowed)
        attended_b = units_to_rows(
            attended_u.astype(jnp.bfloat16)[:, :, None], seq_count, micro, 1
        )
    else:
        attended, saved = fallback_attention(queries, keys_now, values_now, bounds, row_count)
        attended_b = attended.astype(jnp.bfloat16)

    branch = jnp.dot(attended_b, proj_out, preferred_element_type=jnp.float32) + bias_out.astype(
        jnp.float32
    )
    middle = seq_in + branch
    normed_two_f, norm_two_back = jax.vjp(
        layer_norm, middle, gain_two.astype(jnp.float32), shift_two.astype(jnp.float32)
    )
    normed_two = normed_two_f.astype(jnp.bfloat16)
    hidden = jnp.dot(normed_two, proj_up, preferred_element_type=jnp.float32) + bias_up.astype(
        jnp.float32
    )
    activated_f, gelu_back = jax.vjp(partial(jax.nn.gelu, approximate=False), hidden)
    activated = activated_f.astype(jnp.bfloat16)
    mlp_out = jnp.dot(activated, proj_down, preferred_element_type=jnp.float32) + bias_down.astype(
        jnp.float32
    )
    outputs = (middle + mlp_out).astype(jnp.bfloat16)

    out_grad = cotangent[:, 0].reshape(rows, width)
    out_grad_f = out_grad.astype(jnp.float32)
    grad_down = outer_rows(activated, out_grad)
    grad_bias_down = jnp.sum(out_grad_f, axis=0)
    act_grad = times_transposed(out_grad, proj_down)
    (hidden_grad,) = gelu_back(act_grad)
    hidden_grad_b = hidden_grad.astype(jnp.bfloat16)
    grad_up = outer_rows(normed_two, hidden_grad_b)
    grad_bias_up = jnp.sum(hidden_grad_b.astype(jnp.float32), axis=0)
    normed_two_grad = times_transposed(hidden_grad_b, proj_up)
    middle_ln_grad, grad_gain_two, grad_shift_two = norm_two_back(normed_two_grad)
    middle_grad = out_grad_f + middle_ln_grad
    branch_grad = middle_grad.astype(jnp.bfloat16)
    grad_out = outer_rows(attended_b, branch_grad)
    grad_bias_out = jnp.sum(branch_grad.astype(jnp.float32), axis=0)
    attended_grad = times_transposed(branch_grad, proj_out).astype(jnp.bfloat16)

    if head_parallel:
        grad_units = rows_to_units(
            attended_grad.reshape(micro, row_count, 1, HEADS, HEAD), seq_count, per_device, 1
        )[:, :, 0]
        qkv_grad_u = unit_backward(uq, uk, uv, weights, totals, attended_u, grad_units)
        proj_grad = units_to_rows(qkv_grad_u, seq_count, micro, 3)
    else:
        proj_grad = fallback_attention_backward(saved, attended_grad, row_count)

    grad_qkv = outer_rows(normed, proj_grad)
    grad_bias_query = jnp.sum(proj_grad[:, :width].astype(jnp.float32), axis=0)
    grad_bias_value = jnp.sum(proj_grad[:, 2 * width :].astype(jnp.float32), axis=0)
    normed_grad = times_transposed(proj_grad, proj_qkv)
    input_ln_grad, grad_gain_one, grad_shift_one = norm_one_back(normed_grad)
    input_grads = (middle_grad + input_ln_grad).astype(jnp.bfloat16)

    full_rows = count * shard_rows
    (
        red_up,
        red_down,
        red_vec_one,
    ) = reduce_params(
        [
            grad_up,
            grad_down.reshape(full_rows, ratio * width),
            vector_block(
                [grad_bias_up, grad_bias_down, grad_gain_two, grad_shift_two], full_rows, jnp.float32
            ),
        ],
        orders,
        count,
        me,
    )
    red_qkv, red_out, red_vec_two = reduce_params(
        [
            grad_qkv,
            grad_out,
            vector_block(
                [grad_gain_one, grad_shift_one, grad_bias_query, grad_bias_value, grad_bias_out],
                full_rows,
                jnp.float32,
            ),
        ],
        orders,
        count,
        me,
    )
    r_bias_up, r_bias_down, r_gain_two, r_shift_two = vector_unblock(red_vec_one, [ratio, 1, 1, 1])
    r_gain_one, r_shift_one, r_bias_query, r_bias_value, r_bias_out = vector_unblock(
        red_vec_two, [1] * 5
    )
    reduced = (
        r_gain_one,
        r_shift_one,
        red_qkv,
        r_bias_query,
        r_bias_value,
        red_out,
        r_bias_out,
        r_gain_two,
        r_shift_two,
        red_up,
        r_bias_up,
        red_down.reshape(shard_rows * ratio, width),
        r_bias_down,
    )
    return (
        outputs.reshape(micro, 1, row_count, width),
        input_grads.reshape(micro, 1, row_count, width),
    ) + reduced


def solution(mesh):
    vec = P(ALL)
    mat = P(ALL, None)
    param_specs = (vec, vec, mat, vec, vec, mat, vec, vec, vec, mat, vec, mat, vec)
    return jax.shard_map(
        body,
        mesh=mesh,
        in_specs=(P(None, "dp", "seq", None), P(None, "dp", "seq", None), P(None, "dp", None, None))
        + param_specs,
        out_specs=(P(None, "dp", "seq", None), P(None, "dp", "seq", None)) + param_specs,
        check_vma=False,
    )
```

```python
from functools import partial

import jax
import jax.numpy as jnp
from jax import lax
from jax.sharding import PartitionSpec as P

HEADS = 12
HEAD = 64
EPSILON = 1e-05
ALL = ("dp", "seq")


def layer_norm(values, ln_gain, ln_shift):
    center = jnp.mean(values, axis=-1, keepdims=True)
    centered = values - center
    spread = jnp.mean(centered * centered, axis=-1, keepdims=True)
    return centered * lax.rsqrt(spread + EPSILON) * ln_gain + ln_shift


def piece_label(positions, bounds):
    inside = (positions[:, None] >= bounds[None, :, 0]) & (positions[:, None] < bounds[None, :, 1])
    labels = jnp.arange(1, bounds.shape[0] + 1, dtype=jnp.int32)
    return jnp.sum(jnp.where(inside, labels[None, :], 0), axis=1) - 1


def allowed_mask(query_pos, key_pos, bounds):
    query_label = piece_label(query_pos, bounds)
    key_label = piece_label(key_pos, bounds)
    causal = key_pos[None, :] <= query_pos[:, None]
    same_piece = (query_label[:, None] == key_label[None, :]) & (query_label[:, None] >= 0)
    return causal | same_piece


def outer_rows(left, right):
    return lax.dot_general(
        left, right, (((0,), (0,)), ((), ())), preferred_element_type=jnp.float32
    )


def times_transposed(left, right):
    return lax.dot_general(
        left, right, (((1,), (1,)), ((), ())), preferred_element_type=jnp.float32
    )


def route_orders(dp_size, seq_size):
    nbits = (dp_size * seq_size).bit_length() - 1
    if (dp_size, seq_size) == (4, 8):
        return [(3, 4, 0, 1, 2), (3, 0, 1, 4, 2), (3, 1, 4, 0, 2)]
    core = (seq_size.bit_length() - 1) if dp_size > 1 else None
    others = [b for b in range(nbits) if b != core]
    head = [core] if core is not None else []
    return [tuple(head + others[i:] + others[:i]) for i in range(3)]


def split_routes(arrays, routes, grain=128):
    sizes = [a.shape[0] * a.shape[1] for a in arrays]
    target = sum(sizes) / routes
    segs = [[] for _ in range(routes)]
    load = 0.0
    for i, a in enumerate(arrays):
        rows, width = a.shape
        c = 0
        while c < width:
            route = min(int(load // target), routes - 1)
            if route == routes - 1:
                take = width - c
            else:
                room = (route + 1) * target - load
                take = min(width - c, max(grain, int(room // rows) // grain * grain))
            segs[route].append((i, c, c + take))
            c += take
            load += take * rows
    return segs


def partner_pairs(count, bit):
    return [(i, i ^ (1 << bit)) for i in range(count)]


def tie(values, anchor):
    if anchor is None:
        return values
    values, _ = lax.optimization_barrier((values, anchor))
    return values


def gather_params(arrays, orders, count, me, anchors=None):
    nbits = count.bit_length() - 1
    segs = split_routes(arrays, len(orders))
    pieces = {}
    for route, order in zip(segs, orders):
        if not route:
            continue
        xs = [arrays[i][:, c0:c1] for i, c0, c1 in route]
        for step, b in enumerate(reversed(order)):
            if anchors is not None:
                xs = tie(xs, anchors[step])
            got = lax.ppermute(xs, ALL, partner_pairs(count, b))
            xs = [jnp.stack([x, g]) for x, g in zip(xs, got)]
        idx = jnp.arange(count, dtype=jnp.int32)
        rel = jnp.zeros((count,), jnp.int32)
        for j, b in enumerate(order):
            rel = rel + ((((idx >> b) & 1) ^ ((me >> b) & 1)) << (nbits - 1 - j))
        for (i, c0, c1), x in zip(route, xs):
            rows = arrays[i].shape[0]
            x = jnp.take(x.reshape(count, rows, c1 - c0), rel, axis=0)
            pieces[(i, c0)] = x.reshape(count * rows, c1 - c0)
    out = []
    for i in range(len(arrays)):
        parts = [pieces[k] for k in sorted(k for k in pieces if k[0] == i)]
        out.append(parts[0] if len(parts) == 1 else jnp.concatenate(parts, axis=1))
    return out


def reduce_params(arrays, orders, count, me, anchors=None):
    nbits = count.bit_length() - 1
    segs = split_routes(arrays, len(orders))
    pieces = {}
    for route, order in zip(segs, orders):
        if not route:
            continue
        xs = []
        for i, c0, c1 in route:
            rows = arrays[i].shape[0] // count
            xs.append(arrays[i][:, c0:c1].reshape([2] * nbits + [rows, c1 - c0]))
        remaining = list(range(nbits - 1, -1, -1))
        for step, b in enumerate(order):
            if anchors is not None:
                xs = tie(xs, anchors[step])
            axis = remaining.index(b)
            mine = (me >> b) & 1
            keep = [lax.dynamic_index_in_dim(x, mine, axis, keepdims=False) for x in xs]
            send = [
                lax.dynamic_index_in_dim(x, 1 - mine, axis, keepdims=False).astype(jnp.bfloat16)
                for x in xs
            ]
            got = lax.ppermute(send, ALL, partner_pairs(count, b))
            xs = [k + g.astype(jnp.float32) for k, g in zip(keep, got)]
            remaining.pop(axis)
        for (i, c0, c1), x in zip(route, xs):
            pieces[(i, c0)] = x.reshape(arrays[i].shape[0] // count, c1 - c0)
    out = []
    for i in range(len(arrays)):
        parts = [pieces[k] for k in sorted(k for k in pieces if k[0] == i)]
        out.append(parts[0] if len(parts) == 1 else jnp.concatenate(parts, axis=1))
    return out


def vector_block(vectors, rows, dtype):
    cols = [v.reshape(rows, -1).astype(dtype) for v in vectors]
    used = sum(c.shape[1] for c in cols)
    pad = -(-used // 128) * 128 - used
    if pad:
        cols.append(jnp.zeros((rows, pad), dtype))
    return jnp.concatenate(cols, axis=1)


def vector_unblock(block, sizes):
    out, at = [], 0
    rows = block.shape[0]
    for s in sizes:
        out.append(block[:, at : at + s].reshape(rows * s))
        at += s
    return out


def unit_bounds(bounds, unit_count, per_device):
    first = lax.axis_index("seq") * per_device
    micro = (first + jnp.arange(per_device, dtype=jnp.int32)) // HEADS
    return bounds[:, 0][micro]


def unit_masks(ubounds, length):
    pos = jnp.arange(length, dtype=jnp.int32)
    return jax.vmap(lambda b: allowed_mask(pos, pos, b))(ubounds)


def rows_to_units(x, seq_count, per_device, parts):
    micro, rows = x.shape[0], x.shape[1]
    x = jnp.transpose(x, (0, 3, 1, 2, 4)).reshape(seq_count, per_device, rows, parts, HEAD)
    x = lax.all_to_all(x, "seq", 0, 0, tiled=True)
    x = jnp.transpose(x, (1, 0, 2, 3, 4))
    return x.reshape(per_device, seq_count * rows, parts, HEAD)


def units_to_rows(x, seq_count, micro, parts):
    per_device, length = x.shape[0], x.shape[1]
    rows = length // seq_count
    x = x.reshape(per_device, seq_count, rows, parts, HEAD)
    x = jnp.transpose(x, (1, 0, 2, 3, 4))
    x = lax.all_to_all(x, "seq", 0, 0, tiled=True)
    x = x.reshape(micro, HEADS, rows, parts, HEAD)
    x = jnp.transpose(x, (0, 2, 3, 1, 4))
    return x.reshape(micro * rows, parts * HEADS * HEAD)


def unit_forward(q, k, v, allowed):
    factor = q.shape[-1] ** (-0.5)
    scores = jnp.einsum("uqd,ukd->uqk", q, k, preferred_element_type=jnp.float32) * factor
    weights = jnp.where(allowed, jnp.exp(scores), 0.0)
    totals = jnp.sum(weights, axis=-1)
    summed = jnp.einsum(
        "uqk,ukd->uqd", weights.astype(jnp.bfloat16), v, preferred_element_type=jnp.float32
    )
    return weights, totals, summed / totals[:, :, None]


def unit_backward(q, k, v, weights, totals, attended, attended_grad):
    factor = q.shape[-1] ** (-0.5)
    grad_f = attended_grad.astype(jnp.float32)
    delta = jnp.sum(grad_f * attended, axis=-1) / totals
    summed_grad = (grad_f / totals[:, :, None]).astype(jnp.bfloat16)
    products = jnp.einsum("uqd,ukd->uqk", summed_grad, v, preferred_element_type=jnp.float32)
    score_grad = (weights * (products - delta[:, :, None])).astype(jnp.bfloat16)
    q_grad = jnp.einsum("uqk,ukd->uqd", score_grad, k, preferred_element_type=jnp.float32) * factor
    k_grad = jnp.einsum("uqk,uqd->ukd", score_grad, q, preferred_element_type=jnp.float32) * factor
    v_grad = jnp.einsum(
        "uqk,uqd->ukd", weights.astype(jnp.bfloat16), summed_grad, preferred_element_type=jnp.float32
    )
    return jnp.stack([q_grad, k_grad, v_grad], axis=2).astype(jnp.bfloat16)


def fallback_attention(queries, keys, values, bounds, row_count):
    micro = bounds.shape[0]
    seq_count = lax.axis_size("seq")
    total_len = row_count * seq_count
    query_pos = lax.axis_index("seq") * row_count + jnp.arange(row_count, dtype=jnp.int32)
    key_pos = jnp.arange(total_len, dtype=jnp.int32)
    saved = []
    attended_all = []
    for m in range(micro):
        sl = slice(m * row_count, (m + 1) * row_count)
        qh = queries[sl].reshape(row_count, HEADS, HEAD)
        k_all = lax.all_gather(keys[sl], "seq", axis=0, tiled=True).reshape(total_len, HEADS, HEAD)
        v_all = lax.all_gather(values[sl], "seq", axis=0, tiled=True).reshape(total_len, HEADS, HEAD)
        allowed = allowed_mask(query_pos, key_pos, bounds[m, 0])
        scores = jnp.einsum("rhd,khd->hrk", qh, k_all, preferred_element_type=jnp.float32) * HEAD ** (-0.5)
        weights = jnp.where(allowed[None], jnp.exp(scores), 0.0)
        totals = jnp.sum(weights, axis=-1)
        summed = jnp.einsum(
            "hrk,khd->rhd", weights.astype(jnp.bfloat16), v_all, preferred_element_type=jnp.float32
        )
        attended = summed / totals.T[:, :, None]
        saved.append((qh, k_all, v_all, weights, totals, attended))
        attended_all.append(attended.reshape(row_count, HEADS * HEAD))
    return jnp.concatenate(attended_all, axis=0), saved


def fallback_attention_backward(saved, attended_grad, row_count):
    factor = HEAD ** (-0.5)
    proj = []
    for m, (qh, k_all, v_all, weights, totals, attended) in enumerate(saved):
        grad = attended_grad[m * row_count : (m + 1) * row_count].astype(jnp.float32)
        grad = grad.reshape(row_count, HEADS, HEAD)
        delta = jnp.sum(grad * attended, axis=-1).T / totals
        grad_heads = (grad / totals.T[:, :, None]).astype(jnp.bfloat16)
        products = jnp.einsum("rhd,khd->hrk", grad_heads, v_all, preferred_element_type=jnp.float32)
        score_grad = (weights * (products - delta[:, :, None])).astype(jnp.bfloat16)
        q_grad = jnp.einsum("hrk,khd->rhd", score_grad, k_all, preferred_element_type=jnp.float32) * factor
        k_rows = jnp.einsum("hrk,rhd->khd", score_grad, qh, preferred_element_type=jnp.float32) * factor
        v_rows = jnp.einsum(
            "hrk,rhd->khd", weights.astype(jnp.bfloat16), grad_heads, preferred_element_type=jnp.float32
        )
        width = HEADS * HEAD
        k_own = lax.psum_scatter(
            k_rows.reshape(-1, width).astype(jnp.bfloat16), "seq", scatter_dimension=0, tiled=True
        )
        v_own = lax.psum_scatter(
            v_rows.reshape(-1, width).astype(jnp.bfloat16), "seq", scatter_dimension=0, tiled=True
        )
        proj.append(
            jnp.concatenate(
                [q_grad.reshape(row_count, width).astype(jnp.bfloat16), k_own, v_own], axis=1
            )
        )
    return jnp.concatenate(proj, axis=0)


def body(inputs, cotangent, bounds, *shards):
    micro = inputs.shape[0]
    row_count = inputs.shape[2]
    width = inputs.shape[3]
    ff = shards[9].shape[1]
    rows = micro * row_count
    seq_count = lax.axis_size("seq")
    unit_count = micro * HEADS
    head_parallel = unit_count % seq_count == 0
    per_device = unit_count // seq_count
    dp_count = lax.axis_size("dp")
    count = dp_count * seq_count
    me = lax.axis_index("dp") * seq_count + lax.axis_index("seq")
    orders = route_orders(dp_count, seq_count)
    steps = len(orders[0])
    ln1_g, ln1_b, w_qkv, b_q, b_v, w_out, b_out, ln2_g, ln2_b, w_up, b_up, w_down, b_down = shards
    shard_rows = w_qkv.shape[0]
    ratio = ff // width
    vec_sizes = [1] * 8 + [ratio]
    vecs_local = vector_block(
        [ln1_g, ln1_b, b_q, b_v, b_out, ln2_g, ln2_b, b_down, b_up], shard_rows, jnp.bfloat16
    )
    proj_qkv, vecs_all = gather_params([w_qkv, vecs_local], orders, count, me)
    (
        gain_one,
        shift_one,
        bias_query,
        bias_value,
        bias_out,
        gain_two,
        shift_two,
        bias_down,
        bias_up,
    ) = vector_unblock(vecs_all, vec_sizes)

    seq_in = inputs[:, 0].reshape(rows, width).astype(jnp.float32)
    normed_f, norm_one_back = jax.vjp(
        layer_norm, seq_in, gain_one.astype(jnp.float32), shift_one.astype(jnp.float32)
    )
    normed = normed_f.astype(jnp.bfloat16)
    projected = jnp.dot(normed, proj_qkv, preferred_element_type=jnp.float32)
    queries = (projected[:, :width] + bias_query.astype(jnp.float32)).astype(jnp.bfloat16)
    keys_now = projected[:, width : 2 * width].astype(jnp.bfloat16)
    values_now = (projected[:, 2 * width :] + bias_value.astype(jnp.float32)).astype(jnp.bfloat16)

    if head_parallel:
        qkv_rows = jnp.concatenate([queries, keys_now, values_now], axis=1)
        qkv_units = rows_to_units(
            qkv_rows.reshape(micro, row_count, 3, HEADS, HEAD), seq_count, per_device, 3
        )
        uq, uk, uv = qkv_units[:, :, 0], qkv_units[:, :, 1], qkv_units[:, :, 2]
        allowed = unit_masks(unit_bounds(bounds, unit_count, per_device), seq_count * row_count)
        weights, totals, attended_u = unit_forward(uq, uk, uv, allowed)
        attended_b = units_to_rows(
            attended_u.astype(jnp.bfloat16)[:, :, None], seq_count, micro, 1
        )
        forward_anchors = [projected, qkv_units, weights, attended_u, attended_u]
    else:
        attended, saved = fallback_attention(queries, keys_now, values_now, bounds, row_count)
        attended_b = attended.astype(jnp.bfloat16)
        forward_anchors = [projected] + [attended] * (steps - 1)

    proj_out, proj_up, proj_down = gather_params(
        [w_out, w_up, w_down], orders, count, me, forward_anchors[:steps]
    )

    branch = jnp.dot(attended_b, proj_out, preferred_element_type=jnp.float32) + bias_out.astype(
        jnp.float32
    )
    middle = seq_in + branch
    normed_two_f, norm_two_back = jax.vjp(
        layer_norm, middle, gain_two.astype(jnp.float32), shift_two.astype(jnp.float32)
    )
    normed_two = normed_two_f.astype(jnp.bfloat16)
    hidden = jnp.dot(normed_two, proj_up, preferred_element_type=jnp.float32) + bias_up.astype(
        jnp.float32
    )
    activated_f, gelu_back = jax.vjp(partial(jax.nn.gelu, approximate=False), hidden)
    activated = activated_f.astype(jnp.bfloat16)
    mlp_out = jnp.dot(activated, proj_down, preferred_element_type=jnp.float32) + bias_down.astype(
        jnp.float32
    )
    outputs = (middle + mlp_out).astype(jnp.bfloat16)

    out_grad = cotangent[:, 0].reshape(rows, width)
    out_grad_f = out_grad.astype(jnp.float32)
    grad_down = outer_rows(activated, out_grad)
    grad_bias_down = jnp.sum(out_grad_f, axis=0)
    act_grad = times_transposed(out_grad, proj_down)
    (hidden_grad,) = gelu_back(act_grad)
    hidden_grad_b = hidden_grad.astype(jnp.bfloat16)
    grad_up = outer_rows(normed_two, hidden_grad_b)
    grad_bias_up = jnp.sum(hidden_grad_b.astype(jnp.float32), axis=0)
    normed_two_grad = times_transposed(hidden_grad_b, proj_up)
    middle_ln_grad, grad_gain_two, grad_shift_two = norm_two_back(normed_two_grad)
    middle_grad = out_grad_f + middle_ln_grad
    branch_grad = middle_grad.astype(jnp.bfloat16)
    grad_out = outer_rows(attended_b, branch_grad)
    grad_bias_out = jnp.sum(branch_grad.astype(jnp.float32), axis=0)
    attended_grad = times_transposed(branch_grad, proj_out).astype(jnp.bfloat16)

    if head_parallel:
        grad_units = rows_to_units(
            attended_grad.reshape(micro, row_count, 1, HEADS, HEAD), seq_count, per_device, 1
        )[:, :, 0]
        qkv_grad_u = unit_backward(uq, uk, uv, weights, totals, attended_u, grad_units)
        proj_grad = units_to_rows(qkv_grad_u, seq_count, micro, 3)
        backward_anchors = [None, grad_units, qkv_grad_u, proj_grad, proj_grad]
    else:
        proj_grad = fallback_attention_backward(saved, attended_grad, row_count)
        backward_anchors = [None] + [proj_grad] * (steps - 1)

    full_rows = count * shard_rows
    red_up, red_down, red_vec_one = reduce_params(
        [
            grad_up,
            grad_down,
            vector_block(
                [grad_bias_up, grad_bias_down, grad_gain_two, grad_shift_two], full_rows, jnp.float32
            ),
        ],
        orders,
        count,
        me,
        backward_anchors[:steps],
    )

    grad_qkv = outer_rows(normed, proj_grad)
    grad_bias_query = jnp.sum(proj_grad[:, :width].astype(jnp.float32), axis=0)
    grad_bias_value = jnp.sum(proj_grad[:, 2 * width :].astype(jnp.float32), axis=0)
    normed_grad = times_transposed(proj_grad, proj_qkv)
    input_ln_grad, grad_gain_one, grad_shift_one = norm_one_back(normed_grad)
    input_grads = (middle_grad + input_ln_grad).astype(jnp.bfloat16)

    red_qkv, red_out, red_vec_two = reduce_params(
        [
            grad_qkv,
            grad_out,
            vector_block(
                [grad_gain_one, grad_shift_one, grad_bias_query, grad_bias_value, grad_bias_out],
                full_rows,
                jnp.float32,
            ),
        ],
        orders,
        count,
        me,
    )
    r_bias_up, r_bias_down, r_gain_two, r_shift_two = vector_unblock(red_vec_one, [ratio, 1, 1, 1])
    r_gain_one, r_shift_one, r_bias_query, r_bias_value, r_bias_out = vector_unblock(
        red_vec_two, [1] * 5
    )
    reduced = (
        r_gain_one,
        r_shift_one,
        red_qkv,
        r_bias_query,
        r_bias_value,
        red_out,
        r_bias_out,
        r_gain_two,
        r_shift_two,
        red_up,
        r_bias_up,
        red_down,
        r_bias_down,
    )
    return (
        outputs.reshape(micro, 1, row_count, width),
        input_grads.reshape(micro, 1, row_count, width),
    ) + reduced


def solution(mesh):
    vec = P(ALL)
    mat = P(ALL, None)
    param_specs = (vec, vec, mat, vec, vec, mat, vec, vec, vec, mat, vec, mat, vec)
    return jax.shard_map(
        body,
        mesh=mesh,
        in_specs=(P(None, "dp", "seq", None), P(None, "dp", "seq", None), P(None, "dp", None, None))
        + param_specs,
        out_specs=(P(None, "dp", "seq", None), P(None, "dp", "seq", None)) + param_specs,
        check_vma=False,
    )
```

```python
from functools import partial

import jax
import jax.numpy as jnp
from jax import lax
from jax.sharding import PartitionSpec as P

HEADS = 12
HEAD = 64
EPSILON = 1e-05
ALL = ("dp", "seq")


def layer_norm(values, ln_gain, ln_shift):
    center = jnp.mean(values, axis=-1, keepdims=True)
    centered = values - center
    spread = jnp.mean(centered * centered, axis=-1, keepdims=True)
    return centered * lax.rsqrt(spread + EPSILON) * ln_gain + ln_shift


def piece_label(positions, bounds):
    inside = (positions[:, None] >= bounds[None, :, 0]) & (positions[:, None] < bounds[None, :, 1])
    labels = jnp.arange(1, bounds.shape[0] + 1, dtype=jnp.int32)
    return jnp.sum(jnp.where(inside, labels[None, :], 0), axis=1) - 1


def allowed_mask(query_pos, key_pos, bounds):
    query_label = piece_label(query_pos, bounds)
    key_label = piece_label(key_pos, bounds)
    causal = key_pos[None, :] <= query_pos[:, None]
    same_piece = (query_label[:, None] == key_label[None, :]) & (query_label[:, None] >= 0)
    return causal | same_piece


def outer_rows(left, right):
    return lax.dot_general(
        left, right, (((0,), (0,)), ((), ())), preferred_element_type=jnp.float32
    )


def times_transposed(left, right):
    return lax.dot_general(
        left, right, (((1,), (1,)), ((), ())), preferred_element_type=jnp.float32
    )


def route_orders(dp_size, seq_size):
    nbits = (dp_size * seq_size).bit_length() - 1
    if (dp_size, seq_size) == (4, 8):
        return [(3, 4, 0, 1, 2), (3, 0, 1, 4, 2), (3, 1, 4, 0, 2)]
    core = (seq_size.bit_length() - 1) if dp_size > 1 else None
    others = [b for b in range(nbits) if b != core]
    head = [core] if core is not None else []
    return [tuple(head + others[i:] + others[:i]) for i in range(3)]


def partner_pairs(count, bit):
    return [(i, i ^ (1 << bit)) for i in range(count)]


def tie(values, anchor):
    if anchor is None:
        return values
    values, _ = lax.optimization_barrier((values, anchor))
    return values


def gather_routes(routes, orders, count, me, anchors=None):
    nbits = count.bit_length() - 1
    idx = jnp.arange(count, dtype=jnp.int32)
    out = []
    for x, order in zip(routes, orders):
        rows, cols = x.shape
        for step, b in enumerate(reversed(order)):
            if anchors is not None:
                x = tie(x, anchors[step])
            got = lax.ppermute(x, ALL, partner_pairs(count, b))
            x = jnp.stack([x, got])
        rel = jnp.zeros((count,), jnp.int32)
        for j, b in enumerate(order):
            rel = rel + ((((idx >> b) & 1) ^ ((me >> b) & 1)) << (nbits - 1 - j))
        x = jnp.take(x.reshape(count, rows, cols), rel, axis=0)
        out.append(x.reshape(count * rows, cols))
    return out


def reduce_routes(routes, orders, count, me, anchors=None):
    nbits = count.bit_length() - 1
    out = []
    for x, order in zip(routes, orders):
        rows = x.shape[0] // count
        cols = x.shape[1]
        x = x.reshape([2] * nbits + [rows, cols])
        remaining = list(range(nbits - 1, -1, -1))
        for step, b in enumerate(order):
            if anchors is not None:
                x = tie(x, anchors[step])
            axis = remaining.index(b)
            mine = (me >> b) & 1
            keep = lax.dynamic_index_in_dim(x, mine, axis, keepdims=False)
            send = lax.dynamic_index_in_dim(x, 1 - mine, axis, keepdims=False).astype(jnp.bfloat16)
            got = lax.ppermute(send, ALL, partner_pairs(count, b))
            x = keep + got.astype(jnp.float32)
            remaining.pop(axis)
        out.append(x.reshape(rows, cols))
    return out


def split_cols(x, widths):
    out, at = [], 0
    for w in widths:
        out.append(x[:, at : at + w])
        at += w
    return out


def thirds(width, grain=128):
    first = -(-width // (3 * grain)) * grain
    return [first, first, width - 2 * first]


def vector_block(vectors, rows, dtype):
    cols = [v.reshape(rows, -1).astype(dtype) for v in vectors]
    used = sum(c.shape[1] for c in cols)
    pad = -(-used // 128) * 128 - used
    if pad:
        cols.append(jnp.zeros((rows, pad), dtype))
    return jnp.concatenate(cols, axis=1)


def vector_unblock(block, sizes):
    out, at = [], 0
    rows = block.shape[0]
    for s in sizes:
        out.append(block[:, at : at + s].reshape(rows * s))
        at += s
    return out


def unit_bounds(bounds, unit_count, per_device):
    first = lax.axis_index("seq") * per_device
    micro = (first + jnp.arange(per_device, dtype=jnp.int32)) // HEADS
    return bounds[:, 0][micro]


def unit_masks(ubounds, length):
    pos = jnp.arange(length, dtype=jnp.int32)
    return jax.vmap(lambda b: allowed_mask(pos, pos, b))(ubounds)


def rows_to_units(x, seq_count, per_device, parts):
    micro, rows = x.shape[0], x.shape[1]
    x = jnp.transpose(x, (0, 3, 1, 2, 4)).reshape(seq_count, per_device, rows, parts, HEAD)
    x = lax.all_to_all(x, "seq", 0, 0, tiled=True)
    x = jnp.transpose(x, (1, 0, 2, 3, 4))
    return x.reshape(per_device, seq_count * rows, parts, HEAD)


def units_to_rows(x, seq_count, micro, parts):
    per_device, length = x.shape[0], x.shape[1]
    rows = length // seq_count
    x = x.reshape(per_device, seq_count, rows, parts, HEAD)
    x = jnp.transpose(x, (1, 0, 2, 3, 4))
    x = lax.all_to_all(x, "seq", 0, 0, tiled=True)
    x = x.reshape(micro, HEADS, rows, parts, HEAD)
    x = jnp.transpose(x, (0, 2, 3, 1, 4))
    return x.reshape(micro * rows, parts * HEADS * HEAD)


def unit_forward(q, k, v, allowed):
    factor = q.shape[-1] ** (-0.5)
    scores = jnp.einsum("uqd,ukd->uqk", q, k, preferred_element_type=jnp.float32) * factor
    weights = jnp.where(allowed, jnp.exp(scores), 0.0)
    totals = jnp.sum(weights, axis=-1)
    summed = jnp.einsum(
        "uqk,ukd->uqd", weights.astype(jnp.bfloat16), v, preferred_element_type=jnp.float32
    )
    return weights, totals, summed / totals[:, :, None]


def unit_backward(q, k, v, weights, totals, attended, attended_grad):
    factor = q.shape[-1] ** (-0.5)
    grad_f = attended_grad.astype(jnp.float32)
    delta = jnp.sum(grad_f * attended, axis=-1) / totals
    summed_grad = (grad_f / totals[:, :, None]).astype(jnp.bfloat16)
    products = jnp.einsum("uqd,ukd->uqk", summed_grad, v, preferred_element_type=jnp.float32)
    score_grad = (weights * (products - delta[:, :, None])).astype(jnp.bfloat16)
    q_grad = jnp.einsum("uqk,ukd->uqd", score_grad, k, preferred_element_type=jnp.float32) * factor
    k_grad = jnp.einsum("uqk,uqd->ukd", score_grad, q, preferred_element_type=jnp.float32) * factor
    v_grad = jnp.einsum(
        "uqk,uqd->ukd", weights.astype(jnp.bfloat16), summed_grad, preferred_element_type=jnp.float32
    )
    return jnp.stack([q_grad, k_grad, v_grad], axis=2).astype(jnp.bfloat16)


def fallback_attention(queries, keys, values, bounds, row_count):
    micro = bounds.shape[0]
    seq_count = lax.axis_size("seq")
    total_len = row_count * seq_count
    query_pos = lax.axis_index("seq") * row_count + jnp.arange(row_count, dtype=jnp.int32)
    key_pos = jnp.arange(total_len, dtype=jnp.int32)
    saved = []
    attended_all = []
    for m in range(micro):
        sl = slice(m * row_count, (m + 1) * row_count)
        qh = queries[sl].reshape(row_count, HEADS, HEAD)
        k_all = lax.all_gather(keys[sl], "seq", axis=0, tiled=True).reshape(total_len, HEADS, HEAD)
        v_all = lax.all_gather(values[sl], "seq", axis=0, tiled=True).reshape(total_len, HEADS, HEAD)
        allowed = allowed_mask(query_pos, key_pos, bounds[m, 0])
        scores = jnp.einsum("rhd,khd->hrk", qh, k_all, preferred_element_type=jnp.float32) * HEAD ** (-0.5)
        weights = jnp.where(allowed[None], jnp.exp(scores), 0.0)
        totals = jnp.sum(weights, axis=-1)
        summed = jnp.einsum(
            "hrk,khd->rhd", weights.astype(jnp.bfloat16), v_all, preferred_element_type=jnp.float32
        )
        attended = summed / totals.T[:, :, None]
        saved.append((qh, k_all, v_all, weights, totals, attended))
        attended_all.append(attended.reshape(row_count, HEADS * HEAD))
    return jnp.concatenate(attended_all, axis=0), saved


def fallback_attention_backward(saved, attended_grad, row_count):
    factor = HEAD ** (-0.5)
    proj = []
    for m, (qh, k_all, v_all, weights, totals, attended) in enumerate(saved):
        grad = attended_grad[m * row_count : (m + 1) * row_count].astype(jnp.float32)
        grad = grad.reshape(row_count, HEADS, HEAD)
        delta = jnp.sum(grad * attended, axis=-1).T / totals
        grad_heads = (grad / totals.T[:, :, None]).astype(jnp.bfloat16)
        products = jnp.einsum("rhd,khd->hrk", grad_heads, v_all, preferred_element_type=jnp.float32)
        score_grad = (weights * (products - delta[:, :, None])).astype(jnp.bfloat16)
        q_grad = jnp.einsum("hrk,khd->rhd", score_grad, k_all, preferred_element_type=jnp.float32) * factor
        k_rows = jnp.einsum("hrk,rhd->khd", score_grad, qh, preferred_element_type=jnp.float32) * factor
        v_rows = jnp.einsum(
            "hrk,rhd->khd", weights.astype(jnp.bfloat16), grad_heads, preferred_element_type=jnp.float32
        )
        width = HEADS * HEAD
        k_own = lax.psum_scatter(
            k_rows.reshape(-1, width).astype(jnp.bfloat16), "seq", scatter_dimension=0, tiled=True
        )
        v_own = lax.psum_scatter(
            v_rows.reshape(-1, width).astype(jnp.bfloat16), "seq", scatter_dimension=0, tiled=True
        )
        proj.append(
            jnp.concatenate(
                [q_grad.reshape(row_count, width).astype(jnp.bfloat16), k_own, v_own], axis=1
            )
        )
    return jnp.concatenate(proj, axis=0)


def body(inputs, cotangent, bounds, *shards):
    micro = inputs.shape[0]
    row_count = inputs.shape[2]
    width = inputs.shape[3]
    ff = shards[9].shape[1]
    rows = micro * row_count
    seq_count = lax.axis_size("seq")
    unit_count = micro * HEADS
    head_parallel = unit_count % seq_count == 0
    per_device = unit_count // seq_count
    dp_count = lax.axis_size("dp")
    count = dp_count * seq_count
    me = lax.axis_index("dp") * seq_count + lax.axis_index("seq")
    orders = route_orders(dp_count, seq_count)
    steps = len(orders[0])
    ln1_g, ln1_b, w_qkv, b_q, b_v, w_out, b_out, ln2_g, ln2_b, w_up, b_up, w_down, b_down = shards
    shard_rows = w_qkv.shape[0]
    ratio = ff // width
    vec_sizes = [1] * 8 + [ratio]
    vecs_local = vector_block(
        [ln1_g, ln1_b, b_q, b_v, b_out, ln2_g, ln2_b, b_down, b_up], shard_rows, jnp.bfloat16
    )
    qkv_cols = thirds(w_qkv.shape[1])
    qkv_parts = split_cols(w_qkv, qkv_cols)
    gathered = gather_routes(
        [qkv_parts[0], qkv_parts[1], jnp.concatenate([qkv_parts[2], vecs_local], axis=1)],
        orders,
        count,
        me,
    )
    last_qkv, vecs_all = split_cols(gathered[2], [qkv_cols[2], vecs_local.shape[1]])
    proj_qkv = jnp.concatenate([gathered[0], gathered[1], last_qkv], axis=1)
    (
        gain_one,
        shift_one,
        bias_query,
        bias_value,
        bias_out,
        gain_two,
        shift_two,
        bias_down,
        bias_up,
    ) = vector_unblock(vecs_all, vec_sizes)

    seq_in = inputs[:, 0].reshape(rows, width).astype(jnp.float32)
    normed_f, norm_one_back = jax.vjp(
        layer_norm, seq_in, gain_one.astype(jnp.float32), shift_one.astype(jnp.float32)
    )
    normed = normed_f.astype(jnp.bfloat16)
    projected = jnp.dot(normed, proj_qkv, preferred_element_type=jnp.float32)
    queries = (projected[:, :width] + bias_query.astype(jnp.float32)).astype(jnp.bfloat16)
    keys_now = projected[:, width : 2 * width].astype(jnp.bfloat16)
    values_now = (projected[:, 2 * width :] + bias_value.astype(jnp.float32)).astype(jnp.bfloat16)

    if head_parallel:
        qkv_rows = jnp.concatenate([queries, keys_now, values_now], axis=1)
        qkv_units = rows_to_units(
            qkv_rows.reshape(micro, row_count, 3, HEADS, HEAD), seq_count, per_device, 3
        )
        uq, uk, uv = qkv_units[:, :, 0], qkv_units[:, :, 1], qkv_units[:, :, 2]
        allowed = unit_masks(unit_bounds(bounds, unit_count, per_device), seq_count * row_count)
        weights, totals, attended_u = unit_forward(uq, uk, uv, allowed)
        attended_b = units_to_rows(
            attended_u.astype(jnp.bfloat16)[:, :, None], seq_count, micro, 1
        )
        forward_anchors = [projected, qkv_units, weights, attended_u, attended_u]
    else:
        attended, saved = fallback_attention(queries, keys_now, values_now, bounds, row_count)
        attended_b = attended.astype(jnp.bfloat16)
        forward_anchors = [projected] + [attended] * (steps - 1)

    proj_up, proj_down, proj_out = gather_routes(
        [w_up, w_down, w_out], orders, count, me, forward_anchors[:steps]
    )

    branch = jnp.dot(attended_b, proj_out, preferred_element_type=jnp.float32) + bias_out.astype(
        jnp.float32
    )
    middle = seq_in + branch
    normed_two_f, norm_two_back = jax.vjp(
        layer_norm, middle, gain_two.astype(jnp.float32), shift_two.astype(jnp.float32)
    )
    normed_two = normed_two_f.astype(jnp.bfloat16)
    hidden = jnp.dot(normed_two, proj_up, preferred_element_type=jnp.float32) + bias_up.astype(
        jnp.float32
    )
    activated_f, gelu_back = jax.vjp(partial(jax.nn.gelu, approximate=False), hidden)
    activated = activated_f.astype(jnp.bfloat16)
    mlp_out = jnp.dot(activated, proj_down, preferred_element_type=jnp.float32) + bias_down.astype(
        jnp.float32
    )
    outputs = (middle + mlp_out).astype(jnp.bfloat16)

    out_grad = cotangent[:, 0].reshape(rows, width)
    out_grad_f = out_grad.astype(jnp.float32)
    grad_down = outer_rows(activated, out_grad)
    grad_bias_down = jnp.sum(out_grad_f, axis=0)
    act_grad = times_transposed(out_grad, proj_down)
    (hidden_grad,) = gelu_back(act_grad)
    hidden_grad_b = hidden_grad.astype(jnp.bfloat16)
    grad_up = outer_rows(normed_two, hidden_grad_b)
    grad_bias_up = jnp.sum(hidden_grad_b.astype(jnp.float32), axis=0)
    normed_two_grad = times_transposed(hidden_grad_b, proj_up)
    middle_ln_grad, grad_gain_two, grad_shift_two = norm_two_back(normed_two_grad)
    middle_grad = out_grad_f + middle_ln_grad
    branch_grad = middle_grad.astype(jnp.bfloat16)
    grad_out = outer_rows(attended_b, branch_grad)
    grad_bias_out = jnp.sum(branch_grad.astype(jnp.float32), axis=0)
    attended_grad = times_transposed(branch_grad, proj_out).astype(jnp.bfloat16)

    if head_parallel:
        grad_units = rows_to_units(
            attended_grad.reshape(micro, row_count, 1, HEADS, HEAD), seq_count, per_device, 1
        )[:, :, 0]
        qkv_grad_u = unit_backward(uq, uk, uv, weights, totals, attended_u, grad_units)
        proj_grad = units_to_rows(qkv_grad_u, seq_count, micro, 3)
        backward_anchors = [None, grad_units, qkv_grad_u, proj_grad, proj_grad]
    else:
        proj_grad = fallback_attention_backward(saved, attended_grad, row_count)
        backward_anchors = [None] + [proj_grad] * (steps - 1)

    full_rows = count * shard_rows
    red_up, red_down, red_vec_one = reduce_routes(
        [
            grad_up,
            grad_down,
            vector_block(
                [grad_bias_up, grad_bias_down, grad_gain_two, grad_shift_two], full_rows, jnp.float32
            ),
        ],
        orders,
        count,
        me,
        backward_anchors[:steps],
    )

    grad_qkv = outer_rows(normed, proj_grad)
    grad_bias_query = jnp.sum(proj_grad[:, :width].astype(jnp.float32), axis=0)
    grad_bias_value = jnp.sum(proj_grad[:, 2 * width :].astype(jnp.float32), axis=0)
    normed_grad = times_transposed(proj_grad, proj_qkv)
    input_ln_grad, grad_gain_one, grad_shift_one = norm_one_back(normed_grad)
    input_grads = (middle_grad + input_ln_grad).astype(jnp.bfloat16)

    vec_two = vector_block(
        [grad_gain_one, grad_shift_one, grad_bias_query, grad_bias_value, grad_bias_out],
        full_rows,
        jnp.float32,
    )
    gq = split_cols(grad_qkv, qkv_cols)
    red = reduce_routes(
        [gq[0], gq[1], jnp.concatenate([gq[2], grad_out, vec_two], axis=1)], orders, count, me
    )
    red_last, red_out, red_vec_two = split_cols(red[2], [qkv_cols[2], width, vec_two.shape[1]])
    red_qkv = jnp.concatenate([red[0], red[1], red_last], axis=1)
    r_bias_up, r_bias_down, r_gain_two, r_shift_two = vector_unblock(red_vec_one, [ratio, 1, 1, 1])
    r_gain_one, r_shift_one, r_bias_query, r_bias_value, r_bias_out = vector_unblock(
        red_vec_two, [1] * 5
    )
    reduced = (
        r_gain_one,
        r_shift_one,
        red_qkv,
        r_bias_query,
        r_bias_value,
        red_out,
        r_bias_out,
        r_gain_two,
        r_shift_two,
        red_up,
        r_bias_up,
        red_down,
        r_bias_down,
    )
    return (
        outputs.reshape(micro, 1, row_count, width),
        input_grads.reshape(micro, 1, row_count, width),
    ) + reduced


def solution(mesh):
    vec = P(ALL)
    mat = P(ALL, None)
    param_specs = (vec, vec, mat, vec, vec, mat, vec, vec, vec, mat, vec, mat, vec)
    return jax.shard_map(
        body,
        mesh=mesh,
        in_specs=(P(None, "dp", "seq", None), P(None, "dp", "seq", None), P(None, "dp", None, None))
        + param_specs,
        out_specs=(P(None, "dp", "seq", None), P(None, "dp", "seq", None)) + param_specs,
        check_vma=False,
    )
```

```python
from functools import partial

import jax
import jax.numpy as jnp
from jax import lax
from jax.sharding import PartitionSpec as P

HEADS = 12
HEAD = 64
EPSILON = 1e-05
ALL = ("dp", "seq")


def layer_norm(values, ln_gain, ln_shift):
    center = jnp.mean(values, axis=-1, keepdims=True)
    centered = values - center
    spread = jnp.mean(centered * centered, axis=-1, keepdims=True)
    return centered * lax.rsqrt(spread + EPSILON) * ln_gain + ln_shift


def piece_label(positions, bounds):
    inside = (positions[:, None] >= bounds[None, :, 0]) & (positions[:, None] < bounds[None, :, 1])
    labels = jnp.arange(1, bounds.shape[0] + 1, dtype=jnp.int32)
    return jnp.sum(jnp.where(inside, labels[None, :], 0), axis=1) - 1


def allowed_mask(query_pos, key_pos, bounds):
    query_label = piece_label(query_pos, bounds)
    key_label = piece_label(key_pos, bounds)
    causal = key_pos[None, :] <= query_pos[:, None]
    same_piece = (query_label[:, None] == key_label[None, :]) & (query_label[:, None] >= 0)
    return causal | same_piece


def outer_rows(left, right):
    return lax.dot_general(
        left, right, (((0,), (0,)), ((), ())), preferred_element_type=jnp.float32
    )


def times_transposed(left, right):
    return lax.dot_general(
        left, right, (((1,), (1,)), ((), ())), preferred_element_type=jnp.float32
    )


def route_orders(dp_size, seq_size):
    nbits = (dp_size * seq_size).bit_length() - 1
    if (dp_size, seq_size) == (4, 8):
        return [(3, 4, 0, 1, 2), (3, 0, 1, 4, 2), (3, 1, 4, 0, 2)]
    core = (seq_size.bit_length() - 1) if dp_size > 1 else None
    others = [b for b in range(nbits) if b != core]
    head = [core] if core is not None else []
    return [tuple(head + others[i:] + others[:i]) for i in range(3)]


def partner_pairs(count, bit):
    return [(i, i ^ (1 << bit)) for i in range(count)]


def tie(values, anchor):
    if anchor is None:
        return values
    values, _ = lax.optimization_barrier((values, anchor))
    return values


def gather_routes(routes, orders, count, me, anchors=None):
    nbits = count.bit_length() - 1
    idx = jnp.arange(count, dtype=jnp.int32)
    out = []
    for x, order in zip(routes, orders):
        rows, cols = x.shape
        for step, b in enumerate(reversed(order)):
            if anchors is not None:
                x = tie(x, anchors[step])
            got = lax.ppermute(x, ALL, partner_pairs(count, b))
            x = jnp.stack([x, got])
        rel = jnp.zeros((count,), jnp.int32)
        for j, b in enumerate(order):
            rel = rel + ((((idx >> b) & 1) ^ ((me >> b) & 1)) << (nbits - 1 - j))
        x = jnp.take(x.reshape(count, rows, cols), rel, axis=0)
        out.append(x.reshape(count * rows, cols))
    return out


def reduce_routes(routes, orders, count, me, anchors=None):
    nbits = count.bit_length() - 1
    out = []
    for x, order in zip(routes, orders):
        rows = x.shape[0] // count
        cols = x.shape[1]
        x = x.reshape([2] * nbits + [rows, cols])
        remaining = list(range(nbits - 1, -1, -1))
        for step, b in enumerate(order):
            if anchors is not None:
                x = tie(x, anchors[step])
            axis = remaining.index(b)
            mine = (me >> b) & 1
            keep = lax.dynamic_index_in_dim(x, mine, axis, keepdims=False)
            send = lax.dynamic_index_in_dim(x, 1 - mine, axis, keepdims=False).astype(jnp.bfloat16)
            got = lax.ppermute(send, ALL, partner_pairs(count, b))
            x = keep + got.astype(jnp.float32)
            remaining.pop(axis)
        out.append(x.reshape(rows, cols))
    return out


def split_cols(x, widths):
    out, at = [], 0
    for w in widths:
        out.append(x[:, at : at + w])
        at += w
    return out


def thirds(width, grain=128):
    first = -(-width // (3 * grain)) * grain
    return [first, first, width - 2 * first]


def vector_block(vectors, rows, dtype):
    cols = [v.reshape(rows, -1).astype(dtype) for v in vectors]
    used = sum(c.shape[1] for c in cols)
    pad = -(-used // 128) * 128 - used
    if pad:
        cols.append(jnp.zeros((rows, pad), dtype))
    return jnp.concatenate(cols, axis=1)


def vector_unblock(block, sizes):
    out, at = [], 0
    rows = block.shape[0]
    for s in sizes:
        out.append(block[:, at : at + s].reshape(rows * s))
        at += s
    return out


def unit_bounds(bounds, unit_count, per_device):
    first = lax.axis_index("seq") * per_device
    micro = (first + jnp.arange(per_device, dtype=jnp.int32)) // HEADS
    return bounds[:, 0][micro]


def unit_masks(ubounds, length):
    pos = jnp.arange(length, dtype=jnp.int32)
    return jax.vmap(lambda b: allowed_mask(pos, pos, b))(ubounds)


def rows_to_units(x, seq_count, per_device, parts):
    micro, rows = x.shape[0], x.shape[1]
    x = jnp.transpose(x, (0, 3, 1, 2, 4)).reshape(seq_count, per_device, rows, parts, HEAD)
    x = lax.all_to_all(x, "seq", 0, 0, tiled=True)
    x = jnp.transpose(x, (1, 0, 2, 3, 4))
    return x.reshape(per_device, seq_count * rows, parts, HEAD)


def units_to_rows(x, seq_count, micro, parts):
    per_device, length = x.shape[0], x.shape[1]
    rows = length // seq_count
    x = x.reshape(per_device, seq_count, rows, parts, HEAD)
    x = jnp.transpose(x, (1, 0, 2, 3, 4))
    x = lax.all_to_all(x, "seq", 0, 0, tiled=True)
    x = x.reshape(micro, HEADS, rows, parts, HEAD)
    x = jnp.transpose(x, (0, 2, 3, 1, 4))
    return x.reshape(micro * rows, parts * HEADS * HEAD)


def unit_forward(q, k, v, allowed):
    factor = q.shape[-1] ** (-0.5)
    scores = jnp.einsum("uqd,ukd->uqk", q, k, preferred_element_type=jnp.float32) * factor
    weights = jnp.where(allowed, jnp.exp(scores), 0.0)
    totals = jnp.sum(weights, axis=-1)
    summed = jnp.einsum(
        "uqk,ukd->uqd", weights.astype(jnp.bfloat16), v, preferred_element_type=jnp.float32
    )
    return weights, totals, summed / totals[:, :, None]


def unit_backward(q, k, v, weights, totals, attended, attended_grad):
    factor = q.shape[-1] ** (-0.5)
    grad_f = attended_grad.astype(jnp.float32)
    delta = jnp.sum(grad_f * attended, axis=-1) / totals
    summed_grad = (grad_f / totals[:, :, None]).astype(jnp.bfloat16)
    products = jnp.einsum("uqd,ukd->uqk", summed_grad, v, preferred_element_type=jnp.float32)
    score_grad = (weights * (products - delta[:, :, None])).astype(jnp.bfloat16)
    q_grad = jnp.einsum("uqk,ukd->uqd", score_grad, k, preferred_element_type=jnp.float32) * factor
    k_grad = jnp.einsum("uqk,uqd->ukd", score_grad, q, preferred_element_type=jnp.float32) * factor
    v_grad = jnp.einsum(
        "uqk,uqd->ukd", weights.astype(jnp.bfloat16), summed_grad, preferred_element_type=jnp.float32
    )
    return jnp.stack([q_grad, k_grad, v_grad], axis=2).astype(jnp.bfloat16)


def fallback_attention(queries, keys, values, bounds, row_count):
    micro = bounds.shape[0]
    seq_count = lax.axis_size("seq")
    total_len = row_count * seq_count
    query_pos = lax.axis_index("seq") * row_count + jnp.arange(row_count, dtype=jnp.int32)
    key_pos = jnp.arange(total_len, dtype=jnp.int32)
    saved = []
    attended_all = []
    for m in range(micro):
        sl = slice(m * row_count, (m + 1) * row_count)
        qh = queries[sl].reshape(row_count, HEADS, HEAD)
        k_all = lax.all_gather(keys[sl], "seq", axis=0, tiled=True).reshape(total_len, HEADS, HEAD)
        v_all = lax.all_gather(values[sl], "seq", axis=0, tiled=True).reshape(total_len, HEADS, HEAD)
        allowed = allowed_mask(query_pos, key_pos, bounds[m, 0])
        scores = jnp.einsum("rhd,khd->hrk", qh, k_all, preferred_element_type=jnp.float32) * HEAD ** (-0.5)
        weights = jnp.where(allowed[None], jnp.exp(scores), 0.0)
        totals = jnp.sum(weights, axis=-1)
        summed = jnp.einsum(
            "hrk,khd->rhd", weights.astype(jnp.bfloat16), v_all, preferred_element_type=jnp.float32
        )
        attended = summed / totals.T[:, :, None]
        saved.append((qh, k_all, v_all, weights, totals, attended))
        attended_all.append(attended.reshape(row_count, HEADS * HEAD))
    return jnp.concatenate(attended_all, axis=0), saved


def fallback_attention_backward(saved, attended_grad, row_count):
    factor = HEAD ** (-0.5)
    proj = []
    for m, (qh, k_all, v_all, weights, totals, attended) in enumerate(saved):
        grad = attended_grad[m * row_count : (m + 1) * row_count].astype(jnp.float32)
        grad = grad.reshape(row_count, HEADS, HEAD)
        delta = jnp.sum(grad * attended, axis=-1).T / totals
        grad_heads = (grad / totals.T[:, :, None]).astype(jnp.bfloat16)
        products = jnp.einsum("rhd,khd->hrk", grad_heads, v_all, preferred_element_type=jnp.float32)
        score_grad = (weights * (products - delta[:, :, None])).astype(jnp.bfloat16)
        q_grad = jnp.einsum("hrk,khd->rhd", score_grad, k_all, preferred_element_type=jnp.float32) * factor
        k_rows = jnp.einsum("hrk,rhd->khd", score_grad, qh, preferred_element_type=jnp.float32) * factor
        v_rows = jnp.einsum(
            "hrk,rhd->khd", weights.astype(jnp.bfloat16), grad_heads, preferred_element_type=jnp.float32
        )
        width = HEADS * HEAD
        k_own = lax.psum_scatter(
            k_rows.reshape(-1, width).astype(jnp.bfloat16), "seq", scatter_dimension=0, tiled=True
        )
        v_own = lax.psum_scatter(
            v_rows.reshape(-1, width).astype(jnp.bfloat16), "seq", scatter_dimension=0, tiled=True
        )
        proj.append(
            jnp.concatenate(
                [q_grad.reshape(row_count, width).astype(jnp.bfloat16), k_own, v_own], axis=1
            )
        )
    return jnp.concatenate(proj, axis=0)


def body(inputs, cotangent, bounds, *shards):
    micro = inputs.shape[0]
    row_count = inputs.shape[2]
    width = inputs.shape[3]
    ff = shards[9].shape[1]
    rows = micro * row_count
    seq_count = lax.axis_size("seq")
    unit_count = micro * HEADS
    head_parallel = unit_count % seq_count == 0
    per_device = unit_count // seq_count
    dp_count = lax.axis_size("dp")
    count = dp_count * seq_count
    me = lax.axis_index("dp") * seq_count + lax.axis_index("seq")
    orders = route_orders(dp_count, seq_count)
    steps = len(orders[0])
    ln1_g, ln1_b, w_qkv, b_q, b_v, w_out, b_out, ln2_g, ln2_b, w_up, b_up, w_down, b_down = shards
    shard_rows = w_qkv.shape[0]
    ratio = ff // width
    vec_sizes = [1] * 8 + [ratio]
    vecs_local = vector_block(
        [ln1_g, ln1_b, b_q, b_v, b_out, ln2_g, ln2_b, b_down, b_up], shard_rows, jnp.bfloat16
    )
    qkv_cols = thirds(w_qkv.shape[1])
    qkv_parts = split_cols(w_qkv, qkv_cols)
    gathered = gather_routes(
        [qkv_parts[0], qkv_parts[1], jnp.concatenate([qkv_parts[2], vecs_local], axis=1)],
        orders,
        count,
        me,
    )
    last_qkv, vecs_all = split_cols(gathered[2], [qkv_cols[2], vecs_local.shape[1]])
    qkv_weights = [gathered[0], gathered[1], last_qkv]
    (
        gain_one,
        shift_one,
        bias_query,
        bias_value,
        bias_out,
        gain_two,
        shift_two,
        bias_down,
        bias_up,
    ) = vector_unblock(vecs_all, vec_sizes)

    seq_in = inputs[:, 0].reshape(rows, width).astype(jnp.float32)
    normed_f, norm_one_back = jax.vjp(
        layer_norm, seq_in, gain_one.astype(jnp.float32), shift_one.astype(jnp.float32)
    )
    normed = normed_f.astype(jnp.bfloat16)
    if qkv_cols == [width] * 3:
        proj_q, proj_k, proj_v = [
            jnp.dot(normed, w, preferred_element_type=jnp.float32) for w in qkv_weights
        ]
    else:
        projected = jnp.dot(
            normed, jnp.concatenate(qkv_weights, axis=1), preferred_element_type=jnp.float32
        )
        proj_q, proj_k, proj_v = split_cols(projected, [width] * 3)
    queries = (proj_q + bias_query.astype(jnp.float32)).astype(jnp.bfloat16)
    keys_now = proj_k.astype(jnp.bfloat16)
    values_now = (proj_v + bias_value.astype(jnp.float32)).astype(jnp.bfloat16)

    if head_parallel:
        qkv_rows = jnp.concatenate([queries, keys_now, values_now], axis=1)
        qkv_units = rows_to_units(
            qkv_rows.reshape(micro, row_count, 3, HEADS, HEAD), seq_count, per_device, 3
        )
        uq, uk, uv = qkv_units[:, :, 0], qkv_units[:, :, 1], qkv_units[:, :, 2]
        allowed = unit_masks(unit_bounds(bounds, unit_count, per_device), seq_count * row_count)
        weights, totals, attended_u = unit_forward(uq, uk, uv, allowed)
        attended_b = units_to_rows(
            attended_u.astype(jnp.bfloat16)[:, :, None], seq_count, micro, 1
        )
        forward_anchors = [queries, qkv_units, weights, attended_u, attended_u]
    else:
        attended, saved = fallback_attention(queries, keys_now, values_now, bounds, row_count)
        attended_b = attended.astype(jnp.bfloat16)
        forward_anchors = [queries] + [attended] * (steps - 1)

    proj_up, proj_down, proj_out = gather_routes(
        [w_up, w_down, w_out], orders, count, me, forward_anchors[:steps]
    )

    branch = jnp.dot(attended_b, proj_out, preferred_element_type=jnp.float32) + bias_out.astype(
        jnp.float32
    )
    middle = seq_in + branch
    normed_two_f, norm_two_back = jax.vjp(
        layer_norm, middle, gain_two.astype(jnp.float32), shift_two.astype(jnp.float32)
    )
    normed_two = normed_two_f.astype(jnp.bfloat16)
    hidden = jnp.dot(normed_two, proj_up, preferred_element_type=jnp.float32) + bias_up.astype(
        jnp.float32
    )
    activated_f, gelu_back = jax.vjp(partial(jax.nn.gelu, approximate=False), hidden)
    activated = activated_f.astype(jnp.bfloat16)
    mlp_out = jnp.dot(activated, proj_down, preferred_element_type=jnp.float32) + bias_down.astype(
        jnp.float32
    )
    outputs = (middle + mlp_out).astype(jnp.bfloat16)

    out_grad = cotangent[:, 0].reshape(rows, width)
    out_grad_f = out_grad.astype(jnp.float32)
    grad_down = outer_rows(activated, out_grad)
    grad_bias_down = jnp.sum(out_grad_f, axis=0)
    act_grad = times_transposed(out_grad, proj_down)
    (hidden_grad,) = gelu_back(act_grad)
    hidden_grad_b = hidden_grad.astype(jnp.bfloat16)
    grad_up = outer_rows(normed_two, hidden_grad_b)
    grad_bias_up = jnp.sum(hidden_grad_b.astype(jnp.float32), axis=0)
    normed_two_grad = times_transposed(hidden_grad_b, proj_up)
    middle_ln_grad, grad_gain_two, grad_shift_two = norm_two_back(normed_two_grad)
    middle_grad = out_grad_f + middle_ln_grad
    branch_grad = middle_grad.astype(jnp.bfloat16)
    grad_out = outer_rows(attended_b, branch_grad)
    grad_bias_out = jnp.sum(branch_grad.astype(jnp.float32), axis=0)
    attended_grad = times_transposed(branch_grad, proj_out).astype(jnp.bfloat16)

    if head_parallel:
        grad_units = rows_to_units(
            attended_grad.reshape(micro, row_count, 1, HEADS, HEAD), seq_count, per_device, 1
        )[:, :, 0]
        qkv_grad_u = unit_backward(uq, uk, uv, weights, totals, attended_u, grad_units)
        proj_grad = units_to_rows(qkv_grad_u, seq_count, micro, 3)
        backward_anchors = [None, grad_units, qkv_grad_u, proj_grad, proj_grad]
    else:
        proj_grad = fallback_attention_backward(saved, attended_grad, row_count)
        backward_anchors = [None] + [proj_grad] * (steps - 1)

    full_rows = count * shard_rows
    vec_one = vector_block(
        [grad_bias_up, grad_bias_down, grad_gain_two, grad_shift_two], full_rows, jnp.float32
    )
    red_up, red_down, red_mixed = reduce_routes(
        [grad_up, grad_down, jnp.concatenate([grad_out, vec_one], axis=1)],
        orders,
        count,
        me,
        backward_anchors[:steps],
    )
    red_out, red_vec_one = split_cols(red_mixed, [width, vec_one.shape[1]])

    grad_bias_query = jnp.sum(proj_grad[:, :width].astype(jnp.float32), axis=0)
    grad_bias_value = jnp.sum(proj_grad[:, 2 * width :].astype(jnp.float32), axis=0)
    grad_parts = split_cols(proj_grad, qkv_cols)
    grad_qkv = [outer_rows(normed, g) for g in grad_parts]
    normed_grad = times_transposed(grad_parts[0], qkv_weights[0])
    for g, w in zip(grad_parts[1:], qkv_weights[1:]):
        normed_grad = normed_grad + times_transposed(g, w)
    input_ln_grad, grad_gain_one, grad_shift_one = norm_one_back(normed_grad)
    input_grads = (middle_grad + input_ln_grad).astype(jnp.bfloat16)

    vec_two = vector_block(
        [grad_gain_one, grad_shift_one, grad_bias_query, grad_bias_value, grad_bias_out],
        full_rows,
        jnp.float32,
    )
    red = reduce_routes(
        [grad_qkv[0], grad_qkv[1], jnp.concatenate([grad_qkv[2], vec_two], axis=1)],
        orders,
        count,
        me,
    )
    red_last, red_vec_two = split_cols(red[2], [qkv_cols[2], vec_two.shape[1]])
    red_qkv = jnp.concatenate([red[0], red[1], red_last], axis=1)
    r_bias_up, r_bias_down, r_gain_two, r_shift_two = vector_unblock(red_vec_one, [ratio, 1, 1, 1])
    r_gain_one, r_shift_one, r_bias_query, r_bias_value, r_bias_out = vector_unblock(
        red_vec_two, [1] * 5
    )
    reduced = (
        r_gain_one,
        r_shift_one,
        red_qkv,
        r_bias_query,
        r_bias_value,
        red_out,
        r_bias_out,
        r_gain_two,
        r_shift_two,
        red_up,
        r_bias_up,
        red_down,
        r_bias_down,
    )
    return (
        outputs.reshape(micro, 1, row_count, width),
        input_grads.reshape(micro, 1, row_count, width),
    ) + reduced


def solution(mesh):
    vec = P(ALL)
    mat = P(ALL, None)
    param_specs = (vec, vec, mat, vec, vec, mat, vec, vec, vec, mat, vec, mat, vec)
    return jax.shard_map(
        body,
        mesh=mesh,
        in_specs=(P(None, "dp", "seq", None), P(None, "dp", "seq", None), P(None, "dp", None, None))
        + param_specs,
        out_specs=(P(None, "dp", "seq", None), P(None, "dp", "seq", None)) + param_specs,
        check_vma=False,
    )
```

```python
from functools import partial

import jax
import jax.numpy as jnp
from jax import lax
from jax.sharding import PartitionSpec as P

HEADS = 12
HEAD = 64
EPSILON = 1e-05
ALL = ("dp", "seq")


def layer_norm(values, ln_gain, ln_shift):
    center = jnp.mean(values, axis=-1, keepdims=True)
    centered = values - center
    spread = jnp.mean(centered * centered, axis=-1, keepdims=True)
    return centered * lax.rsqrt(spread + EPSILON) * ln_gain + ln_shift


def piece_label(positions, bounds):
    inside = (positions[:, None] >= bounds[None, :, 0]) & (positions[:, None] < bounds[None, :, 1])
    labels = jnp.arange(1, bounds.shape[0] + 1, dtype=jnp.int32)
    return jnp.sum(jnp.where(inside, labels[None, :], 0), axis=1) - 1


def allowed_mask(query_pos, key_pos, bounds):
    query_label = piece_label(query_pos, bounds)
    key_label = piece_label(key_pos, bounds)
    causal = key_pos[None, :] <= query_pos[:, None]
    same_piece = (query_label[:, None] == key_label[None, :]) & (query_label[:, None] >= 0)
    return causal | same_piece


def outer_rows(left, right):
    return lax.dot_general(
        left, right, (((0,), (0,)), ((), ())), preferred_element_type=jnp.float32
    )


def times_transposed(left, right):
    return lax.dot_general(
        left, right, (((1,), (1,)), ((), ())), preferred_element_type=jnp.float32
    )


def route_orders(dp_size, seq_size):
    nbits = (dp_size * seq_size).bit_length() - 1
    if (dp_size, seq_size) == (4, 8):
        return [(3, 4, 0, 1, 2), (3, 0, 1, 4, 2), (3, 1, 4, 0, 2)]
    core = (seq_size.bit_length() - 1) if dp_size > 1 else None
    others = [b for b in range(nbits) if b != core]
    head = [core] if core is not None else []
    return [tuple(head + others[i:] + others[:i]) for i in range(3)]


def partner_pairs(count, bit):
    return [(i, i ^ (1 << bit)) for i in range(count)]


def tie(values, anchor):
    if anchor is None:
        return values
    values, _ = lax.optimization_barrier((values, anchor))
    return values


def gather_routes(routes, orders, count, me, anchors=None):
    nbits = count.bit_length() - 1
    idx = jnp.arange(count, dtype=jnp.int32)
    out = []
    for x, order in zip(routes, orders):
        rows, cols = x.shape
        for step, b in enumerate(reversed(order)):
            if anchors is not None:
                x = tie(x, anchors[step])
            got = lax.ppermute(x, ALL, partner_pairs(count, b))
            x = jnp.stack([x, got])
        rel = jnp.zeros((count,), jnp.int32)
        for j, b in enumerate(order):
            rel = rel + ((((idx >> b) & 1) ^ ((me >> b) & 1)) << (nbits - 1 - j))
        x = jnp.take(x.reshape(count, rows, cols), rel, axis=0)
        out.append(x.reshape(count * rows, cols))
    return out


def reduce_routes(routes, orders, count, me, anchors=None):
    nbits = count.bit_length() - 1
    out = []
    for x, order in zip(routes, orders):
        rows = x.shape[0] // count
        cols = x.shape[1]
        x = x.reshape([2] * nbits + [rows, cols])
        remaining = list(range(nbits - 1, -1, -1))
        for step, b in enumerate(order):
            if anchors is not None:
                x = tie(x, anchors[step])
            axis = remaining.index(b)
            mine = (me >> b) & 1
            keep = lax.dynamic_index_in_dim(x, mine, axis, keepdims=False)
            send = lax.dynamic_index_in_dim(x, 1 - mine, axis, keepdims=False).astype(jnp.bfloat16)
            got = lax.ppermute(send, ALL, partner_pairs(count, b))
            x = keep + got.astype(jnp.float32)
            remaining.pop(axis)
        out.append(x.reshape(rows, cols))
    return out


def split_cols(x, widths):
    out, at = [], 0
    for w in widths:
        out.append(x[:, at : at + w])
        at += w
    return out


def thirds(width, grain=128):
    first = -(-width // (3 * grain)) * grain
    return [first, first, width - 2 * first]


def vector_block(vectors, rows, dtype):
    cols = [v.reshape(rows, -1).astype(dtype) for v in vectors]
    used = sum(c.shape[1] for c in cols)
    pad = -(-used // 128) * 128 - used
    if pad:
        cols.append(jnp.zeros((rows, pad), dtype))
    return jnp.concatenate(cols, axis=1)


def vector_unblock(block, sizes):
    out, at = [], 0
    rows = block.shape[0]
    for s in sizes:
        out.append(block[:, at : at + s].reshape(rows * s))
        at += s
    return out


def unit_bounds(bounds, unit_count, per_device):
    first = lax.axis_index("seq") * per_device
    micro = (first + jnp.arange(per_device, dtype=jnp.int32)) // HEADS
    return bounds[:, 0][micro]


def unit_masks(ubounds, length):
    pos = jnp.arange(length, dtype=jnp.int32)
    return jax.vmap(lambda b: allowed_mask(pos, pos, b))(ubounds)


def rows_to_units(x, seq_count, per_device, parts):
    micro, rows = x.shape[0], x.shape[1]
    x = jnp.transpose(x, (0, 3, 1, 2, 4)).reshape(seq_count, per_device, rows, parts, HEAD)
    x = lax.all_to_all(x, "seq", 0, 0, tiled=True)
    x = jnp.transpose(x, (1, 0, 2, 3, 4))
    return x.reshape(per_device, seq_count * rows, parts, HEAD)


def units_to_rows(x, seq_count, micro, parts):
    per_device, length = x.shape[0], x.shape[1]
    rows = length // seq_count
    x = x.reshape(per_device, seq_count, rows, parts, HEAD)
    x = jnp.transpose(x, (1, 0, 2, 3, 4))
    x = lax.all_to_all(x, "seq", 0, 0, tiled=True)
    x = x.reshape(micro, HEADS, rows, parts, HEAD)
    x = jnp.transpose(x, (0, 2, 3, 1, 4))
    return x.reshape(micro * rows, parts * HEADS * HEAD)


def unit_forward(q, k, v, allowed):
    factor = q.shape[-1] ** (-0.5)
    scores = jnp.einsum("uqd,ukd->uqk", q, k, preferred_element_type=jnp.float32) * factor
    weights = jnp.where(allowed, jnp.exp(scores), 0.0)
    totals = jnp.sum(weights, axis=-1)
    summed = jnp.einsum(
        "uqk,ukd->uqd", weights.astype(jnp.bfloat16), v, preferred_element_type=jnp.float32
    )
    return weights, totals, summed / totals[:, :, None]


def unit_backward(q, k, v, weights, totals, attended, attended_grad):
    factor = q.shape[-1] ** (-0.5)
    grad_f = attended_grad.astype(jnp.float32)
    delta = jnp.sum(grad_f * attended, axis=-1) / totals
    summed_grad = (grad_f / totals[:, :, None]).astype(jnp.bfloat16)
    products = jnp.einsum("uqd,ukd->uqk", summed_grad, v, preferred_element_type=jnp.float32)
    score_grad = (weights * (products - delta[:, :, None])).astype(jnp.bfloat16)
    q_grad = jnp.einsum("uqk,ukd->uqd", score_grad, k, preferred_element_type=jnp.float32) * factor
    k_grad = jnp.einsum("uqk,uqd->ukd", score_grad, q, preferred_element_type=jnp.float32) * factor
    v_grad = jnp.einsum(
        "uqk,uqd->ukd", weights.astype(jnp.bfloat16), summed_grad, preferred_element_type=jnp.float32
    )
    return jnp.stack([q_grad, k_grad, v_grad], axis=2).astype(jnp.bfloat16)


def fallback_attention(queries, keys, values, bounds, row_count):
    micro = bounds.shape[0]
    seq_count = lax.axis_size("seq")
    total_len = row_count * seq_count
    query_pos = lax.axis_index("seq") * row_count + jnp.arange(row_count, dtype=jnp.int32)
    key_pos = jnp.arange(total_len, dtype=jnp.int32)
    saved = []
    attended_all = []
    for m in range(micro):
        sl = slice(m * row_count, (m + 1) * row_count)
        qh = queries[sl].reshape(row_count, HEADS, HEAD)
        k_all = lax.all_gather(keys[sl], "seq", axis=0, tiled=True).reshape(total_len, HEADS, HEAD)
        v_all = lax.all_gather(values[sl], "seq", axis=0, tiled=True).reshape(total_len, HEADS, HEAD)
        allowed = allowed_mask(query_pos, key_pos, bounds[m, 0])
        scores = jnp.einsum("rhd,khd->hrk", qh, k_all, preferred_element_type=jnp.float32) * HEAD ** (-0.5)
        weights = jnp.where(allowed[None], jnp.exp(scores), 0.0)
        totals = jnp.sum(weights, axis=-1)
        summed = jnp.einsum(
            "hrk,khd->rhd", weights.astype(jnp.bfloat16), v_all, preferred_element_type=jnp.float32
        )
        attended = summed / totals.T[:, :, None]
        saved.append((qh, k_all, v_all, weights, totals, attended))
        attended_all.append(attended.reshape(row_count, HEADS * HEAD))
    return jnp.concatenate(attended_all, axis=0), saved


def fallback_attention_backward(saved, attended_grad, row_count):
    factor = HEAD ** (-0.5)
    proj = []
    for m, (qh, k_all, v_all, weights, totals, attended) in enumerate(saved):
        grad = attended_grad[m * row_count : (m + 1) * row_count].astype(jnp.float32)
        grad = grad.reshape(row_count, HEADS, HEAD)
        delta = jnp.sum(grad * attended, axis=-1).T / totals
        grad_heads = (grad / totals.T[:, :, None]).astype(jnp.bfloat16)
        products = jnp.einsum("rhd,khd->hrk", grad_heads, v_all, preferred_element_type=jnp.float32)
        score_grad = (weights * (products - delta[:, :, None])).astype(jnp.bfloat16)
        q_grad = jnp.einsum("hrk,khd->rhd", score_grad, k_all, preferred_element_type=jnp.float32) * factor
        k_rows = jnp.einsum("hrk,rhd->khd", score_grad, qh, preferred_element_type=jnp.float32) * factor
        v_rows = jnp.einsum(
            "hrk,rhd->khd", weights.astype(jnp.bfloat16), grad_heads, preferred_element_type=jnp.float32
        )
        width = HEADS * HEAD
        k_own = lax.psum_scatter(
            k_rows.reshape(-1, width).astype(jnp.bfloat16), "seq", scatter_dimension=0, tiled=True
        )
        v_own = lax.psum_scatter(
            v_rows.reshape(-1, width).astype(jnp.bfloat16), "seq", scatter_dimension=0, tiled=True
        )
        proj.append(
            jnp.concatenate(
                [q_grad.reshape(row_count, width).astype(jnp.bfloat16), k_own, v_own], axis=1
            )
        )
    return jnp.concatenate(proj, axis=0)


def body(inputs, cotangent, bounds, *shards):
    micro = inputs.shape[0]
    row_count = inputs.shape[2]
    width = inputs.shape[3]
    ff = shards[9].shape[1]
    rows = micro * row_count
    seq_count = lax.axis_size("seq")
    unit_count = micro * HEADS
    head_parallel = unit_count % seq_count == 0
    per_device = unit_count // seq_count
    dp_count = lax.axis_size("dp")
    count = dp_count * seq_count
    me = lax.axis_index("dp") * seq_count + lax.axis_index("seq")
    orders = route_orders(dp_count, seq_count)
    steps = len(orders[0])
    ln1_g, ln1_b, w_qkv, b_q, b_v, w_out, b_out, ln2_g, ln2_b, w_up, b_up, w_down, b_down = shards
    shard_rows = w_qkv.shape[0]
    ratio = ff // width
    vec_sizes = [1] * 8 + [ratio]
    vecs_local = vector_block(
        [ln1_g, ln1_b, b_q, b_v, b_out, ln2_g, ln2_b, b_down, b_up], shard_rows, jnp.bfloat16
    )
    qkv_cols = thirds(w_qkv.shape[1])
    qkv_parts = split_cols(w_qkv, qkv_cols)
    gathered = gather_routes(
        [qkv_parts[0], qkv_parts[1], jnp.concatenate([qkv_parts[2], vecs_local], axis=1)],
        orders,
        count,
        me,
    )
    last_qkv, vecs_all = split_cols(gathered[2], [qkv_cols[2], vecs_local.shape[1]])
    qkv_weights = [gathered[0], gathered[1], last_qkv]
    (
        gain_one,
        shift_one,
        bias_query,
        bias_value,
        bias_out,
        gain_two,
        shift_two,
        bias_down,
        bias_up,
    ) = vector_unblock(vecs_all, vec_sizes)

    seq_in = inputs[:, 0].reshape(rows, width).astype(jnp.float32)
    normed_f, norm_one_back = jax.vjp(
        layer_norm, seq_in, gain_one.astype(jnp.float32), shift_one.astype(jnp.float32)
    )
    normed = normed_f.astype(jnp.bfloat16)
    if qkv_cols == [width] * 3:
        proj_q, proj_k, proj_v = [
            jnp.dot(normed, w, preferred_element_type=jnp.float32) for w in qkv_weights
        ]
    else:
        projected = jnp.dot(
            normed, jnp.concatenate(qkv_weights, axis=1), preferred_element_type=jnp.float32
        )
        proj_q, proj_k, proj_v = split_cols(projected, [width] * 3)
    queries = (proj_q + bias_query.astype(jnp.float32)).astype(jnp.bfloat16)
    keys_now = proj_k.astype(jnp.bfloat16)
    values_now = (proj_v + bias_value.astype(jnp.float32)).astype(jnp.bfloat16)

    if head_parallel:
        qkv_rows = jnp.concatenate([queries, keys_now, values_now], axis=1)
        qkv_units = rows_to_units(
            qkv_rows.reshape(micro, row_count, 3, HEADS, HEAD), seq_count, per_device, 3
        )
        uq, uk, uv = qkv_units[:, :, 0], qkv_units[:, :, 1], qkv_units[:, :, 2]
        allowed = unit_masks(unit_bounds(bounds, unit_count, per_device), seq_count * row_count)
        weights, totals, attended_u = unit_forward(uq, uk, uv, allowed)
        attended_b = units_to_rows(
            attended_u.astype(jnp.bfloat16)[:, :, None], seq_count, micro, 1
        )
        forward_anchors = [normed, qkv_units, weights, attended_u, attended_u]
    else:
        attended, saved = fallback_attention(queries, keys_now, values_now, bounds, row_count)
        attended_b = attended.astype(jnp.bfloat16)
        forward_anchors = [queries] + [attended] * (steps - 1)

    proj_up, proj_down, proj_out = gather_routes(
        [w_up, w_down, w_out], orders, count, me, forward_anchors[:steps]
    )

    branch = jnp.dot(attended_b, proj_out, preferred_element_type=jnp.float32) + bias_out.astype(
        jnp.float32
    )
    middle = seq_in + branch
    normed_two_f, norm_two_back = jax.vjp(
        layer_norm, middle, gain_two.astype(jnp.float32), shift_two.astype(jnp.float32)
    )
    normed_two = normed_two_f.astype(jnp.bfloat16)
    hidden = jnp.dot(normed_two, proj_up, preferred_element_type=jnp.float32) + bias_up.astype(
        jnp.float32
    )
    activated_f, gelu_back = jax.vjp(partial(jax.nn.gelu, approximate=False), hidden)
    activated = activated_f.astype(jnp.bfloat16)
    mlp_out = jnp.dot(activated, proj_down, preferred_element_type=jnp.float32) + bias_down.astype(
        jnp.float32
    )
    outputs = (middle + mlp_out).astype(jnp.bfloat16)

    out_grad = cotangent[:, 0].reshape(rows, width)
    out_grad_f = out_grad.astype(jnp.float32)
    grad_down = outer_rows(activated, out_grad)
    grad_bias_down = jnp.sum(out_grad_f, axis=0)
    act_grad = times_transposed(out_grad, proj_down)
    (hidden_grad,) = gelu_back(act_grad)
    hidden_grad_b = hidden_grad.astype(jnp.bfloat16)
    grad_up = outer_rows(normed_two, hidden_grad_b)
    grad_bias_up = jnp.sum(hidden_grad_b.astype(jnp.float32), axis=0)
    normed_two_grad = times_transposed(hidden_grad_b, proj_up)
    middle_ln_grad, grad_gain_two, grad_shift_two = norm_two_back(normed_two_grad)
    middle_grad = out_grad_f + middle_ln_grad
    branch_grad = middle_grad.astype(jnp.bfloat16)
    grad_out = outer_rows(attended_b, branch_grad)
    grad_bias_out = jnp.sum(branch_grad.astype(jnp.float32), axis=0)
    attended_grad = times_transposed(branch_grad, proj_out).astype(jnp.bfloat16)

    if head_parallel:
        grad_units = rows_to_units(
            attended_grad.reshape(micro, row_count, 1, HEADS, HEAD), seq_count, per_device, 1
        )[:, :, 0]
        qkv_grad_u = unit_backward(uq, uk, uv, weights, totals, attended_u, grad_units)
        proj_grad = units_to_rows(qkv_grad_u, seq_count, micro, 3)
        backward_anchors = [None, grad_units, qkv_grad_u, proj_grad, proj_grad]
    else:
        proj_grad = fallback_attention_backward(saved, attended_grad, row_count)
        backward_anchors = [None] + [proj_grad] * (steps - 1)

    full_rows = count * shard_rows
    vec_one = vector_block(
        [grad_bias_up, grad_bias_down, grad_gain_two, grad_shift_two], full_rows, jnp.float32
    )
    red_up, red_down, red_mixed = reduce_routes(
        [grad_up, grad_down, jnp.concatenate([grad_out, vec_one], axis=1)],
        orders,
        count,
        me,
        backward_anchors[:steps],
    )
    red_out, red_vec_one = split_cols(red_mixed, [width, vec_one.shape[1]])

    grad_bias_query = jnp.sum(proj_grad[:, :width].astype(jnp.float32), axis=0)
    grad_bias_value = jnp.sum(proj_grad[:, 2 * width :].astype(jnp.float32), axis=0)
    grad_parts = split_cols(proj_grad, qkv_cols)
    grad_qkv = [outer_rows(normed, g) for g in grad_parts]
    normed_grad = times_transposed(grad_parts[0], qkv_weights[0])
    for g, w in zip(grad_parts[1:], qkv_weights[1:]):
        normed_grad = normed_grad + times_transposed(g, w)
    input_ln_grad, grad_gain_one, grad_shift_one = norm_one_back(normed_grad)
    input_grads = (middle_grad + input_ln_grad).astype(jnp.bfloat16)

    vec_two = vector_block(
        [grad_gain_one, grad_shift_one, grad_bias_query, grad_bias_value, grad_bias_out],
        full_rows,
        jnp.float32,
    )
    red = reduce_routes(
        [grad_qkv[0], grad_qkv[1], jnp.concatenate([grad_qkv[2], vec_two], axis=1)],
        orders,
        count,
        me,
    )
    red_last, red_vec_two = split_cols(red[2], [qkv_cols[2], vec_two.shape[1]])
    red_qkv = jnp.concatenate([red[0], red[1], red_last], axis=1)
    r_bias_up, r_bias_down, r_gain_two, r_shift_two = vector_unblock(red_vec_one, [ratio, 1, 1, 1])
    r_gain_one, r_shift_one, r_bias_query, r_bias_value, r_bias_out = vector_unblock(
        red_vec_two, [1] * 5
    )
    reduced = (
        r_gain_one,
        r_shift_one,
        red_qkv,
        r_bias_query,
        r_bias_value,
        red_out,
        r_bias_out,
        r_gain_two,
        r_shift_two,
        red_up,
        r_bias_up,
        red_down,
        r_bias_down,
    )
    return (
        outputs.reshape(micro, 1, row_count, width),
        input_grads.reshape(micro, 1, row_count, width),
    ) + reduced


def solution(mesh):
    vec = P(ALL)
    mat = P(ALL, None)
    param_specs = (vec, vec, mat, vec, vec, mat, vec, vec, vec, mat, vec, mat, vec)
    return jax.shard_map(
        body,
        mesh=mesh,
        in_specs=(P(None, "dp", "seq", None), P(None, "dp", "seq", None), P(None, "dp", None, None))
        + param_specs,
        out_specs=(P(None, "dp", "seq", None), P(None, "dp", "seq", None)) + param_specs,
        check_vma=False,
    )
```

```python
from functools import partial

import jax
import jax.numpy as jnp
from jax import lax
from jax.sharding import PartitionSpec as P

HEADS = 12
HEAD = 64
EPSILON = 1e-05
ALL = ("dp", "seq")


def layer_norm(values, ln_gain, ln_shift):
    center = jnp.mean(values, axis=-1, keepdims=True)
    centered = values - center
    spread = jnp.mean(centered * centered, axis=-1, keepdims=True)
    return centered * lax.rsqrt(spread + EPSILON) * ln_gain + ln_shift


def piece_label(positions, bounds):
    inside = (positions[:, None] >= bounds[None, :, 0]) & (positions[:, None] < bounds[None, :, 1])
    labels = jnp.arange(1, bounds.shape[0] + 1, dtype=jnp.int32)
    return jnp.sum(jnp.where(inside, labels[None, :], 0), axis=1) - 1


def allowed_mask(query_pos, key_pos, bounds):
    query_label = piece_label(query_pos, bounds)
    key_label = piece_label(key_pos, bounds)
    causal = key_pos[None, :] <= query_pos[:, None]
    same_piece = (query_label[:, None] == key_label[None, :]) & (query_label[:, None] >= 0)
    return causal | same_piece


def outer_rows(left, right):
    return lax.dot_general(
        left, right, (((0,), (0,)), ((), ())), preferred_element_type=jnp.float32
    )


def times_transposed(left, right):
    return lax.dot_general(
        left, right, (((1,), (1,)), ((), ())), preferred_element_type=jnp.float32
    )


def route_orders(dp_size, seq_size):
    nbits = (dp_size * seq_size).bit_length() - 1
    if (dp_size, seq_size) == (4, 8):
        return [(3, 4, 0, 1, 2), (3, 0, 1, 4, 2), (3, 1, 4, 0, 2)]
    core = (seq_size.bit_length() - 1) if dp_size > 1 else None
    others = [b for b in range(nbits) if b != core]
    head = [core] if core is not None else []
    return [tuple(head + others[i:] + others[:i]) for i in range(3)]


def partner_pairs(count, bit):
    return [(i, i ^ (1 << bit)) for i in range(count)]


def tie(values, anchor):
    if anchor is None:
        return values
    values, _ = lax.optimization_barrier((values, anchor))
    return values


def gather_routes(routes, orders, count, me, anchors=None):
    nbits = count.bit_length() - 1
    idx = jnp.arange(count, dtype=jnp.int32)
    out = []
    for x, order in zip(routes, orders):
        rows, cols = x.shape
        for step, b in enumerate(reversed(order)):
            if anchors is not None:
                x = tie(x, anchors[step])
            got = lax.ppermute(x, ALL, partner_pairs(count, b))
            x = jnp.stack([x, got])
        rel = jnp.zeros((count,), jnp.int32)
        for j, b in enumerate(order):
            rel = rel + ((((idx >> b) & 1) ^ ((me >> b) & 1)) << (nbits - 1 - j))
        x = jnp.take(x.reshape(count, rows, cols), rel, axis=0)
        out.append(x.reshape(count * rows, cols))
    return out


def reduce_routes(routes, orders, count, me, anchors=None):
    nbits = count.bit_length() - 1
    out = []
    for x, order in zip(routes, orders):
        rows = x.shape[0] // count
        cols = x.shape[1]
        x = x.reshape([2] * nbits + [rows, cols])
        remaining = list(range(nbits - 1, -1, -1))
        for step, b in enumerate(order):
            if anchors is not None:
                x = tie(x, anchors[step])
            axis = remaining.index(b)
            mine = (me >> b) & 1
            keep = lax.dynamic_index_in_dim(x, mine, axis, keepdims=False)
            send = lax.dynamic_index_in_dim(x, 1 - mine, axis, keepdims=False).astype(jnp.bfloat16)
            got = lax.ppermute(send, ALL, partner_pairs(count, b))
            x = keep + got.astype(jnp.float32)
            remaining.pop(axis)
        out.append(x.reshape(rows, cols))
    return out


def split_cols(x, widths):
    out, at = [], 0
    for w in widths:
        out.append(x[:, at : at + w])
        at += w
    return out


def thirds(width, grain=128):
    first = -(-width // (3 * grain)) * grain
    return [first, first, width - 2 * first]


def vector_block(vectors, rows, dtype):
    cols = [v.reshape(rows, -1).astype(dtype) for v in vectors]
    used = sum(c.shape[1] for c in cols)
    pad = -(-used // 128) * 128 - used
    if pad:
        cols.append(jnp.zeros((rows, pad), dtype))
    return jnp.concatenate(cols, axis=1)


def vector_unblock(block, sizes):
    out, at = [], 0
    rows = block.shape[0]
    for s in sizes:
        out.append(block[:, at : at + s].reshape(rows * s))
        at += s
    return out


def unit_bounds(bounds, unit_count, per_device):
    first = lax.axis_index("seq") * per_device
    micro = (first + jnp.arange(per_device, dtype=jnp.int32)) // HEADS
    return bounds[:, 0][micro]


def unit_masks(ubounds, length):
    pos = jnp.arange(length, dtype=jnp.int32)
    return jax.vmap(lambda b: allowed_mask(pos, pos, b))(ubounds)


def rows_to_units(x, seq_count, per_device, parts):
    micro, rows = x.shape[0], x.shape[1]
    x = jnp.transpose(x, (0, 3, 1, 2, 4)).reshape(seq_count, per_device, rows, parts, HEAD)
    x = lax.all_to_all(x, "seq", 0, 0, tiled=True)
    x = jnp.transpose(x, (1, 0, 2, 3, 4))
    return x.reshape(per_device, seq_count * rows, parts, HEAD)


def units_to_rows(x, seq_count, micro, parts):
    per_device, length = x.shape[0], x.shape[1]
    rows = length // seq_count
    x = x.reshape(per_device, seq_count, rows, parts, HEAD)
    x = jnp.transpose(x, (1, 0, 2, 3, 4))
    x = lax.all_to_all(x, "seq", 0, 0, tiled=True)
    x = x.reshape(micro, HEADS, rows, parts, HEAD)
    x = jnp.transpose(x, (0, 2, 3, 1, 4))
    return x.reshape(micro * rows, parts * HEADS * HEAD)


def unit_forward(q, k, v, allowed):
    factor = q.shape[-1] ** (-0.5)
    scores = jnp.einsum("uqd,ukd->uqk", q, k, preferred_element_type=jnp.float32) * factor
    weights = jnp.where(allowed, jnp.exp(scores), 0.0)
    totals = jnp.sum(weights, axis=-1)
    summed = jnp.einsum(
        "uqk,ukd->uqd", weights.astype(jnp.bfloat16), v, preferred_element_type=jnp.float32
    )
    return weights, totals, summed / totals[:, :, None]


def unit_backward(q, k, v, weights, totals, attended, attended_grad):
    factor = q.shape[-1] ** (-0.5)
    grad_f = attended_grad.astype(jnp.float32)
    delta = jnp.sum(grad_f * attended, axis=-1) / totals
    summed_grad = (grad_f / totals[:, :, None]).astype(jnp.bfloat16)
    products = jnp.einsum("uqd,ukd->uqk", summed_grad, v, preferred_element_type=jnp.float32)
    score_grad = (weights * (products - delta[:, :, None])).astype(jnp.bfloat16)
    q_grad = jnp.einsum("uqk,ukd->uqd", score_grad, k, preferred_element_type=jnp.float32) * factor
    k_grad = jnp.einsum("uqk,uqd->ukd", score_grad, q, preferred_element_type=jnp.float32) * factor
    v_grad = jnp.einsum(
        "uqk,uqd->ukd", weights.astype(jnp.bfloat16), summed_grad, preferred_element_type=jnp.float32
    )
    return jnp.stack([q_grad, k_grad, v_grad], axis=2).astype(jnp.bfloat16)


def fallback_attention(queries, keys, values, bounds, row_count):
    micro = bounds.shape[0]
    seq_count = lax.axis_size("seq")
    total_len = row_count * seq_count
    query_pos = lax.axis_index("seq") * row_count + jnp.arange(row_count, dtype=jnp.int32)
    key_pos = jnp.arange(total_len, dtype=jnp.int32)
    saved = []
    attended_all = []
    for m in range(micro):
        sl = slice(m * row_count, (m + 1) * row_count)
        qh = queries[sl].reshape(row_count, HEADS, HEAD)
        k_all = lax.all_gather(keys[sl], "seq", axis=0, tiled=True).reshape(total_len, HEADS, HEAD)
        v_all = lax.all_gather(values[sl], "seq", axis=0, tiled=True).reshape(total_len, HEADS, HEAD)
        allowed = allowed_mask(query_pos, key_pos, bounds[m, 0])
        scores = jnp.einsum("rhd,khd->hrk", qh, k_all, preferred_element_type=jnp.float32) * HEAD ** (-0.5)
        weights = jnp.where(allowed[None], jnp.exp(scores), 0.0)
        totals = jnp.sum(weights, axis=-1)
        summed = jnp.einsum(
            "hrk,khd->rhd", weights.astype(jnp.bfloat16), v_all, preferred_element_type=jnp.float32
        )
        attended = summed / totals.T[:, :, None]
        saved.append((qh, k_all, v_all, weights, totals, attended))
        attended_all.append(attended.reshape(row_count, HEADS * HEAD))
    return jnp.concatenate(attended_all, axis=0), saved


def fallback_attention_backward(saved, attended_grad, row_count):
    factor = HEAD ** (-0.5)
    proj = []
    for m, (qh, k_all, v_all, weights, totals, attended) in enumerate(saved):
        grad = attended_grad[m * row_count : (m + 1) * row_count].astype(jnp.float32)
        grad = grad.reshape(row_count, HEADS, HEAD)
        delta = jnp.sum(grad * attended, axis=-1).T / totals
        grad_heads = (grad / totals.T[:, :, None]).astype(jnp.bfloat16)
        products = jnp.einsum("rhd,khd->hrk", grad_heads, v_all, preferred_element_type=jnp.float32)
        score_grad = (weights * (products - delta[:, :, None])).astype(jnp.bfloat16)
        q_grad = jnp.einsum("hrk,khd->rhd", score_grad, k_all, preferred_element_type=jnp.float32) * factor
        k_rows = jnp.einsum("hrk,rhd->khd", score_grad, qh, preferred_element_type=jnp.float32) * factor
        v_rows = jnp.einsum(
            "hrk,rhd->khd", weights.astype(jnp.bfloat16), grad_heads, preferred_element_type=jnp.float32
        )
        width = HEADS * HEAD
        k_own = lax.psum_scatter(
            k_rows.reshape(-1, width).astype(jnp.bfloat16), "seq", scatter_dimension=0, tiled=True
        )
        v_own = lax.psum_scatter(
            v_rows.reshape(-1, width).astype(jnp.bfloat16), "seq", scatter_dimension=0, tiled=True
        )
        proj.append(
            jnp.concatenate(
                [q_grad.reshape(row_count, width).astype(jnp.bfloat16), k_own, v_own], axis=1
            )
        )
    return jnp.concatenate(proj, axis=0)


def body(inputs, cotangent, bounds, *shards):
    micro = inputs.shape[0]
    row_count = inputs.shape[2]
    width = inputs.shape[3]
    ff = shards[9].shape[1]
    rows = micro * row_count
    seq_count = lax.axis_size("seq")
    unit_count = micro * HEADS
    head_parallel = unit_count % seq_count == 0
    per_device = unit_count // seq_count
    dp_count = lax.axis_size("dp")
    count = dp_count * seq_count
    me = lax.axis_index("dp") * seq_count + lax.axis_index("seq")
    orders = route_orders(dp_count, seq_count)
    steps = len(orders[0])
    ln1_g, ln1_b, w_qkv, b_q, b_v, w_out, b_out, ln2_g, ln2_b, w_up, b_up, w_down, b_down = shards
    shard_rows = w_qkv.shape[0]
    ratio = ff // width
    vec_sizes = [1] * 8 + [ratio]
    vecs_local = vector_block(
        [ln1_g, ln1_b, b_q, b_v, b_out, ln2_g, ln2_b, b_down, b_up], shard_rows, jnp.bfloat16
    )
    qkv_cols = thirds(w_qkv.shape[1])
    qkv_parts = split_cols(w_qkv, qkv_cols)
    gathered = gather_routes(
        [qkv_parts[0], qkv_parts[1], jnp.concatenate([qkv_parts[2], vecs_local], axis=1)],
        orders,
        count,
        me,
    )
    last_qkv, vecs_all = split_cols(gathered[2], [qkv_cols[2], vecs_local.shape[1]])
    qkv_weights = [gathered[0], gathered[1], last_qkv]
    (
        gain_one,
        shift_one,
        bias_query,
        bias_value,
        bias_out,
        gain_two,
        shift_two,
        bias_down,
        bias_up,
    ) = vector_unblock(vecs_all, vec_sizes)

    seq_in = inputs[:, 0].reshape(rows, width).astype(jnp.float32)
    normed_f, norm_one_back = jax.vjp(
        layer_norm, seq_in, gain_one.astype(jnp.float32), shift_one.astype(jnp.float32)
    )
    normed = normed_f.astype(jnp.bfloat16)
    if qkv_cols == [width] * 3:
        proj_q, proj_k, proj_v = [
            jnp.dot(normed, w, preferred_element_type=jnp.float32) for w in qkv_weights
        ]
    else:
        projected = jnp.dot(
            normed, jnp.concatenate(qkv_weights, axis=1), preferred_element_type=jnp.float32
        )
        proj_q, proj_k, proj_v = split_cols(projected, [width] * 3)
    queries = (proj_q + bias_query.astype(jnp.float32)).astype(jnp.bfloat16)
    keys_now = proj_k.astype(jnp.bfloat16)
    values_now = (proj_v + bias_value.astype(jnp.float32)).astype(jnp.bfloat16)

    if head_parallel:
        qkv_rows = jnp.concatenate([queries, keys_now, values_now], axis=1)
        qkv_units = rows_to_units(
            qkv_rows.reshape(micro, row_count, 3, HEADS, HEAD), seq_count, per_device, 3
        )
        uq, uk, uv = qkv_units[:, :, 0], qkv_units[:, :, 1], qkv_units[:, :, 2]
        allowed = unit_masks(unit_bounds(bounds, unit_count, per_device), seq_count * row_count)
        weights, totals, attended_u = unit_forward(uq, uk, uv, allowed)
        attended_b = units_to_rows(
            attended_u.astype(jnp.bfloat16)[:, :, None], seq_count, micro, 1
        )
        forward_anchors = [normed, qkv_units, weights, attended_u, attended_u]
    else:
        attended, saved = fallback_attention(queries, keys_now, values_now, bounds, row_count)
        attended_b = attended.astype(jnp.bfloat16)
        forward_anchors = [queries] + [attended] * (steps - 1)

    proj_up, proj_down, proj_out = gather_routes(
        [w_up, w_down, w_out], orders, count, me, forward_anchors[:steps]
    )

    branch = jnp.dot(attended_b, proj_out, preferred_element_type=jnp.float32) + bias_out.astype(
        jnp.float32
    )
    middle = seq_in + branch
    normed_two_f, norm_two_back = jax.vjp(
        layer_norm, middle, gain_two.astype(jnp.float32), shift_two.astype(jnp.float32)
    )
    normed_two = normed_two_f.astype(jnp.bfloat16)
    hidden = jnp.dot(normed_two, proj_up, preferred_element_type=jnp.float32) + bias_up.astype(
        jnp.float32
    )
    activated_f, gelu_back = jax.vjp(partial(jax.nn.gelu, approximate=False), hidden)
    activated = activated_f.astype(jnp.bfloat16)
    mlp_out = jnp.dot(activated, proj_down, preferred_element_type=jnp.float32) + bias_down.astype(
        jnp.float32
    )
    outputs = (middle + mlp_out).astype(jnp.bfloat16)

    out_grad = cotangent[:, 0].reshape(rows, width)
    out_grad_f = out_grad.astype(jnp.float32)
    grad_down = outer_rows(activated, out_grad)
    grad_bias_down = jnp.sum(out_grad_f, axis=0)
    act_grad = times_transposed(out_grad, proj_down)
    (hidden_grad,) = gelu_back(act_grad)
    hidden_grad_b = hidden_grad.astype(jnp.bfloat16)
    grad_up = outer_rows(normed_two, hidden_grad_b)
    grad_bias_up = jnp.sum(hidden_grad_b.astype(jnp.float32), axis=0)
    normed_two_grad = times_transposed(hidden_grad_b, proj_up)
    middle_ln_grad, grad_gain_two, grad_shift_two = norm_two_back(normed_two_grad)
    middle_grad = out_grad_f + middle_ln_grad
    branch_grad = middle_grad.astype(jnp.bfloat16)
    grad_out = outer_rows(attended_b, branch_grad)
    grad_bias_out = jnp.sum(branch_grad.astype(jnp.float32), axis=0)
    attended_grad = times_transposed(branch_grad, proj_out).astype(jnp.bfloat16)

    if head_parallel:
        grad_units = rows_to_units(
            attended_grad.reshape(micro, row_count, 1, HEADS, HEAD), seq_count, per_device, 1
        )[:, :, 0]
        qkv_grad_u = unit_backward(uq, uk, uv, weights, totals, attended_u, grad_units)
        proj_grad = units_to_rows(qkv_grad_u, seq_count, micro, 3)
        backward_anchors = [None, None, grad_units, qkv_grad_u, qkv_grad_u]
    else:
        proj_grad = fallback_attention_backward(saved, attended_grad, row_count)
        backward_anchors = [None] + [proj_grad] * (steps - 1)

    full_rows = count * shard_rows
    vec_one = vector_block(
        [grad_bias_up, grad_bias_down, grad_gain_two, grad_shift_two], full_rows, jnp.float32
    )
    red_up, red_down, red_mixed = reduce_routes(
        [grad_up, grad_down, jnp.concatenate([grad_out, vec_one], axis=1)],
        orders,
        count,
        me,
        backward_anchors[:steps],
    )
    red_out, red_vec_one = split_cols(red_mixed, [width, vec_one.shape[1]])

    grad_bias_query = jnp.sum(proj_grad[:, :width].astype(jnp.float32), axis=0)
    grad_bias_value = jnp.sum(proj_grad[:, 2 * width :].astype(jnp.float32), axis=0)
    grad_parts = split_cols(proj_grad, qkv_cols)
    grad_qkv = [outer_rows(normed, g) for g in grad_parts]
    normed_grad = times_transposed(grad_parts[0], qkv_weights[0])
    for g, w in zip(grad_parts[1:], qkv_weights[1:]):
        normed_grad = normed_grad + times_transposed(g, w)
    input_ln_grad, grad_gain_one, grad_shift_one = norm_one_back(normed_grad)
    input_grads = (middle_grad + input_ln_grad).astype(jnp.bfloat16)

    vec_two = vector_block(
        [grad_gain_one, grad_shift_one, grad_bias_query, grad_bias_value, grad_bias_out],
        full_rows,
        jnp.float32,
    )
    red = reduce_routes(
        [grad_qkv[0], grad_qkv[1], jnp.concatenate([grad_qkv[2], vec_two], axis=1)],
        orders,
        count,
        me,
    )
    red_last, red_vec_two = split_cols(red[2], [qkv_cols[2], vec_two.shape[1]])
    red_qkv = jnp.concatenate([red[0], red[1], red_last], axis=1)
    r_bias_up, r_bias_down, r_gain_two, r_shift_two = vector_unblock(red_vec_one, [ratio, 1, 1, 1])
    r_gain_one, r_shift_one, r_bias_query, r_bias_value, r_bias_out = vector_unblock(
        red_vec_two, [1] * 5
    )
    reduced = (
        r_gain_one,
        r_shift_one,
        red_qkv,
        r_bias_query,
        r_bias_value,
        red_out,
        r_bias_out,
        r_gain_two,
        r_shift_two,
        red_up,
        r_bias_up,
        red_down,
        r_bias_down,
    )
    return (
        outputs.reshape(micro, 1, row_count, width),
        input_grads.reshape(micro, 1, row_count, width),
    ) + reduced


def solution(mesh):
    vec = P(ALL)
    mat = P(ALL, None)
    param_specs = (vec, vec, mat, vec, vec, mat, vec, vec, vec, mat, vec, mat, vec)
    return jax.shard_map(
        body,
        mesh=mesh,
        in_specs=(P(None, "dp", "seq", None), P(None, "dp", "seq", None), P(None, "dp", None, None))
        + param_specs,
        out_specs=(P(None, "dp", "seq", None), P(None, "dp", "seq", None)) + param_specs,
        check_vma=False,
    )
```

```python
from functools import partial

import jax
import jax.numpy as jnp
from jax import lax
from jax.sharding import PartitionSpec as P

HEADS = 12
HEAD = 64
EPSILON = 1e-05
ALL = ("dp", "seq")


def layer_norm(values, ln_gain, ln_shift):
    center = jnp.mean(values, axis=-1, keepdims=True)
    centered = values - center
    spread = jnp.mean(centered * centered, axis=-1, keepdims=True)
    return centered * lax.rsqrt(spread + EPSILON) * ln_gain + ln_shift


def piece_label(positions, bounds):
    inside = (positions[:, None] >= bounds[None, :, 0]) & (positions[:, None] < bounds[None, :, 1])
    labels = jnp.arange(1, bounds.shape[0] + 1, dtype=jnp.int32)
    return jnp.sum(jnp.where(inside, labels[None, :], 0), axis=1) - 1


def allowed_mask(query_pos, key_pos, bounds):
    query_label = piece_label(query_pos, bounds)
    key_label = piece_label(key_pos, bounds)
    causal = key_pos[None, :] <= query_pos[:, None]
    same_piece = (query_label[:, None] == key_label[None, :]) & (query_label[:, None] >= 0)
    return causal | same_piece


def outer_rows(left, right):
    return lax.dot_general(
        left, right, (((0,), (0,)), ((), ())), preferred_element_type=jnp.float32
    )


def times_transposed(left, right):
    return lax.dot_general(
        left, right, (((1,), (1,)), ((), ())), preferred_element_type=jnp.float32
    )


def route_orders(dp_size, seq_size):
    nbits = (dp_size * seq_size).bit_length() - 1
    if (dp_size, seq_size) == (4, 8):
        return [(3, 4, 0, 1, 2), (3, 0, 1, 4, 2), (3, 1, 4, 0, 2)]
    core = (seq_size.bit_length() - 1) if dp_size > 1 else None
    others = [b for b in range(nbits) if b != core]
    head = [core] if core is not None else []
    return [tuple(head + others[i:] + others[:i]) for i in range(3)]


def partner_pairs(count, bit):
    return [(i, i ^ (1 << bit)) for i in range(count)]


def tie(values, anchor):
    if anchor is None:
        return values
    values, _ = lax.optimization_barrier((values, anchor))
    return values


def gather_routes(routes, orders, count, me, anchors=None):
    nbits = count.bit_length() - 1
    idx = jnp.arange(count, dtype=jnp.int32)
    out = []
    for x, order in zip(routes, orders):
        rows, cols = x.shape
        for step, b in enumerate(reversed(order)):
            if anchors is not None:
                x = tie(x, anchors[step])
            got = lax.ppermute(x, ALL, partner_pairs(count, b))
            x = jnp.stack([x, got])
        rel = jnp.zeros((count,), jnp.int32)
        for j, b in enumerate(order):
            rel = rel + ((((idx >> b) & 1) ^ ((me >> b) & 1)) << (nbits - 1 - j))
        x = jnp.take(x.reshape(count, rows, cols), rel, axis=0)
        out.append(x.reshape(count * rows, cols))
    return out


def reduce_routes(routes, orders, count, me, anchors=None):
    nbits = count.bit_length() - 1
    out = []
    for x, order in zip(routes, orders):
        rows = x.shape[0] // count
        cols = x.shape[1]
        x = x.reshape([2] * nbits + [rows, cols])
        remaining = list(range(nbits - 1, -1, -1))
        for step, b in enumerate(order):
            if anchors is not None:
                x = tie(x, anchors[step])
            axis = remaining.index(b)
            mine = (me >> b) & 1
            keep = lax.dynamic_index_in_dim(x, mine, axis, keepdims=False)
            send = lax.dynamic_index_in_dim(x, 1 - mine, axis, keepdims=False).astype(jnp.bfloat16)
            got = lax.ppermute(send, ALL, partner_pairs(count, b))
            x = keep + got.astype(jnp.float32)
            remaining.pop(axis)
        out.append(x.reshape(rows, cols))
    return out


def split_cols(x, widths):
    out, at = [], 0
    for w in widths:
        out.append(x[:, at : at + w])
        at += w
    return out


def thirds(width, grain=128):
    first = -(-width // (3 * grain)) * grain
    return [first, first, width - 2 * first]


def vector_block(vectors, rows, dtype):
    cols = [v.reshape(rows, -1).astype(dtype) for v in vectors]
    used = sum(c.shape[1] for c in cols)
    pad = -(-used // 128) * 128 - used
    if pad:
        cols.append(jnp.zeros((rows, pad), dtype))
    return jnp.concatenate(cols, axis=1)


def vector_unblock(block, sizes):
    out, at = [], 0
    rows = block.shape[0]
    for s in sizes:
        out.append(block[:, at : at + s].reshape(rows * s))
        at += s
    return out


def unit_bounds(bounds, unit_count, per_device):
    first = lax.axis_index("seq") * per_device
    micro = (first + jnp.arange(per_device, dtype=jnp.int32)) // HEADS
    return bounds[:, 0][micro]


def unit_masks(ubounds, length):
    pos = jnp.arange(length, dtype=jnp.int32)
    return jax.vmap(lambda b: allowed_mask(pos, pos, b))(ubounds)


def rows_to_units(x, seq_count, per_device, parts):
    micro, rows = x.shape[0], x.shape[1]
    x = jnp.transpose(x, (0, 3, 1, 2, 4)).reshape(seq_count, per_device, rows, parts, HEAD)
    x = lax.all_to_all(x, "seq", 0, 0, tiled=True)
    x = jnp.transpose(x, (1, 0, 2, 3, 4))
    return x.reshape(per_device, seq_count * rows, parts, HEAD)


def units_to_rows(x, seq_count, micro, parts):
    per_device, length = x.shape[0], x.shape[1]
    rows = length // seq_count
    x = x.reshape(per_device, seq_count, rows, parts, HEAD)
    x = jnp.transpose(x, (1, 0, 2, 3, 4))
    x = lax.all_to_all(x, "seq", 0, 0, tiled=True)
    x = x.reshape(micro, HEADS, rows, parts, HEAD)
    x = jnp.transpose(x, (0, 2, 3, 1, 4))
    return x.reshape(micro * rows, parts * HEADS * HEAD)


def unit_forward(q, k, v, allowed):
    factor = q.shape[-1] ** (-0.5)
    scores = jnp.einsum("uqd,ukd->uqk", q, k, preferred_element_type=jnp.float32) * factor
    weights = jnp.where(allowed, jnp.exp(scores), 0.0)
    totals = jnp.sum(weights, axis=-1)
    summed = jnp.einsum(
        "uqk,ukd->uqd", weights.astype(jnp.bfloat16), v, preferred_element_type=jnp.float32
    )
    return weights, totals, summed / totals[:, :, None]


def unit_backward(q, k, v, weights, totals, attended, attended_grad):
    factor = q.shape[-1] ** (-0.5)
    grad_f = attended_grad.astype(jnp.float32)
    delta = jnp.sum(grad_f * attended, axis=-1) / totals
    summed_grad = (grad_f / totals[:, :, None]).astype(jnp.bfloat16)
    products = jnp.einsum("uqd,ukd->uqk", summed_grad, v, preferred_element_type=jnp.float32)
    score_grad = (weights * (products - delta[:, :, None])).astype(jnp.bfloat16)
    q_grad = jnp.einsum("uqk,ukd->uqd", score_grad, k, preferred_element_type=jnp.float32) * factor
    k_grad = jnp.einsum("uqk,uqd->ukd", score_grad, q, preferred_element_type=jnp.float32) * factor
    v_grad = jnp.einsum(
        "uqk,uqd->ukd", weights.astype(jnp.bfloat16), summed_grad, preferred_element_type=jnp.float32
    )
    return jnp.stack([q_grad, k_grad, v_grad], axis=2).astype(jnp.bfloat16)


def fallback_attention(queries, keys, values, bounds, row_count):
    micro = bounds.shape[0]
    seq_count = lax.axis_size("seq")
    total_len = row_count * seq_count
    query_pos = lax.axis_index("seq") * row_count + jnp.arange(row_count, dtype=jnp.int32)
    key_pos = jnp.arange(total_len, dtype=jnp.int32)
    saved = []
    attended_all = []
    for m in range(micro):
        sl = slice(m * row_count, (m + 1) * row_count)
        qh = queries[sl].reshape(row_count, HEADS, HEAD)
        k_all = lax.all_gather(keys[sl], "seq", axis=0, tiled=True).reshape(total_len, HEADS, HEAD)
        v_all = lax.all_gather(values[sl], "seq", axis=0, tiled=True).reshape(total_len, HEADS, HEAD)
        allowed = allowed_mask(query_pos, key_pos, bounds[m, 0])
        scores = jnp.einsum("rhd,khd->hrk", qh, k_all, preferred_element_type=jnp.float32) * HEAD ** (-0.5)
        weights = jnp.where(allowed[None], jnp.exp(scores), 0.0)
        totals = jnp.sum(weights, axis=-1)
        summed = jnp.einsum(
            "hrk,khd->rhd", weights.astype(jnp.bfloat16), v_all, preferred_element_type=jnp.float32
        )
        attended = summed / totals.T[:, :, None]
        saved.append((qh, k_all, v_all, weights, totals, attended))
        attended_all.append(attended.reshape(row_count, HEADS * HEAD))
    return jnp.concatenate(attended_all, axis=0), saved


def fallback_attention_backward(saved, attended_grad, row_count):
    factor = HEAD ** (-0.5)
    proj = []
    for m, (qh, k_all, v_all, weights, totals, attended) in enumerate(saved):
        grad = attended_grad[m * row_count : (m + 1) * row_count].astype(jnp.float32)
        grad = grad.reshape(row_count, HEADS, HEAD)
        delta = jnp.sum(grad * attended, axis=-1).T / totals
        grad_heads = (grad / totals.T[:, :, None]).astype(jnp.bfloat16)
        products = jnp.einsum("rhd,khd->hrk", grad_heads, v_all, preferred_element_type=jnp.float32)
        score_grad = (weights * (products - delta[:, :, None])).astype(jnp.bfloat16)
        q_grad = jnp.einsum("hrk,khd->rhd", score_grad, k_all, preferred_element_type=jnp.float32) * factor
        k_rows = jnp.einsum("hrk,rhd->khd", score_grad, qh, preferred_element_type=jnp.float32) * factor
        v_rows = jnp.einsum(
            "hrk,rhd->khd", weights.astype(jnp.bfloat16), grad_heads, preferred_element_type=jnp.float32
        )
        width = HEADS * HEAD
        k_own = lax.psum_scatter(
            k_rows.reshape(-1, width).astype(jnp.bfloat16), "seq", scatter_dimension=0, tiled=True
        )
        v_own = lax.psum_scatter(
            v_rows.reshape(-1, width).astype(jnp.bfloat16), "seq", scatter_dimension=0, tiled=True
        )
        proj.append(
            jnp.concatenate(
                [q_grad.reshape(row_count, width).astype(jnp.bfloat16), k_own, v_own], axis=1
            )
        )
    return jnp.concatenate(proj, axis=0)


def body(inputs, cotangent, bounds, *shards):
    micro = inputs.shape[0]
    row_count = inputs.shape[2]
    width = inputs.shape[3]
    ff = shards[9].shape[1]
    rows = micro * row_count
    seq_count = lax.axis_size("seq")
    unit_count = micro * HEADS
    head_parallel = unit_count % seq_count == 0
    per_device = unit_count // seq_count
    dp_count = lax.axis_size("dp")
    count = dp_count * seq_count
    me = lax.axis_index("dp") * seq_count + lax.axis_index("seq")
    orders = route_orders(dp_count, seq_count)
    steps = len(orders[0])
    ln1_g, ln1_b, w_qkv, b_q, b_v, w_out, b_out, ln2_g, ln2_b, w_up, b_up, w_down, b_down = shards
    shard_rows = w_qkv.shape[0]
    ratio = ff // width
    vec_sizes = [1] * 8 + [ratio]
    vecs_local = vector_block(
        [ln1_g, ln1_b, b_q, b_v, b_out, ln2_g, ln2_b, b_down, b_up], shard_rows, jnp.bfloat16
    )
    mlp_pack = jnp.concatenate([w_out, w_up, w_down.reshape(shard_rows, ratio * width)], axis=1)
    qkv_cols = thirds(w_qkv.shape[1])
    qkv_parts = split_cols(w_qkv, qkv_cols)
    gathered = gather_routes(
        [qkv_parts[0], qkv_parts[1], jnp.concatenate([qkv_parts[2], vecs_local], axis=1)],
        orders,
        count,
        me,
    )
    last_qkv, vecs_all = split_cols(gathered[2], [qkv_cols[2], vecs_local.shape[1]])
    qkv_weights = [gathered[0], gathered[1], last_qkv]
    (
        gain_one,
        shift_one,
        bias_query,
        bias_value,
        bias_out,
        gain_two,
        shift_two,
        bias_down,
        bias_up,
    ) = vector_unblock(vecs_all, vec_sizes)

    seq_in = inputs[:, 0].reshape(rows, width).astype(jnp.float32)
    normed_f, norm_one_back = jax.vjp(
        layer_norm, seq_in, gain_one.astype(jnp.float32), shift_one.astype(jnp.float32)
    )
    normed = normed_f.astype(jnp.bfloat16)
    if qkv_cols == [width] * 3:
        proj_q, proj_k, proj_v = [
            jnp.dot(normed, w, preferred_element_type=jnp.float32) for w in qkv_weights
        ]
    else:
        projected = jnp.dot(
            normed, jnp.concatenate(qkv_weights, axis=1), preferred_element_type=jnp.float32
        )
        proj_q, proj_k, proj_v = split_cols(projected, [width] * 3)
    queries = (proj_q + bias_query.astype(jnp.float32)).astype(jnp.bfloat16)
    keys_now = proj_k.astype(jnp.bfloat16)
    values_now = (proj_v + bias_value.astype(jnp.float32)).astype(jnp.bfloat16)

    if head_parallel:
        qkv_rows = jnp.concatenate([queries, keys_now, values_now], axis=1)
        qkv_units = rows_to_units(
            qkv_rows.reshape(micro, row_count, 3, HEADS, HEAD), seq_count, per_device, 3
        )
        uq, uk, uv = qkv_units[:, :, 0], qkv_units[:, :, 1], qkv_units[:, :, 2]
        allowed = unit_masks(unit_bounds(bounds, unit_count, per_device), seq_count * row_count)
        weights, totals, attended_u = unit_forward(uq, uk, uv, allowed)
        attended_b = units_to_rows(
            attended_u.astype(jnp.bfloat16)[:, :, None], seq_count, micro, 1
        )
        forward_anchors = [normed, qkv_units, weights, attended_u, attended_u]
    else:
        attended, saved = fallback_attention(queries, keys_now, values_now, bounds, row_count)
        attended_b = attended.astype(jnp.bfloat16)
        forward_anchors = [queries] + [attended] * (steps - 1)

    proj_out, proj_up, down_view = split_cols(
        lax.all_gather(mlp_pack, ALL, axis=0, tiled=True), [width, ff, ff]
    )
    proj_down = down_view.reshape(count * shard_rows * ratio, width)

    branch = jnp.dot(attended_b, proj_out, preferred_element_type=jnp.float32) + bias_out.astype(
        jnp.float32
    )
    middle = seq_in + branch
    normed_two_f, norm_two_back = jax.vjp(
        layer_norm, middle, gain_two.astype(jnp.float32), shift_two.astype(jnp.float32)
    )
    normed_two = normed_two_f.astype(jnp.bfloat16)
    hidden = jnp.dot(normed_two, proj_up, preferred_element_type=jnp.float32) + bias_up.astype(
        jnp.float32
    )
    activated_f, gelu_back = jax.vjp(partial(jax.nn.gelu, approximate=False), hidden)
    activated = activated_f.astype(jnp.bfloat16)
    mlp_out = jnp.dot(activated, proj_down, preferred_element_type=jnp.float32) + bias_down.astype(
        jnp.float32
    )
    outputs = (middle + mlp_out).astype(jnp.bfloat16)

    out_grad = cotangent[:, 0].reshape(rows, width)
    out_grad_f = out_grad.astype(jnp.float32)
    grad_down = outer_rows(activated, out_grad)
    grad_bias_down = jnp.sum(out_grad_f, axis=0)
    act_grad = times_transposed(out_grad, proj_down)
    (hidden_grad,) = gelu_back(act_grad)
    hidden_grad_b = hidden_grad.astype(jnp.bfloat16)
    grad_up = outer_rows(normed_two, hidden_grad_b)
    grad_bias_up = jnp.sum(hidden_grad_b.astype(jnp.float32), axis=0)
    normed_two_grad = times_transposed(hidden_grad_b, proj_up)
    middle_ln_grad, grad_gain_two, grad_shift_two = norm_two_back(normed_two_grad)
    middle_grad = out_grad_f + middle_ln_grad
    branch_grad = middle_grad.astype(jnp.bfloat16)
    grad_out = outer_rows(attended_b, branch_grad)
    grad_bias_out = jnp.sum(branch_grad.astype(jnp.float32), axis=0)
    attended_grad = times_transposed(branch_grad, proj_out).astype(jnp.bfloat16)

    if head_parallel:
        grad_units = rows_to_units(
            attended_grad.reshape(micro, row_count, 1, HEADS, HEAD), seq_count, per_device, 1
        )[:, :, 0]
        qkv_grad_u = unit_backward(uq, uk, uv, weights, totals, attended_u, grad_units)
        proj_grad = units_to_rows(qkv_grad_u, seq_count, micro, 3)
        backward_anchors = [None, grad_units, qkv_grad_u, proj_grad, proj_grad]
    else:
        proj_grad = fallback_attention_backward(saved, attended_grad, row_count)
        backward_anchors = [None] + [proj_grad] * (steps - 1)

    full_rows = count * shard_rows
    vec_one = vector_block(
        [grad_bias_up, grad_bias_down, grad_gain_two, grad_shift_two], full_rows, jnp.float32
    )
    red_up, red_down, red_mixed = reduce_routes(
        [grad_up, grad_down, jnp.concatenate([grad_out, vec_one], axis=1)],
        orders,
        count,
        me,
        backward_anchors[:steps],
    )
    red_out, red_vec_one = split_cols(red_mixed, [width, vec_one.shape[1]])

    grad_bias_query = jnp.sum(proj_grad[:, :width].astype(jnp.float32), axis=0)
    grad_bias_value = jnp.sum(proj_grad[:, 2 * width :].astype(jnp.float32), axis=0)
    grad_parts = split_cols(proj_grad, qkv_cols)
    grad_qkv = [outer_rows(normed, g) for g in grad_parts]
    normed_grad = times_transposed(grad_parts[0], qkv_weights[0])
    for g, w in zip(grad_parts[1:], qkv_weights[1:]):
        normed_grad = normed_grad + times_transposed(g, w)
    input_ln_grad, grad_gain_one, grad_shift_one = norm_one_back(normed_grad)
    input_grads = (middle_grad + input_ln_grad).astype(jnp.bfloat16)

    vec_two = vector_block(
        [grad_gain_one, grad_shift_one, grad_bias_query, grad_bias_value, grad_bias_out],
        full_rows,
        jnp.float32,
    )
    red = reduce_routes(
        [grad_qkv[0], grad_qkv[1], jnp.concatenate([grad_qkv[2], vec_two], axis=1)],
        orders,
        count,
        me,
    )
    red_last, red_vec_two = split_cols(red[2], [qkv_cols[2], vec_two.shape[1]])
    red_qkv = jnp.concatenate([red[0], red[1], red_last], axis=1)
    r_bias_up, r_bias_down, r_gain_two, r_shift_two = vector_unblock(red_vec_one, [ratio, 1, 1, 1])
    r_gain_one, r_shift_one, r_bias_query, r_bias_value, r_bias_out = vector_unblock(
        red_vec_two, [1] * 5
    )
    reduced = (
        r_gain_one,
        r_shift_one,
        red_qkv,
        r_bias_query,
        r_bias_value,
        red_out,
        r_bias_out,
        r_gain_two,
        r_shift_two,
        red_up,
        r_bias_up,
        red_down,
        r_bias_down,
    )
    return (
        outputs.reshape(micro, 1, row_count, width),
        input_grads.reshape(micro, 1, row_count, width),
    ) + reduced


def solution(mesh):
    vec = P(ALL)
    mat = P(ALL, None)
    param_specs = (vec, vec, mat, vec, vec, mat, vec, vec, vec, mat, vec, mat, vec)
    return jax.shard_map(
        body,
        mesh=mesh,
        in_specs=(P(None, "dp", "seq", None), P(None, "dp", "seq", None), P(None, "dp", None, None))
        + param_specs,
        out_specs=(P(None, "dp", "seq", None), P(None, "dp", "seq", None)) + param_specs,
        check_vma=False,
    )
```

```python
from functools import partial

import jax
import jax.numpy as jnp
from jax import lax
from jax.sharding import PartitionSpec as P

HEADS = 12
HEAD = 64
EPSILON = 1e-05
ALL = ("dp", "seq")


def layer_norm(values, ln_gain, ln_shift):
    center = jnp.mean(values, axis=-1, keepdims=True)
    centered = values - center
    spread = jnp.mean(centered * centered, axis=-1, keepdims=True)
    return centered * lax.rsqrt(spread + EPSILON) * ln_gain + ln_shift


def piece_label(positions, bounds):
    inside = (positions[:, None] >= bounds[None, :, 0]) & (positions[:, None] < bounds[None, :, 1])
    labels = jnp.arange(1, bounds.shape[0] + 1, dtype=jnp.int32)
    return jnp.sum(jnp.where(inside, labels[None, :], 0), axis=1) - 1


def allowed_mask(query_pos, key_pos, bounds):
    query_label = piece_label(query_pos, bounds)
    key_label = piece_label(key_pos, bounds)
    causal = key_pos[None, :] <= query_pos[:, None]
    same_piece = (query_label[:, None] == key_label[None, :]) & (query_label[:, None] >= 0)
    return causal | same_piece


def outer_rows(left, right):
    return lax.dot_general(
        left, right, (((0,), (0,)), ((), ())), preferred_element_type=jnp.float32
    )


def times_transposed(left, right):
    return lax.dot_general(
        left, right, (((1,), (1,)), ((), ())), preferred_element_type=jnp.float32
    )


def route_orders(dp_size, seq_size):
    nbits = (dp_size * seq_size).bit_length() - 1
    if (dp_size, seq_size) == (4, 8):
        return [(3, 4, 0, 1, 2), (3, 0, 1, 4, 2), (3, 1, 4, 0, 2)]
    core = (seq_size.bit_length() - 1) if dp_size > 1 else None
    others = [b for b in range(nbits) if b != core]
    head = [core] if core is not None else []
    return [tuple(head + others[i:] + others[:i]) for i in range(3)]


def partner_pairs(count, bit):
    return [(i, i ^ (1 << bit)) for i in range(count)]


def tie(values, anchor):
    if anchor is None:
        return values
    values, _ = lax.optimization_barrier((values, anchor))
    return values


def gather_routes(routes, orders, count, me, anchors=None):
    nbits = count.bit_length() - 1
    idx = jnp.arange(count, dtype=jnp.int32)
    out = []
    for x, order in zip(routes, orders):
        rows, cols = x.shape
        for step, b in enumerate(reversed(order)):
            if anchors is not None:
                x = tie(x, anchors[step])
            got = lax.ppermute(x, ALL, partner_pairs(count, b))
            x = jnp.stack([x, got])
        rel = jnp.zeros((count,), jnp.int32)
        for j, b in enumerate(order):
            rel = rel + ((((idx >> b) & 1) ^ ((me >> b) & 1)) << (nbits - 1 - j))
        x = jnp.take(x.reshape(count, rows, cols), rel, axis=0)
        out.append(x.reshape(count * rows, cols))
    return out


def reduce_routes(routes, orders, count, me, anchors=None):
    nbits = count.bit_length() - 1
    out = []
    for x, order in zip(routes, orders):
        rows = x.shape[0] // count
        cols = x.shape[1]
        x = x.reshape([2] * nbits + [rows, cols])
        remaining = list(range(nbits - 1, -1, -1))
        for step, b in enumerate(order):
            if anchors is not None:
                x = tie(x, anchors[step])
            axis = remaining.index(b)
            mine = (me >> b) & 1
            keep = lax.dynamic_index_in_dim(x, mine, axis, keepdims=False)
            send = lax.dynamic_index_in_dim(x, 1 - mine, axis, keepdims=False).astype(jnp.bfloat16)
            got = lax.ppermute(send, ALL, partner_pairs(count, b))
            x = keep + got.astype(jnp.float32)
            remaining.pop(axis)
        out.append(x.reshape(rows, cols))
    return out


def split_cols(x, widths):
    out, at = [], 0
    for w in widths:
        out.append(x[:, at : at + w])
        at += w
    return out


def thirds(width, grain=128):
    first = -(-width // (3 * grain)) * grain
    return [first, first, width - 2 * first]


def vector_block(vectors, rows, dtype):
    cols = [v.reshape(rows, -1).astype(dtype) for v in vectors]
    used = sum(c.shape[1] for c in cols)
    pad = -(-used // 128) * 128 - used
    if pad:
        cols.append(jnp.zeros((rows, pad), dtype))
    return jnp.concatenate(cols, axis=1)


def vector_unblock(block, sizes):
    out, at = [], 0
    rows = block.shape[0]
    for s in sizes:
        out.append(block[:, at : at + s].reshape(rows * s))
        at += s
    return out


def unit_bounds(bounds, unit_count, per_device):
    first = lax.axis_index("seq") * per_device
    micro = (first + jnp.arange(per_device, dtype=jnp.int32)) // HEADS
    return bounds[:, 0][micro]


def unit_masks(ubounds, length):
    pos = jnp.arange(length, dtype=jnp.int32)
    return jax.vmap(lambda b: allowed_mask(pos, pos, b))(ubounds)


def rows_to_units(x, seq_count, per_device, parts):
    micro, rows = x.shape[0], x.shape[1]
    x = jnp.transpose(x, (0, 3, 1, 2, 4)).reshape(seq_count, per_device, rows, parts, HEAD)
    x = lax.all_to_all(x, "seq", 0, 0, tiled=True)
    x = jnp.transpose(x, (1, 0, 2, 3, 4))
    return x.reshape(per_device, seq_count * rows, parts, HEAD)


def units_to_rows(x, seq_count, micro, parts):
    per_device, length = x.shape[0], x.shape[1]
    rows = length // seq_count
    x = x.reshape(per_device, seq_count, rows, parts, HEAD)
    x = jnp.transpose(x, (1, 0, 2, 3, 4))
    x = lax.all_to_all(x, "seq", 0, 0, tiled=True)
    x = x.reshape(micro, HEADS, rows, parts, HEAD)
    x = jnp.transpose(x, (0, 2, 3, 1, 4))
    return x.reshape(micro * rows, parts * HEADS * HEAD)


def unit_forward(q, k, v, allowed):
    factor = q.shape[-1] ** (-0.5)
    scores = jnp.einsum("uqd,ukd->uqk", q, k, preferred_element_type=jnp.float32) * factor
    weights = jnp.where(allowed, jnp.exp(scores), 0.0)
    totals = jnp.sum(weights, axis=-1)
    summed = jnp.einsum(
        "uqk,ukd->uqd", weights.astype(jnp.bfloat16), v, preferred_element_type=jnp.float32
    )
    return weights, totals, summed / totals[:, :, None]


def unit_backward(q, k, v, weights, totals, attended, attended_grad):
    factor = q.shape[-1] ** (-0.5)
    grad_f = attended_grad.astype(jnp.float32)
    delta = jnp.sum(grad_f * attended, axis=-1) / totals
    summed_grad = (grad_f / totals[:, :, None]).astype(jnp.bfloat16)
    products = jnp.einsum("uqd,ukd->uqk", summed_grad, v, preferred_element_type=jnp.float32)
    score_grad = (weights * (products - delta[:, :, None])).astype(jnp.bfloat16)
    q_grad = jnp.einsum("uqk,ukd->uqd", score_grad, k, preferred_element_type=jnp.float32) * factor
    k_grad = jnp.einsum("uqk,uqd->ukd", score_grad, q, preferred_element_type=jnp.float32) * factor
    v_grad = jnp.einsum(
        "uqk,uqd->ukd", weights.astype(jnp.bfloat16), summed_grad, preferred_element_type=jnp.float32
    )
    return jnp.stack([q_grad, k_grad, v_grad], axis=2).astype(jnp.bfloat16)


def fallback_attention(queries, keys, values, bounds, row_count):
    micro = bounds.shape[0]
    seq_count = lax.axis_size("seq")
    total_len = row_count * seq_count
    query_pos = lax.axis_index("seq") * row_count + jnp.arange(row_count, dtype=jnp.int32)
    key_pos = jnp.arange(total_len, dtype=jnp.int32)
    saved = []
    attended_all = []
    for m in range(micro):
        sl = slice(m * row_count, (m + 1) * row_count)
        qh = queries[sl].reshape(row_count, HEADS, HEAD)
        k_all = lax.all_gather(keys[sl], "seq", axis=0, tiled=True).reshape(total_len, HEADS, HEAD)
        v_all = lax.all_gather(values[sl], "seq", axis=0, tiled=True).reshape(total_len, HEADS, HEAD)
        allowed = allowed_mask(query_pos, key_pos, bounds[m, 0])
        scores = jnp.einsum("rhd,khd->hrk", qh, k_all, preferred_element_type=jnp.float32) * HEAD ** (-0.5)
        weights = jnp.where(allowed[None], jnp.exp(scores), 0.0)
        totals = jnp.sum(weights, axis=-1)
        summed = jnp.einsum(
            "hrk,khd->rhd", weights.astype(jnp.bfloat16), v_all, preferred_element_type=jnp.float32
        )
        attended = summed / totals.T[:, :, None]
        saved.append((qh, k_all, v_all, weights, totals, attended))
        attended_all.append(attended.reshape(row_count, HEADS * HEAD))
    return jnp.concatenate(attended_all, axis=0), saved


def fallback_attention_backward(saved, attended_grad, row_count):
    factor = HEAD ** (-0.5)
    proj = []
    for m, (qh, k_all, v_all, weights, totals, attended) in enumerate(saved):
        grad = attended_grad[m * row_count : (m + 1) * row_count].astype(jnp.float32)
        grad = grad.reshape(row_count, HEADS, HEAD)
        delta = jnp.sum(grad * attended, axis=-1).T / totals
        grad_heads = (grad / totals.T[:, :, None]).astype(jnp.bfloat16)
        products = jnp.einsum("rhd,khd->hrk", grad_heads, v_all, preferred_element_type=jnp.float32)
        score_grad = (weights * (products - delta[:, :, None])).astype(jnp.bfloat16)
        q_grad = jnp.einsum("hrk,khd->rhd", score_grad, k_all, preferred_element_type=jnp.float32) * factor
        k_rows = jnp.einsum("hrk,rhd->khd", score_grad, qh, preferred_element_type=jnp.float32) * factor
        v_rows = jnp.einsum(
            "hrk,rhd->khd", weights.astype(jnp.bfloat16), grad_heads, preferred_element_type=jnp.float32
        )
        width = HEADS * HEAD
        k_own = lax.psum_scatter(
            k_rows.reshape(-1, width).astype(jnp.bfloat16), "seq", scatter_dimension=0, tiled=True
        )
        v_own = lax.psum_scatter(
            v_rows.reshape(-1, width).astype(jnp.bfloat16), "seq", scatter_dimension=0, tiled=True
        )
        proj.append(
            jnp.concatenate(
                [q_grad.reshape(row_count, width).astype(jnp.bfloat16), k_own, v_own], axis=1
            )
        )
    return jnp.concatenate(proj, axis=0)


def body(inputs, cotangent, bounds, *shards):
    micro = inputs.shape[0]
    row_count = inputs.shape[2]
    width = inputs.shape[3]
    ff = shards[9].shape[1]
    rows = micro * row_count
    seq_count = lax.axis_size("seq")
    unit_count = micro * HEADS
    head_parallel = unit_count % seq_count == 0
    per_device = unit_count // seq_count
    dp_count = lax.axis_size("dp")
    count = dp_count * seq_count
    me = lax.axis_index("dp") * seq_count + lax.axis_index("seq")
    orders = route_orders(dp_count, seq_count)
    steps = len(orders[0])
    ln1_g, ln1_b, w_qkv, b_q, b_v, w_out, b_out, ln2_g, ln2_b, w_up, b_up, w_down, b_down = shards
    shard_rows = w_qkv.shape[0]
    ratio = ff // width
    vec_sizes = [1] * 8 + [ratio]
    vecs_local = vector_block(
        [ln1_g, ln1_b, b_q, b_v, b_out, ln2_g, ln2_b, b_down, b_up], shard_rows, jnp.bfloat16
    )
    mlp_pack = jnp.concatenate([w_out, w_up, w_down.reshape(shard_rows, ratio * width)], axis=1)
    qkv_cols = thirds(w_qkv.shape[1])
    qkv_parts = split_cols(w_qkv, qkv_cols)
    gathered = gather_routes(
        [qkv_parts[0], qkv_parts[1], jnp.concatenate([qkv_parts[2], vecs_local], axis=1)],
        orders,
        count,
        me,
    )
    last_qkv, vecs_all = split_cols(gathered[2], [qkv_cols[2], vecs_local.shape[1]])
    qkv_weights = [gathered[0], gathered[1], last_qkv]
    (
        gain_one,
        shift_one,
        bias_query,
        bias_value,
        bias_out,
        gain_two,
        shift_two,
        bias_down,
        bias_up,
    ) = vector_unblock(vecs_all, vec_sizes)

    seq_in = inputs[:, 0].reshape(rows, width).astype(jnp.float32)
    normed_f, norm_one_back = jax.vjp(
        layer_norm, seq_in, gain_one.astype(jnp.float32), shift_one.astype(jnp.float32)
    )
    normed = normed_f.astype(jnp.bfloat16)
    if qkv_cols == [width] * 3:
        proj_q, proj_k, proj_v = [
            jnp.dot(normed, w, preferred_element_type=jnp.float32) for w in qkv_weights
        ]
    else:
        projected = jnp.dot(
            normed, jnp.concatenate(qkv_weights, axis=1), preferred_element_type=jnp.float32
        )
        proj_q, proj_k, proj_v = split_cols(projected, [width] * 3)
    queries = (proj_q + bias_query.astype(jnp.float32)).astype(jnp.bfloat16)
    keys_now = proj_k.astype(jnp.bfloat16)
    values_now = (proj_v + bias_value.astype(jnp.float32)).astype(jnp.bfloat16)

    if head_parallel:
        qkv_rows = jnp.concatenate([queries, keys_now, values_now], axis=1)
        qkv_units = rows_to_units(
            qkv_rows.reshape(micro, row_count, 3, HEADS, HEAD), seq_count, per_device, 3
        )
        uq, uk, uv = qkv_units[:, :, 0], qkv_units[:, :, 1], qkv_units[:, :, 2]
        allowed = unit_masks(unit_bounds(bounds, unit_count, per_device), seq_count * row_count)
        weights, totals, attended_u = unit_forward(uq, uk, uv, allowed)
        attended_b = units_to_rows(
            attended_u.astype(jnp.bfloat16)[:, :, None], seq_count, micro, 1
        )
        forward_anchors = [normed, qkv_units, weights, attended_u, attended_u]
    else:
        attended, saved = fallback_attention(queries, keys_now, values_now, bounds, row_count)
        attended_b = attended.astype(jnp.bfloat16)
        forward_anchors = [queries] + [attended] * (steps - 1)

    proj_out, proj_up, down_view = split_cols(
        lax.all_gather(mlp_pack, ALL, axis=0, tiled=True), [width, ff, ff]
    )
    proj_down = down_view.reshape(count * shard_rows * ratio, width)

    branch = jnp.dot(attended_b, proj_out, preferred_element_type=jnp.float32) + bias_out.astype(
        jnp.float32
    )
    middle = seq_in + branch
    normed_two_f, norm_two_back = jax.vjp(
        layer_norm, middle, gain_two.astype(jnp.float32), shift_two.astype(jnp.float32)
    )
    normed_two = normed_two_f.astype(jnp.bfloat16)
    hidden = jnp.dot(normed_two, proj_up, preferred_element_type=jnp.float32) + bias_up.astype(
        jnp.float32
    )
    activated_f, gelu_back = jax.vjp(partial(jax.nn.gelu, approximate=False), hidden)
    activated = activated_f.astype(jnp.bfloat16)
    mlp_out = jnp.dot(activated, proj_down, preferred_element_type=jnp.float32) + bias_down.astype(
        jnp.float32
    )
    outputs = (middle + mlp_out).astype(jnp.bfloat16)

    out_grad = cotangent[:, 0].reshape(rows, width)
    out_grad_f = out_grad.astype(jnp.float32)
    grad_down = outer_rows(activated, out_grad)
    grad_bias_down = jnp.sum(out_grad_f, axis=0)
    act_grad = times_transposed(out_grad, proj_down)
    (hidden_grad,) = gelu_back(act_grad)
    hidden_grad_b = hidden_grad.astype(jnp.bfloat16)
    grad_up = outer_rows(normed_two, hidden_grad_b)
    grad_bias_up = jnp.sum(hidden_grad_b.astype(jnp.float32), axis=0)
    normed_two_grad = times_transposed(hidden_grad_b, proj_up)
    middle_ln_grad, grad_gain_two, grad_shift_two = norm_two_back(normed_two_grad)
    middle_grad = out_grad_f + middle_ln_grad
    branch_grad = middle_grad.astype(jnp.bfloat16)
    grad_out = outer_rows(attended_b, branch_grad)
    grad_bias_out = jnp.sum(branch_grad.astype(jnp.float32), axis=0)
    attended_grad = times_transposed(branch_grad, proj_out).astype(jnp.bfloat16)

    if head_parallel:
        grad_units = rows_to_units(
            attended_grad.reshape(micro, row_count, 1, HEADS, HEAD), seq_count, per_device, 1
        )[:, :, 0]
        qkv_grad_u = unit_backward(uq, uk, uv, weights, totals, attended_u, grad_units)
        proj_grad = units_to_rows(qkv_grad_u, seq_count, micro, 3)
        backward_anchors = [None, grad_units, qkv_grad_u, proj_grad, proj_grad]
    else:
        proj_grad = fallback_attention_backward(saved, attended_grad, row_count)
        backward_anchors = [None] + [proj_grad] * (steps - 1)

    full_rows = count * shard_rows
    vec_one = vector_block(
        [grad_bias_up, grad_bias_down, grad_gain_two, grad_shift_two], full_rows, jnp.float32
    )
    red_down = lax.psum_scatter(
        grad_down.astype(jnp.bfloat16), ALL, scatter_dimension=0, tiled=True
    ).astype(jnp.float32)
    up_cols = [ff // 2, ff - ff // 2]
    up_parts = split_cols(grad_up, up_cols)
    red_up_a, red_up_b, red_mixed = reduce_routes(
        [up_parts[0], up_parts[1], jnp.concatenate([grad_out, vec_one], axis=1)],
        orders,
        count,
        me,
        backward_anchors[:steps],
    )
    red_up = jnp.concatenate([red_up_a, red_up_b], axis=1)
    red_out, red_vec_one = split_cols(red_mixed, [width, vec_one.shape[1]])

    grad_bias_query = jnp.sum(proj_grad[:, :width].astype(jnp.float32), axis=0)
    grad_bias_value = jnp.sum(proj_grad[:, 2 * width :].astype(jnp.float32), axis=0)
    grad_parts = split_cols(proj_grad, qkv_cols)
    grad_qkv = [outer_rows(normed, g) for g in grad_parts]
    normed_grad = times_transposed(grad_parts[0], qkv_weights[0])
    for g, w in zip(grad_parts[1:], qkv_weights[1:]):
        normed_grad = normed_grad + times_transposed(g, w)
    input_ln_grad, grad_gain_one, grad_shift_one = norm_one_back(normed_grad)
    input_grads = (middle_grad + input_ln_grad).astype(jnp.bfloat16)

    vec_two = vector_block(
        [grad_gain_one, grad_shift_one, grad_bias_query, grad_bias_value, grad_bias_out],
        full_rows,
        jnp.float32,
    )
    red = reduce_routes(
        [grad_qkv[0], grad_qkv[1], jnp.concatenate([grad_qkv[2], vec_two], axis=1)],
        orders,
        count,
        me,
    )
    red_last, red_vec_two = split_cols(red[2], [qkv_cols[2], vec_two.shape[1]])
    red_qkv = jnp.concatenate([red[0], red[1], red_last], axis=1)
    r_bias_up, r_bias_down, r_gain_two, r_shift_two = vector_unblock(red_vec_one, [ratio, 1, 1, 1])
    r_gain_one, r_shift_one, r_bias_query, r_bias_value, r_bias_out = vector_unblock(
        red_vec_two, [1] * 5
    )
    reduced = (
        r_gain_one,
        r_shift_one,
        red_qkv,
        r_bias_query,
        r_bias_value,
        red_out,
        r_bias_out,
        r_gain_two,
        r_shift_two,
        red_up,
        r_bias_up,
        red_down,
        r_bias_down,
    )
    return (
        outputs.reshape(micro, 1, row_count, width),
        input_grads.reshape(micro, 1, row_count, width),
    ) + reduced


def solution(mesh):
    vec = P(ALL)
    mat = P(ALL, None)
    param_specs = (vec, vec, mat, vec, vec, mat, vec, vec, vec, mat, vec, mat, vec)
    return jax.shard_map(
        body,
        mesh=mesh,
        in_specs=(P(None, "dp", "seq", None), P(None, "dp", "seq", None), P(None, "dp", None, None))
        + param_specs,
        out_specs=(P(None, "dp", "seq", None), P(None, "dp", "seq", None)) + param_specs,
        check_vma=False,
    )
```

```python
from functools import partial

import jax
import jax.numpy as jnp
from jax import lax
from jax.sharding import PartitionSpec as P

HEADS = 12
HEAD = 64
EPSILON = 1e-05
ALL = ("dp", "seq")


def layer_norm(values, ln_gain, ln_shift):
    center = jnp.mean(values, axis=-1, keepdims=True)
    centered = values - center
    spread = jnp.mean(centered * centered, axis=-1, keepdims=True)
    return centered * lax.rsqrt(spread + EPSILON) * ln_gain + ln_shift


def piece_label(positions, bounds):
    inside = (positions[:, None] >= bounds[None, :, 0]) & (positions[:, None] < bounds[None, :, 1])
    labels = jnp.arange(1, bounds.shape[0] + 1, dtype=jnp.int32)
    return jnp.sum(jnp.where(inside, labels[None, :], 0), axis=1) - 1


def allowed_mask(query_pos, key_pos, bounds):
    query_label = piece_label(query_pos, bounds)
    key_label = piece_label(key_pos, bounds)
    causal = key_pos[None, :] <= query_pos[:, None]
    same_piece = (query_label[:, None] == key_label[None, :]) & (query_label[:, None] >= 0)
    return causal | same_piece


def outer_rows(left, right):
    return lax.dot_general(
        left, right, (((0,), (0,)), ((), ())), preferred_element_type=jnp.float32
    )


def times_transposed(left, right):
    return lax.dot_general(
        left, right, (((1,), (1,)), ((), ())), preferred_element_type=jnp.float32
    )


def route_orders(dp_size, seq_size):
    nbits = (dp_size * seq_size).bit_length() - 1
    if (dp_size, seq_size) == (4, 8):
        return [(3, 4, 0, 1, 2), (3, 0, 1, 4, 2), (3, 1, 4, 0, 2)]
    core = (seq_size.bit_length() - 1) if dp_size > 1 else None
    others = [b for b in range(nbits) if b != core]
    head = [core] if core is not None else []
    return [tuple(head + others[i:] + others[:i]) for i in range(3)]


def partner_pairs(count, bit):
    return [(i, i ^ (1 << bit)) for i in range(count)]


def tie(values, anchor):
    if anchor is None:
        return values
    values, _ = lax.optimization_barrier((values, anchor))
    return values


def gather_routes(routes, orders, count, me, anchors=None):
    nbits = count.bit_length() - 1
    idx = jnp.arange(count, dtype=jnp.int32)
    out = []
    for x, order in zip(routes, orders):
        rows, cols = x.shape
        for step, b in enumerate(reversed(order)):
            if anchors is not None:
                x = tie(x, anchors[step])
            got = lax.ppermute(x, ALL, partner_pairs(count, b))
            x = jnp.stack([x, got])
        rel = jnp.zeros((count,), jnp.int32)
        for j, b in enumerate(order):
            rel = rel + ((((idx >> b) & 1) ^ ((me >> b) & 1)) << (nbits - 1 - j))
        x = jnp.take(x.reshape(count, rows, cols), rel, axis=0)
        out.append(x.reshape(count * rows, cols))
    return out


def reduce_routes(routes, orders, count, me, anchors=None):
    nbits = count.bit_length() - 1
    out = []
    for x, order in zip(routes, orders):
        rows = x.shape[0] // count
        cols = x.shape[1]
        x = x.reshape([2] * nbits + [rows, cols])
        remaining = list(range(nbits - 1, -1, -1))
        for step, b in enumerate(order):
            if anchors is not None:
                x = tie(x, anchors[step])
            axis = remaining.index(b)
            mine = (me >> b) & 1
            keep = lax.dynamic_index_in_dim(x, mine, axis, keepdims=False)
            send = lax.dynamic_index_in_dim(x, 1 - mine, axis, keepdims=False).astype(jnp.bfloat16)
            got = lax.ppermute(send, ALL, partner_pairs(count, b))
            x = keep + got.astype(jnp.float32)
            remaining.pop(axis)
        out.append(x.reshape(rows, cols))
    return out


def split_cols(x, widths):
    out, at = [], 0
    for w in widths:
        out.append(x[:, at : at + w])
        at += w
    return out


def thirds(width, grain=128):
    first = -(-width // (3 * grain)) * grain
    return [first, first, width - 2 * first]


def vector_block(vectors, rows, dtype):
    cols = [v.reshape(rows, -1).astype(dtype) for v in vectors]
    used = sum(c.shape[1] for c in cols)
    pad = -(-used // 128) * 128 - used
    if pad:
        cols.append(jnp.zeros((rows, pad), dtype))
    return jnp.concatenate(cols, axis=1)


def vector_unblock(block, sizes):
    out, at = [], 0
    rows = block.shape[0]
    for s in sizes:
        out.append(block[:, at : at + s].reshape(rows * s))
        at += s
    return out


def unit_bounds(bounds, unit_count, per_device):
    first = lax.axis_index("seq") * per_device
    micro = (first + jnp.arange(per_device, dtype=jnp.int32)) // HEADS
    return bounds[:, 0][micro]


def unit_masks(ubounds, length):
    pos = jnp.arange(length, dtype=jnp.int32)
    return jax.vmap(lambda b: allowed_mask(pos, pos, b))(ubounds)


def rows_to_units(x, seq_count, per_device, parts):
    micro, rows = x.shape[0], x.shape[1]
    x = jnp.transpose(x, (0, 3, 1, 2, 4)).reshape(seq_count, per_device, rows, parts, HEAD)
    x = lax.all_to_all(x, "seq", 0, 0, tiled=True)
    x = jnp.transpose(x, (1, 0, 2, 3, 4))
    return x.reshape(per_device, seq_count * rows, parts, HEAD)


def units_to_rows(x, seq_count, micro, parts):
    per_device, length = x.shape[0], x.shape[1]
    rows = length // seq_count
    x = x.reshape(per_device, seq_count, rows, parts, HEAD)
    x = jnp.transpose(x, (1, 0, 2, 3, 4))
    x = lax.all_to_all(x, "seq", 0, 0, tiled=True)
    x = x.reshape(micro, HEADS, rows, parts, HEAD)
    x = jnp.transpose(x, (0, 2, 3, 1, 4))
    return x.reshape(micro * rows, parts * HEADS * HEAD)


def unit_forward(q, k, v, allowed):
    factor = q.shape[-1] ** (-0.5)
    scores = jnp.einsum("uqd,ukd->uqk", q, k, preferred_element_type=jnp.float32) * factor
    weights = jnp.where(allowed, jnp.exp(scores), 0.0)
    totals = jnp.sum(weights, axis=-1)
    summed = jnp.einsum(
        "uqk,ukd->uqd", weights.astype(jnp.bfloat16), v, preferred_element_type=jnp.float32
    )
    return weights, totals, summed / totals[:, :, None]


def unit_backward(q, k, v, weights, totals, attended, attended_grad):
    factor = q.shape[-1] ** (-0.5)
    grad_f = attended_grad.astype(jnp.float32)
    delta = jnp.sum(grad_f * attended, axis=-1) / totals
    summed_grad = (grad_f / totals[:, :, None]).astype(jnp.bfloat16)
    products = jnp.einsum("uqd,ukd->uqk", summed_grad, v, preferred_element_type=jnp.float32)
    score_grad = (weights * (products - delta[:, :, None])).astype(jnp.bfloat16)
    q_grad = jnp.einsum("uqk,ukd->uqd", score_grad, k, preferred_element_type=jnp.float32) * factor
    k_grad = jnp.einsum("uqk,uqd->ukd", score_grad, q, preferred_element_type=jnp.float32) * factor
    v_grad = jnp.einsum(
        "uqk,uqd->ukd", weights.astype(jnp.bfloat16), summed_grad, preferred_element_type=jnp.float32
    )
    return jnp.stack([q_grad, k_grad, v_grad], axis=2).astype(jnp.bfloat16)


def fallback_attention(queries, keys, values, bounds, row_count):
    micro = bounds.shape[0]
    seq_count = lax.axis_size("seq")
    total_len = row_count * seq_count
    query_pos = lax.axis_index("seq") * row_count + jnp.arange(row_count, dtype=jnp.int32)
    key_pos = jnp.arange(total_len, dtype=jnp.int32)
    saved = []
    attended_all = []
    for m in range(micro):
        sl = slice(m * row_count, (m + 1) * row_count)
        qh = queries[sl].reshape(row_count, HEADS, HEAD)
        k_all = lax.all_gather(keys[sl], "seq", axis=0, tiled=True).reshape(total_len, HEADS, HEAD)
        v_all = lax.all_gather(values[sl], "seq", axis=0, tiled=True).reshape(total_len, HEADS, HEAD)
        allowed = allowed_mask(query_pos, key_pos, bounds[m, 0])
        scores = jnp.einsum("rhd,khd->hrk", qh, k_all, preferred_element_type=jnp.float32) * HEAD ** (-0.5)
        weights = jnp.where(allowed[None], jnp.exp(scores), 0.0)
        totals = jnp.sum(weights, axis=-1)
        summed = jnp.einsum(
            "hrk,khd->rhd", weights.astype(jnp.bfloat16), v_all, preferred_element_type=jnp.float32
        )
        attended = summed / totals.T[:, :, None]
        saved.append((qh, k_all, v_all, weights, totals, attended))
        attended_all.append(attended.reshape(row_count, HEADS * HEAD))
    return jnp.concatenate(attended_all, axis=0), saved


def fallback_attention_backward(saved, attended_grad, row_count):
    factor = HEAD ** (-0.5)
    proj = []
    for m, (qh, k_all, v_all, weights, totals, attended) in enumerate(saved):
        grad = attended_grad[m * row_count : (m + 1) * row_count].astype(jnp.float32)
        grad = grad.reshape(row_count, HEADS, HEAD)
        delta = jnp.sum(grad * attended, axis=-1).T / totals
        grad_heads = (grad / totals.T[:, :, None]).astype(jnp.bfloat16)
        products = jnp.einsum("rhd,khd->hrk", grad_heads, v_all, preferred_element_type=jnp.float32)
        score_grad = (weights * (products - delta[:, :, None])).astype(jnp.bfloat16)
        q_grad = jnp.einsum("hrk,khd->rhd", score_grad, k_all, preferred_element_type=jnp.float32) * factor
        k_rows = jnp.einsum("hrk,rhd->khd", score_grad, qh, preferred_element_type=jnp.float32) * factor
        v_rows = jnp.einsum(
            "hrk,rhd->khd", weights.astype(jnp.bfloat16), grad_heads, preferred_element_type=jnp.float32
        )
        width = HEADS * HEAD
        k_own = lax.psum_scatter(
            k_rows.reshape(-1, width).astype(jnp.bfloat16), "seq", scatter_dimension=0, tiled=True
        )
        v_own = lax.psum_scatter(
            v_rows.reshape(-1, width).astype(jnp.bfloat16), "seq", scatter_dimension=0, tiled=True
        )
        proj.append(
            jnp.concatenate(
                [q_grad.reshape(row_count, width).astype(jnp.bfloat16), k_own, v_own], axis=1
            )
        )
    return jnp.concatenate(proj, axis=0)


def body(inputs, cotangent, bounds, *shards):
    micro = inputs.shape[0]
    row_count = inputs.shape[2]
    width = inputs.shape[3]
    ff = shards[9].shape[1]
    rows = micro * row_count
    seq_count = lax.axis_size("seq")
    unit_count = micro * HEADS
    head_parallel = unit_count % seq_count == 0
    per_device = unit_count // seq_count
    dp_count = lax.axis_size("dp")
    count = dp_count * seq_count
    me = lax.axis_index("dp") * seq_count + lax.axis_index("seq")
    orders = route_orders(dp_count, seq_count)
    steps = len(orders[0])
    ln1_g, ln1_b, w_qkv, b_q, b_v, w_out, b_out, ln2_g, ln2_b, w_up, b_up, w_down, b_down = shards
    shard_rows = w_qkv.shape[0]
    ratio = ff // width
    vec_sizes = [1] * 8 + [ratio]
    vecs_local = vector_block(
        [ln1_g, ln1_b, b_q, b_v, b_out, ln2_g, ln2_b, b_down, b_up], shard_rows, jnp.bfloat16
    )
    mlp_pack = jnp.concatenate([w_out, w_up, w_down.reshape(shard_rows, ratio * width)], axis=1)
    qkv_cols = thirds(w_qkv.shape[1])
    qkv_parts = split_cols(w_qkv, qkv_cols)
    gathered = gather_routes(
        [qkv_parts[0], qkv_parts[1], jnp.concatenate([qkv_parts[2], vecs_local], axis=1)],
        orders,
        count,
        me,
    )
    last_qkv, vecs_all = split_cols(gathered[2], [qkv_cols[2], vecs_local.shape[1]])
    qkv_weights = [gathered[0], gathered[1], last_qkv]
    (
        gain_one,
        shift_one,
        bias_query,
        bias_value,
        bias_out,
        gain_two,
        shift_two,
        bias_down,
        bias_up,
    ) = vector_unblock(vecs_all, vec_sizes)

    seq_in = inputs[:, 0].reshape(rows, width).astype(jnp.float32)
    normed_f, norm_one_back = jax.vjp(
        layer_norm, seq_in, gain_one.astype(jnp.float32), shift_one.astype(jnp.float32)
    )
    normed = normed_f.astype(jnp.bfloat16)
    if qkv_cols == [width] * 3:
        proj_q, proj_k, proj_v = [
            jnp.dot(normed, w, preferred_element_type=jnp.float32) for w in qkv_weights
        ]
    else:
        projected = jnp.dot(
            normed, jnp.concatenate(qkv_weights, axis=1), preferred_element_type=jnp.float32
        )
        proj_q, proj_k, proj_v = split_cols(projected, [width] * 3)
    queries = (proj_q + bias_query.astype(jnp.float32)).astype(jnp.bfloat16)
    keys_now = proj_k.astype(jnp.bfloat16)
    values_now = (proj_v + bias_value.astype(jnp.float32)).astype(jnp.bfloat16)

    if head_parallel:
        qkv_rows = jnp.concatenate([queries, keys_now, values_now], axis=1)
        qkv_units = rows_to_units(
            qkv_rows.reshape(micro, row_count, 3, HEADS, HEAD), seq_count, per_device, 3
        )
        uq, uk, uv = qkv_units[:, :, 0], qkv_units[:, :, 1], qkv_units[:, :, 2]
        allowed = unit_masks(unit_bounds(bounds, unit_count, per_device), seq_count * row_count)
        weights, totals, attended_u = unit_forward(uq, uk, uv, allowed)
        attended_b = units_to_rows(
            attended_u.astype(jnp.bfloat16)[:, :, None], seq_count, micro, 1
        )
        forward_anchors = [normed, qkv_units, weights, attended_u, attended_u]
    else:
        attended, saved = fallback_attention(queries, keys_now, values_now, bounds, row_count)
        attended_b = attended.astype(jnp.bfloat16)
        forward_anchors = [queries] + [attended] * (steps - 1)

    proj_out, proj_up, down_view = split_cols(
        lax.all_gather(mlp_pack, ALL, axis=0, tiled=True), [width, ff, ff]
    )
    down_parts = split_cols(down_view, [width] * ratio)

    branch = jnp.dot(attended_b, proj_out, preferred_element_type=jnp.float32) + bias_out.astype(
        jnp.float32
    )
    middle = seq_in + branch
    normed_two_f, norm_two_back = jax.vjp(
        layer_norm, middle, gain_two.astype(jnp.float32), shift_two.astype(jnp.float32)
    )
    normed_two = normed_two_f.astype(jnp.bfloat16)
    hidden = jnp.dot(normed_two, proj_up, preferred_element_type=jnp.float32) + bias_up.astype(
        jnp.float32
    )
    activated_f, gelu_back = jax.vjp(partial(jax.nn.gelu, approximate=False), hidden)
    activated = activated_f.astype(jnp.bfloat16)
    mlp_sum = None
    for c, part in enumerate(down_parts):
        term = jnp.dot(activated[:, c::ratio], part, preferred_element_type=jnp.float32)
        mlp_sum = term if mlp_sum is None else mlp_sum + term
    mlp_out = mlp_sum + bias_down.astype(jnp.float32)
    outputs = (middle + mlp_out).astype(jnp.bfloat16)

    out_grad = cotangent[:, 0].reshape(rows, width)
    out_grad_f = out_grad.astype(jnp.float32)
    grad_down = outer_rows(activated, out_grad)
    grad_bias_down = jnp.sum(out_grad_f, axis=0)
    act_grad = jnp.stack([times_transposed(out_grad, part) for part in down_parts], axis=-1)
    act_grad = act_grad.reshape(rows, ratio * width)
    (hidden_grad,) = gelu_back(act_grad)
    hidden_grad_b = hidden_grad.astype(jnp.bfloat16)
    grad_up = outer_rows(normed_two, hidden_grad_b)
    grad_bias_up = jnp.sum(hidden_grad_b.astype(jnp.float32), axis=0)
    normed_two_grad = times_transposed(hidden_grad_b, proj_up)
    middle_ln_grad, grad_gain_two, grad_shift_two = norm_two_back(normed_two_grad)
    middle_grad = out_grad_f + middle_ln_grad
    branch_grad = middle_grad.astype(jnp.bfloat16)
    grad_out = outer_rows(attended_b, branch_grad)
    grad_bias_out = jnp.sum(branch_grad.astype(jnp.float32), axis=0)
    attended_grad = times_transposed(branch_grad, proj_out).astype(jnp.bfloat16)

    if head_parallel:
        grad_units = rows_to_units(
            attended_grad.reshape(micro, row_count, 1, HEADS, HEAD), seq_count, per_device, 1
        )[:, :, 0]
        qkv_grad_u = unit_backward(uq, uk, uv, weights, totals, attended_u, grad_units)
        proj_grad = units_to_rows(qkv_grad_u, seq_count, micro, 3)
        backward_anchors = [None, grad_units, qkv_grad_u, proj_grad, proj_grad]
    else:
        proj_grad = fallback_attention_backward(saved, attended_grad, row_count)
        backward_anchors = [None] + [proj_grad] * (steps - 1)

    full_rows = count * shard_rows
    vec_one = vector_block(
        [grad_bias_up, grad_bias_down, grad_gain_two, grad_shift_two], full_rows, jnp.float32
    )
    red_up, red_down, red_mixed = reduce_routes(
        [grad_up, grad_down, jnp.concatenate([grad_out, vec_one], axis=1)],
        orders,
        count,
        me,
        backward_anchors[:steps],
    )
    red_out, red_vec_one = split_cols(red_mixed, [width, vec_one.shape[1]])

    grad_bias_query = jnp.sum(proj_grad[:, :width].astype(jnp.float32), axis=0)
    grad_bias_value = jnp.sum(proj_grad[:, 2 * width :].astype(jnp.float32), axis=0)
    grad_parts = split_cols(proj_grad, qkv_cols)
    grad_qkv = [outer_rows(normed, g) for g in grad_parts]
    normed_grad = times_transposed(grad_parts[0], qkv_weights[0])
    for g, w in zip(grad_parts[1:], qkv_weights[1:]):
        normed_grad = normed_grad + times_transposed(g, w)
    input_ln_grad, grad_gain_one, grad_shift_one = norm_one_back(normed_grad)
    input_grads = (middle_grad + input_ln_grad).astype(jnp.bfloat16)

    vec_two = vector_block(
        [grad_gain_one, grad_shift_one, grad_bias_query, grad_bias_value, grad_bias_out],
        full_rows,
        jnp.float32,
    )
    red = reduce_routes(
        [grad_qkv[0], grad_qkv[1], jnp.concatenate([grad_qkv[2], vec_two], axis=1)],
        orders,
        count,
        me,
    )
    red_last, red_vec_two = split_cols(red[2], [qkv_cols[2], vec_two.shape[1]])
    red_qkv = jnp.concatenate([red[0], red[1], red_last], axis=1)
    r_bias_up, r_bias_down, r_gain_two, r_shift_two = vector_unblock(red_vec_one, [ratio, 1, 1, 1])
    r_gain_one, r_shift_one, r_bias_query, r_bias_value, r_bias_out = vector_unblock(
        red_vec_two, [1] * 5
    )
    reduced = (
        r_gain_one,
        r_shift_one,
        red_qkv,
        r_bias_query,
        r_bias_value,
        red_out,
        r_bias_out,
        r_gain_two,
        r_shift_two,
        red_up,
        r_bias_up,
        red_down,
        r_bias_down,
    )
    return (
        outputs.reshape(micro, 1, row_count, width),
        input_grads.reshape(micro, 1, row_count, width),
    ) + reduced


def solution(mesh):
    vec = P(ALL)
    mat = P(ALL, None)
    param_specs = (vec, vec, mat, vec, vec, mat, vec, vec, vec, mat, vec, mat, vec)
    return jax.shard_map(
        body,
        mesh=mesh,
        in_specs=(P(None, "dp", "seq", None), P(None, "dp", "seq", None), P(None, "dp", None, None))
        + param_specs,
        out_specs=(P(None, "dp", "seq", None), P(None, "dp", "seq", None)) + param_specs,
        check_vma=False,
    )
```

```python
from functools import partial

import jax
import jax.numpy as jnp
from jax import lax
from jax.sharding import PartitionSpec as P

HEADS = 12
HEAD = 64
EPSILON = 1e-05
ALL = ("dp", "seq")


def layer_norm(values, ln_gain, ln_shift):
    center = jnp.mean(values, axis=-1, keepdims=True)
    centered = values - center
    spread = jnp.mean(centered * centered, axis=-1, keepdims=True)
    return centered * lax.rsqrt(spread + EPSILON) * ln_gain + ln_shift


def piece_label(positions, bounds):
    inside = (positions[:, None] >= bounds[None, :, 0]) & (positions[:, None] < bounds[None, :, 1])
    labels = jnp.arange(1, bounds.shape[0] + 1, dtype=jnp.int32)
    return jnp.sum(jnp.where(inside, labels[None, :], 0), axis=1) - 1


def allowed_mask(query_pos, key_pos, bounds):
    query_label = piece_label(query_pos, bounds)
    key_label = piece_label(key_pos, bounds)
    causal = key_pos[None, :] <= query_pos[:, None]
    same_piece = (query_label[:, None] == key_label[None, :]) & (query_label[:, None] >= 0)
    return causal | same_piece


def outer_rows(left, right):
    return lax.dot_general(
        left, right, (((0,), (0,)), ((), ())), preferred_element_type=jnp.float32
    )


def times_transposed(left, right):
    return lax.dot_general(
        left, right, (((1,), (1,)), ((), ())), preferred_element_type=jnp.float32
    )


def route_orders(dp_size, seq_size):
    nbits = (dp_size * seq_size).bit_length() - 1
    if (dp_size, seq_size) == (4, 8):
        return [(3, 4, 0, 1, 2), (3, 0, 1, 4, 2), (3, 1, 4, 0, 2)]
    core = (seq_size.bit_length() - 1) if dp_size > 1 else None
    others = [b for b in range(nbits) if b != core]
    head = [core] if core is not None else []
    return [tuple(head + others[i:] + others[:i]) for i in range(3)]


def partner_pairs(count, bit):
    return [(i, i ^ (1 << bit)) for i in range(count)]


def tie(values, anchor):
    if anchor is None:
        return values
    values, _ = lax.optimization_barrier((values, anchor))
    return values


def gather_routes(routes, orders, count, me, anchors=None):
    nbits = count.bit_length() - 1
    idx = jnp.arange(count, dtype=jnp.int32)
    out = []
    for x, order in zip(routes, orders):
        rows, cols = x.shape
        for step, b in enumerate(reversed(order)):
            if anchors is not None:
                x = tie(x, anchors[step])
            got = lax.ppermute(x, ALL, partner_pairs(count, b))
            x = jnp.stack([x, got])
        rel = jnp.zeros((count,), jnp.int32)
        for j, b in enumerate(order):
            rel = rel + ((((idx >> b) & 1) ^ ((me >> b) & 1)) << (nbits - 1 - j))
        x = jnp.take(x.reshape(count, rows, cols), rel, axis=0)
        out.append(x.reshape(count * rows, cols))
    return out


def reduce_routes(routes, orders, count, me, anchors=None):
    nbits = count.bit_length() - 1
    out = []
    for x, order in zip(routes, orders):
        lead = list(x.shape[:-2])
        rows = x.shape[-2] // count
        cols = x.shape[-1]
        x = x.reshape(lead + [2] * nbits + [rows, cols])
        remaining = list(range(nbits - 1, -1, -1))
        for step, b in enumerate(order):
            if anchors is not None:
                x = tie(x, anchors[step])
            axis = len(lead) + remaining.index(b)
            mine = (me >> b) & 1
            keep = lax.dynamic_index_in_dim(x, mine, axis, keepdims=False)
            send = lax.dynamic_index_in_dim(x, 1 - mine, axis, keepdims=False).astype(jnp.bfloat16)
            got = lax.ppermute(send, ALL, partner_pairs(count, b))
            x = keep + got.astype(jnp.float32)
            remaining.pop(axis - len(lead))
        out.append(x.reshape(lead + [rows, cols]))
    return out


def split_cols(x, widths):
    out, at = [], 0
    for w in widths:
        out.append(x[:, at : at + w])
        at += w
    return out


def thirds(width, grain=128):
    first = -(-width // (3 * grain)) * grain
    return [first, first, width - 2 * first]


def vector_block(vectors, rows, dtype):
    cols = [v.reshape(rows, -1).astype(dtype) for v in vectors]
    used = sum(c.shape[1] for c in cols)
    pad = -(-used // 128) * 128 - used
    if pad:
        cols.append(jnp.zeros((rows, pad), dtype))
    return jnp.concatenate(cols, axis=1)


def vector_unblock(block, sizes):
    out, at = [], 0
    rows = block.shape[0]
    for s in sizes:
        out.append(block[:, at : at + s].reshape(rows * s))
        at += s
    return out


def unit_bounds(bounds, unit_count, per_device):
    first = lax.axis_index("seq") * per_device
    micro = (first + jnp.arange(per_device, dtype=jnp.int32)) // HEADS
    return bounds[:, 0][micro]


def unit_masks(ubounds, length):
    pos = jnp.arange(length, dtype=jnp.int32)
    return jax.vmap(lambda b: allowed_mask(pos, pos, b))(ubounds)


def rows_to_units(x, seq_count, per_device, parts):
    micro, rows = x.shape[0], x.shape[1]
    x = jnp.transpose(x, (0, 3, 1, 2, 4)).reshape(seq_count, per_device, rows, parts, HEAD)
    x = lax.all_to_all(x, "seq", 0, 0, tiled=True)
    x = jnp.transpose(x, (1, 0, 2, 3, 4))
    return x.reshape(per_device, seq_count * rows, parts, HEAD)


def units_to_rows(x, seq_count, micro, parts):
    per_device, length = x.shape[0], x.shape[1]
    rows = length // seq_count
    x = x.reshape(per_device, seq_count, rows, parts, HEAD)
    x = jnp.transpose(x, (1, 0, 2, 3, 4))
    x = lax.all_to_all(x, "seq", 0, 0, tiled=True)
    x = x.reshape(micro, HEADS, rows, parts, HEAD)
    x = jnp.transpose(x, (0, 2, 3, 1, 4))
    return x.reshape(micro * rows, parts * HEADS * HEAD)


def unit_forward(q, k, v, allowed):
    factor = q.shape[-1] ** (-0.5)
    scores = jnp.einsum("uqd,ukd->uqk", q, k, preferred_element_type=jnp.float32) * factor
    weights = jnp.where(allowed, jnp.exp(scores), 0.0)
    totals = jnp.sum(weights, axis=-1)
    summed = jnp.einsum(
        "uqk,ukd->uqd", weights.astype(jnp.bfloat16), v, preferred_element_type=jnp.float32
    )
    return weights, totals, summed / totals[:, :, None]


def unit_backward(q, k, v, weights, totals, attended, attended_grad):
    factor = q.shape[-1] ** (-0.5)
    grad_f = attended_grad.astype(jnp.float32)
    delta = jnp.sum(grad_f * attended, axis=-1) / totals
    summed_grad = (grad_f / totals[:, :, None]).astype(jnp.bfloat16)
    products = jnp.einsum("uqd,ukd->uqk", summed_grad, v, preferred_element_type=jnp.float32)
    score_grad = (weights * (products - delta[:, :, None])).astype(jnp.bfloat16)
    q_grad = jnp.einsum("uqk,ukd->uqd", score_grad, k, preferred_element_type=jnp.float32) * factor
    k_grad = jnp.einsum("uqk,uqd->ukd", score_grad, q, preferred_element_type=jnp.float32) * factor
    v_grad = jnp.einsum(
        "uqk,uqd->ukd", weights.astype(jnp.bfloat16), summed_grad, preferred_element_type=jnp.float32
    )
    return jnp.stack([q_grad, k_grad, v_grad], axis=2).astype(jnp.bfloat16)


def fallback_attention(queries, keys, values, bounds, row_count):
    micro = bounds.shape[0]
    seq_count = lax.axis_size("seq")
    total_len = row_count * seq_count
    query_pos = lax.axis_index("seq") * row_count + jnp.arange(row_count, dtype=jnp.int32)
    key_pos = jnp.arange(total_len, dtype=jnp.int32)
    saved = []
    attended_all = []
    for m in range(micro):
        sl = slice(m * row_count, (m + 1) * row_count)
        qh = queries[sl].reshape(row_count, HEADS, HEAD)
        k_all = lax.all_gather(keys[sl], "seq", axis=0, tiled=True).reshape(total_len, HEADS, HEAD)
        v_all = lax.all_gather(values[sl], "seq", axis=0, tiled=True).reshape(total_len, HEADS, HEAD)
        allowed = allowed_mask(query_pos, key_pos, bounds[m, 0])
        scores = jnp.einsum("rhd,khd->hrk", qh, k_all, preferred_element_type=jnp.float32) * HEAD ** (-0.5)
        weights = jnp.where(allowed[None], jnp.exp(scores), 0.0)
        totals = jnp.sum(weights, axis=-1)
        summed = jnp.einsum(
            "hrk,khd->rhd", weights.astype(jnp.bfloat16), v_all, preferred_element_type=jnp.float32
        )
        attended = summed / totals.T[:, :, None]
        saved.append((qh, k_all, v_all, weights, totals, attended))
        attended_all.append(attended.reshape(row_count, HEADS * HEAD))
    return jnp.concatenate(attended_all, axis=0), saved


def fallback_attention_backward(saved, attended_grad, row_count):
    factor = HEAD ** (-0.5)
    proj = []
    for m, (qh, k_all, v_all, weights, totals, attended) in enumerate(saved):
        grad = attended_grad[m * row_count : (m + 1) * row_count].astype(jnp.float32)
        grad = grad.reshape(row_count, HEADS, HEAD)
        delta = jnp.sum(grad * attended, axis=-1).T / totals
        grad_heads = (grad / totals.T[:, :, None]).astype(jnp.bfloat16)
        products = jnp.einsum("rhd,khd->hrk", grad_heads, v_all, preferred_element_type=jnp.float32)
        score_grad = (weights * (products - delta[:, :, None])).astype(jnp.bfloat16)
        q_grad = jnp.einsum("hrk,khd->rhd", score_grad, k_all, preferred_element_type=jnp.float32) * factor
        k_rows = jnp.einsum("hrk,rhd->khd", score_grad, qh, preferred_element_type=jnp.float32) * factor
        v_rows = jnp.einsum(
            "hrk,rhd->khd", weights.astype(jnp.bfloat16), grad_heads, preferred_element_type=jnp.float32
        )
        width = HEADS * HEAD
        k_own = lax.psum_scatter(
            k_rows.reshape(-1, width).astype(jnp.bfloat16), "seq", scatter_dimension=0, tiled=True
        )
        v_own = lax.psum_scatter(
            v_rows.reshape(-1, width).astype(jnp.bfloat16), "seq", scatter_dimension=0, tiled=True
        )
        proj.append(
            jnp.concatenate(
                [q_grad.reshape(row_count, width).astype(jnp.bfloat16), k_own, v_own], axis=1
            )
        )
    return jnp.concatenate(proj, axis=0)


def body(inputs, cotangent, bounds, *shards):
    micro = inputs.shape[0]
    row_count = inputs.shape[2]
    width = inputs.shape[3]
    ff = shards[9].shape[1]
    rows = micro * row_count
    seq_count = lax.axis_size("seq")
    unit_count = micro * HEADS
    head_parallel = unit_count % seq_count == 0
    per_device = unit_count // seq_count
    dp_count = lax.axis_size("dp")
    count = dp_count * seq_count
    me = lax.axis_index("dp") * seq_count + lax.axis_index("seq")
    orders = route_orders(dp_count, seq_count)
    steps = len(orders[0])
    ln1_g, ln1_b, w_qkv, b_q, b_v, w_out, b_out, ln2_g, ln2_b, w_up, b_up, w_down, b_down = shards
    shard_rows = w_qkv.shape[0]
    ratio = ff // width
    vec_sizes = [1] * 8 + [ratio]
    vecs_local = vector_block(
        [ln1_g, ln1_b, b_q, b_v, b_out, ln2_g, ln2_b, b_down, b_up], shard_rows, jnp.bfloat16
    )
    w_up_p = jnp.transpose(w_up.reshape(shard_rows, ff // ratio, ratio), (0, 2, 1)).reshape(
        shard_rows, ff
    )
    mlp_pack = jnp.concatenate([w_out, w_up_p, w_down.reshape(shard_rows, ratio * width)], axis=1)
    qkv_cols = thirds(w_qkv.shape[1])
    qkv_parts = split_cols(w_qkv, qkv_cols)
    gathered = gather_routes(
        [qkv_parts[0], qkv_parts[1], jnp.concatenate([qkv_parts[2], vecs_local], axis=1)],
        orders,
        count,
        me,
    )
    last_qkv, vecs_all = split_cols(gathered[2], [qkv_cols[2], vecs_local.shape[1]])
    qkv_weights = [gathered[0], gathered[1], last_qkv]
    (
        gain_one,
        shift_one,
        bias_query,
        bias_value,
        bias_out,
        gain_two,
        shift_two,
        bias_down,
        bias_up,
    ) = vector_unblock(vecs_all, vec_sizes)

    seq_in = inputs[:, 0].reshape(rows, width).astype(jnp.float32)
    normed_f, norm_one_back = jax.vjp(
        layer_norm, seq_in, gain_one.astype(jnp.float32), shift_one.astype(jnp.float32)
    )
    normed = normed_f.astype(jnp.bfloat16)
    if qkv_cols == [width] * 3:
        proj_q, proj_k, proj_v = [
            jnp.dot(normed, w, preferred_element_type=jnp.float32) for w in qkv_weights
        ]
    else:
        projected = jnp.dot(
            normed, jnp.concatenate(qkv_weights, axis=1), preferred_element_type=jnp.float32
        )
        proj_q, proj_k, proj_v = split_cols(projected, [width] * 3)
    queries = (proj_q + bias_query.astype(jnp.float32)).astype(jnp.bfloat16)
    keys_now = proj_k.astype(jnp.bfloat16)
    values_now = (proj_v + bias_value.astype(jnp.float32)).astype(jnp.bfloat16)

    if head_parallel:
        qkv_rows = jnp.concatenate([queries, keys_now, values_now], axis=1)
        qkv_units = rows_to_units(
            qkv_rows.reshape(micro, row_count, 3, HEADS, HEAD), seq_count, per_device, 3
        )
        uq, uk, uv = qkv_units[:, :, 0], qkv_units[:, :, 1], qkv_units[:, :, 2]
        allowed = unit_masks(unit_bounds(bounds, unit_count, per_device), seq_count * row_count)
        weights, totals, attended_u = unit_forward(uq, uk, uv, allowed)
        attended_b = units_to_rows(
            attended_u.astype(jnp.bfloat16)[:, :, None], seq_count, micro, 1
        )
        forward_anchors = [normed, qkv_units, weights, attended_u, attended_u]
    else:
        attended, saved = fallback_attention(queries, keys_now, values_now, bounds, row_count)
        attended_b = attended.astype(jnp.bfloat16)
        forward_anchors = [queries] + [attended] * (steps - 1)

    proj_out, proj_up, down_view = split_cols(
        lax.all_gather(mlp_pack, ALL, axis=0, tiled=True), [width, ff, ff]
    )
    down_parts = split_cols(down_view, [width] * ratio)
    bias_up_p = jnp.transpose(bias_up.reshape(ff // ratio, ratio)).reshape(ff)

    branch = jnp.dot(attended_b, proj_out, preferred_element_type=jnp.float32) + bias_out.astype(
        jnp.float32
    )
    middle = seq_in + branch
    normed_two_f, norm_two_back = jax.vjp(
        layer_norm, middle, gain_two.astype(jnp.float32), shift_two.astype(jnp.float32)
    )
    normed_two = normed_two_f.astype(jnp.bfloat16)
    hidden = jnp.dot(normed_two, proj_up, preferred_element_type=jnp.float32) + bias_up_p.astype(
        jnp.float32
    )
    activated_f, gelu_back = jax.vjp(partial(jax.nn.gelu, approximate=False), hidden)
    activated = activated_f.astype(jnp.bfloat16)
    act_parts = split_cols(activated, [width] * ratio)
    mlp_sum = jnp.dot(act_parts[0], down_parts[0], preferred_element_type=jnp.float32)
    for a, w in zip(act_parts[1:], down_parts[1:]):
        mlp_sum = mlp_sum + jnp.dot(a, w, preferred_element_type=jnp.float32)
    mlp_out = mlp_sum + bias_down.astype(jnp.float32)
    outputs = (middle + mlp_out).astype(jnp.bfloat16)

    out_grad = cotangent[:, 0].reshape(rows, width)
    out_grad_f = out_grad.astype(jnp.float32)
    grad_down = outer_rows(activated, out_grad).reshape(ratio, ff // ratio, width)
    grad_bias_down = jnp.sum(out_grad_f, axis=0)
    act_grad = jnp.concatenate([times_transposed(out_grad, w) for w in down_parts], axis=1)
    (hidden_grad,) = gelu_back(act_grad)
    hidden_grad_b = hidden_grad.astype(jnp.bfloat16)
    grad_up = outer_rows(normed_two, hidden_grad_b)
    grad_bias_up = jnp.transpose(
        jnp.sum(hidden_grad_b.astype(jnp.float32), axis=0).reshape(ratio, ff // ratio)
    ).reshape(ff)
    normed_two_grad = times_transposed(hidden_grad_b, proj_up)
    middle_ln_grad, grad_gain_two, grad_shift_two = norm_two_back(normed_two_grad)
    middle_grad = out_grad_f + middle_ln_grad
    branch_grad = middle_grad.astype(jnp.bfloat16)
    grad_out = outer_rows(attended_b, branch_grad)
    grad_bias_out = jnp.sum(branch_grad.astype(jnp.float32), axis=0)
    attended_grad = times_transposed(branch_grad, proj_out).astype(jnp.bfloat16)

    if head_parallel:
        grad_units = rows_to_units(
            attended_grad.reshape(micro, row_count, 1, HEADS, HEAD), seq_count, per_device, 1
        )[:, :, 0]
        qkv_grad_u = unit_backward(uq, uk, uv, weights, totals, attended_u, grad_units)
        proj_grad = units_to_rows(qkv_grad_u, seq_count, micro, 3)
        backward_anchors = [None, grad_units, qkv_grad_u, proj_grad, proj_grad]
    else:
        proj_grad = fallback_attention_backward(saved, attended_grad, row_count)
        backward_anchors = [None] + [proj_grad] * (steps - 1)

    full_rows = count * shard_rows
    vec_one = vector_block(
        [grad_bias_up, grad_bias_down, grad_gain_two, grad_shift_two], full_rows, jnp.float32
    )
    red_up, red_down, red_mixed = reduce_routes(
        [grad_up, grad_down, jnp.concatenate([grad_out, vec_one], axis=1)],
        orders,
        count,
        me,
        backward_anchors[:steps],
    )
    red_out, red_vec_one = split_cols(red_mixed, [width, vec_one.shape[1]])
    red_up = jnp.transpose(red_up.reshape(shard_rows, ratio, ff // ratio), (0, 2, 1)).reshape(
        shard_rows, ff
    )
    red_down = jnp.transpose(red_down, (1, 0, 2)).reshape(shard_rows * ratio, width)

    grad_bias_query = jnp.sum(proj_grad[:, :width].astype(jnp.float32), axis=0)
    grad_bias_value = jnp.sum(proj_grad[:, 2 * width :].astype(jnp.float32), axis=0)
    grad_parts = split_cols(proj_grad, qkv_cols)
    grad_qkv = [outer_rows(normed, g) for g in grad_parts]
    normed_grad = times_transposed(grad_parts[0], qkv_weights[0])
    for g, w in zip(grad_parts[1:], qkv_weights[1:]):
        normed_grad = normed_grad + times_transposed(g, w)
    input_ln_grad, grad_gain_one, grad_shift_one = norm_one_back(normed_grad)
    input_grads = (middle_grad + input_ln_grad).astype(jnp.bfloat16)

    vec_two = vector_block(
        [grad_gain_one, grad_shift_one, grad_bias_query, grad_bias_value, grad_bias_out],
        full_rows,
        jnp.float32,
    )
    red = reduce_routes(
        [grad_qkv[0], grad_qkv[1], jnp.concatenate([grad_qkv[2], vec_two], axis=1)],
        orders,
        count,
        me,
    )
    red_last, red_vec_two = split_cols(red[2], [qkv_cols[2], vec_two.shape[1]])
    red_qkv = jnp.concatenate([red[0], red[1], red_last], axis=1)
    r_bias_up, r_bias_down, r_gain_two, r_shift_two = vector_unblock(red_vec_one, [ratio, 1, 1, 1])
    r_gain_one, r_shift_one, r_bias_query, r_bias_value, r_bias_out = vector_unblock(
        red_vec_two, [1] * 5
    )
    reduced = (
        r_gain_one,
        r_shift_one,
        red_qkv,
        r_bias_query,
        r_bias_value,
        red_out,
        r_bias_out,
        r_gain_two,
        r_shift_two,
        red_up,
        r_bias_up,
        red_down,
        r_bias_down,
    )
    return (
        outputs.reshape(micro, 1, row_count, width),
        input_grads.reshape(micro, 1, row_count, width),
    ) + reduced


def solution(mesh):
    vec = P(ALL)
    mat = P(ALL, None)
    param_specs = (vec, vec, mat, vec, vec, mat, vec, vec, vec, mat, vec, mat, vec)
    return jax.shard_map(
        body,
        mesh=mesh,
        in_specs=(P(None, "dp", "seq", None), P(None, "dp", "seq", None), P(None, "dp", None, None))
        + param_specs,
        out_specs=(P(None, "dp", "seq", None), P(None, "dp", "seq", None)) + param_specs,
        check_vma=False,
    )
```

```python
from functools import partial

import jax
import jax.numpy as jnp
from jax import lax
from jax.sharding import PartitionSpec as P

HEADS = 12
HEAD = 64
EPSILON = 1e-05
ALL = ("dp", "seq")


def layer_norm(values, ln_gain, ln_shift):
    center = jnp.mean(values, axis=-1, keepdims=True)
    centered = values - center
    spread = jnp.mean(centered * centered, axis=-1, keepdims=True)
    return centered * lax.rsqrt(spread + EPSILON) * ln_gain + ln_shift


def piece_label(positions, bounds):
    inside = (positions[:, None] >= bounds[None, :, 0]) & (positions[:, None] < bounds[None, :, 1])
    labels = jnp.arange(1, bounds.shape[0] + 1, dtype=jnp.int32)
    return jnp.sum(jnp.where(inside, labels[None, :], 0), axis=1) - 1


def allowed_mask(query_pos, key_pos, bounds):
    query_label = piece_label(query_pos, bounds)
    key_label = piece_label(key_pos, bounds)
    causal = key_pos[None, :] <= query_pos[:, None]
    same_piece = (query_label[:, None] == key_label[None, :]) & (query_label[:, None] >= 0)
    return causal | same_piece


def outer_rows(left, right):
    return lax.dot_general(
        left, right, (((0,), (0,)), ((), ())), preferred_element_type=jnp.float32
    )


def times_transposed(left, right):
    return lax.dot_general(
        left, right, (((1,), (1,)), ((), ())), preferred_element_type=jnp.float32
    )


def route_orders(dp_size, seq_size):
    nbits = (dp_size * seq_size).bit_length() - 1
    if (dp_size, seq_size) == (4, 8):
        return [(3, 4, 0, 1, 2), (3, 0, 1, 4, 2), (3, 1, 4, 0, 2)]
    core = (seq_size.bit_length() - 1) if dp_size > 1 else None
    others = [b for b in range(nbits) if b != core]
    head = [core] if core is not None else []
    return [tuple(head + others[i:] + others[:i]) for i in range(3)]


def partner_pairs(count, bit):
    return [(i, i ^ (1 << bit)) for i in range(count)]


def tie(values, anchor):
    if anchor is None:
        return values
    values, _ = lax.optimization_barrier((values, anchor))
    return values


def gather_routes(routes, orders, count, me, anchors=None):
    nbits = count.bit_length() - 1
    idx = jnp.arange(count, dtype=jnp.int32)
    out = []
    for x, order in zip(routes, orders):
        rows, cols = x.shape
        for step, b in enumerate(reversed(order)):
            if anchors is not None:
                x = tie(x, anchors[step])
            got = lax.ppermute(x, ALL, partner_pairs(count, b))
            x = jnp.stack([x, got])
        rel = jnp.zeros((count,), jnp.int32)
        for j, b in enumerate(order):
            rel = rel + ((((idx >> b) & 1) ^ ((me >> b) & 1)) << (nbits - 1 - j))
        x = jnp.take(x.reshape(count, rows, cols), rel, axis=0)
        out.append(x.reshape(count * rows, cols))
    return out


def reduce_routes(routes, orders, count, me, anchors=None):
    nbits = count.bit_length() - 1
    out = []
    for x, order in zip(routes, orders):
        rows = x.shape[0] // count
        cols = x.shape[1]
        x = x.reshape([2] * nbits + [rows, cols])
        remaining = list(range(nbits - 1, -1, -1))
        for step, b in enumerate(order):
            if anchors is not None:
                x = tie(x, anchors[step])
            axis = remaining.index(b)
            mine = (me >> b) & 1
            keep = lax.dynamic_index_in_dim(x, mine, axis, keepdims=False)
            send = lax.dynamic_index_in_dim(x, 1 - mine, axis, keepdims=False).astype(jnp.bfloat16)
            got = lax.ppermute(send, ALL, partner_pairs(count, b))
            x = keep + got.astype(jnp.float32)
            remaining.pop(axis)
        out.append(x.reshape(rows, cols))
    return out


def split_cols(x, widths):
    out, at = [], 0
    for w in widths:
        out.append(x[:, at : at + w])
        at += w
    return out


def thirds(width, grain=128):
    first = -(-width // (3 * grain)) * grain
    return [first, first, width - 2 * first]


def vector_block(vectors, rows, dtype):
    cols = [v.reshape(rows, -1).astype(dtype) for v in vectors]
    used = sum(c.shape[1] for c in cols)
    pad = -(-used // 128) * 128 - used
    if pad:
        cols.append(jnp.zeros((rows, pad), dtype))
    return jnp.concatenate(cols, axis=1)


def vector_unblock(block, sizes):
    out, at = [], 0
    rows = block.shape[0]
    for s in sizes:
        out.append(block[:, at : at + s].reshape(rows * s))
        at += s
    return out


def unit_bounds(bounds, unit_count, per_device):
    first = lax.axis_index("seq") * per_device
    micro = (first + jnp.arange(per_device, dtype=jnp.int32)) // HEADS
    return bounds[:, 0][micro]


def unit_masks(ubounds, length):
    pos = jnp.arange(length, dtype=jnp.int32)
    return jax.vmap(lambda b: allowed_mask(pos, pos, b))(ubounds)


def rows_to_units(x, seq_count, per_device, parts):
    micro, rows = x.shape[0], x.shape[1]
    x = jnp.transpose(x, (0, 3, 1, 2, 4)).reshape(seq_count, per_device, rows, parts, HEAD)
    x = lax.all_to_all(x, "seq", 0, 0, tiled=True)
    x = jnp.transpose(x, (1, 0, 2, 3, 4))
    return x.reshape(per_device, seq_count * rows, parts, HEAD)


def units_to_rows(x, seq_count, micro, parts):
    per_device, length = x.shape[0], x.shape[1]
    rows = length // seq_count
    x = x.reshape(per_device, seq_count, rows, parts, HEAD)
    x = jnp.transpose(x, (1, 0, 2, 3, 4))
    x = lax.all_to_all(x, "seq", 0, 0, tiled=True)
    x = x.reshape(micro, HEADS, rows, parts, HEAD)
    x = jnp.transpose(x, (0, 2, 3, 1, 4))
    return x.reshape(micro * rows, parts * HEADS * HEAD)


def unit_forward(q, k, v, allowed):
    factor = q.shape[-1] ** (-0.5)
    scores = jnp.einsum("uqd,ukd->uqk", q, k, preferred_element_type=jnp.float32) * factor
    weights = jnp.where(allowed, jnp.exp(scores), 0.0)
    totals = jnp.sum(weights, axis=-1)
    summed = jnp.einsum(
        "uqk,ukd->uqd", weights.astype(jnp.bfloat16), v, preferred_element_type=jnp.float32
    )
    return weights, totals, summed / totals[:, :, None]


def unit_backward(q, k, v, weights, totals, attended, attended_grad):
    factor = q.shape[-1] ** (-0.5)
    grad_f = attended_grad.astype(jnp.float32)
    delta = jnp.sum(grad_f * attended, axis=-1) / totals
    summed_grad = (grad_f / totals[:, :, None]).astype(jnp.bfloat16)
    products = jnp.einsum("uqd,ukd->uqk", summed_grad, v, preferred_element_type=jnp.float32)
    score_grad = (weights * (products - delta[:, :, None])).astype(jnp.bfloat16)
    q_grad = jnp.einsum("uqk,ukd->uqd", score_grad, k, preferred_element_type=jnp.float32) * factor
    k_grad = jnp.einsum("uqk,uqd->ukd", score_grad, q, preferred_element_type=jnp.float32) * factor
    v_grad = jnp.einsum(
        "uqk,uqd->ukd", weights.astype(jnp.bfloat16), summed_grad, preferred_element_type=jnp.float32
    )
    return jnp.stack([q_grad, k_grad, v_grad], axis=2).astype(jnp.bfloat16)


def fallback_attention(queries, keys, values, bounds, row_count):
    micro = bounds.shape[0]
    seq_count = lax.axis_size("seq")
    total_len = row_count * seq_count
    query_pos = lax.axis_index("seq") * row_count + jnp.arange(row_count, dtype=jnp.int32)
    key_pos = jnp.arange(total_len, dtype=jnp.int32)
    saved = []
    attended_all = []
    for m in range(micro):
        sl = slice(m * row_count, (m + 1) * row_count)
        qh = queries[sl].reshape(row_count, HEADS, HEAD)
        k_all = lax.all_gather(keys[sl], "seq", axis=0, tiled=True).reshape(total_len, HEADS, HEAD)
        v_all = lax.all_gather(values[sl], "seq", axis=0, tiled=True).reshape(total_len, HEADS, HEAD)
        allowed = allowed_mask(query_pos, key_pos, bounds[m, 0])
        scores = jnp.einsum("rhd,khd->hrk", qh, k_all, preferred_element_type=jnp.float32) * HEAD ** (-0.5)
        weights = jnp.where(allowed[None], jnp.exp(scores), 0.0)
        totals = jnp.sum(weights, axis=-1)
        summed = jnp.einsum(
            "hrk,khd->rhd", weights.astype(jnp.bfloat16), v_all, preferred_element_type=jnp.float32
        )
        attended = summed / totals.T[:, :, None]
        saved.append((qh, k_all, v_all, weights, totals, attended))
        attended_all.append(attended.reshape(row_count, HEADS * HEAD))
    return jnp.concatenate(attended_all, axis=0), saved


def fallback_attention_backward(saved, attended_grad, row_count):
    factor = HEAD ** (-0.5)
    proj = []
    for m, (qh, k_all, v_all, weights, totals, attended) in enumerate(saved):
        grad = attended_grad[m * row_count : (m + 1) * row_count].astype(jnp.float32)
        grad = grad.reshape(row_count, HEADS, HEAD)
        delta = jnp.sum(grad * attended, axis=-1).T / totals
        grad_heads = (grad / totals.T[:, :, None]).astype(jnp.bfloat16)
        products = jnp.einsum("rhd,khd->hrk", grad_heads, v_all, preferred_element_type=jnp.float32)
        score_grad = (weights * (products - delta[:, :, None])).astype(jnp.bfloat16)
        q_grad = jnp.einsum("hrk,khd->rhd", score_grad, k_all, preferred_element_type=jnp.float32) * factor
        k_rows = jnp.einsum("hrk,rhd->khd", score_grad, qh, preferred_element_type=jnp.float32) * factor
        v_rows = jnp.einsum(
            "hrk,rhd->khd", weights.astype(jnp.bfloat16), grad_heads, preferred_element_type=jnp.float32
        )
        width = HEADS * HEAD
        k_own = lax.psum_scatter(
            k_rows.reshape(-1, width).astype(jnp.bfloat16), "seq", scatter_dimension=0, tiled=True
        )
        v_own = lax.psum_scatter(
            v_rows.reshape(-1, width).astype(jnp.bfloat16), "seq", scatter_dimension=0, tiled=True
        )
        proj.append(
            jnp.concatenate(
                [q_grad.reshape(row_count, width).astype(jnp.bfloat16), k_own, v_own], axis=1
            )
        )
    return jnp.concatenate(proj, axis=0)


def body(inputs, cotangent, bounds, *shards):
    micro = inputs.shape[0]
    row_count = inputs.shape[2]
    width = inputs.shape[3]
    ff = shards[9].shape[1]
    rows = micro * row_count
    seq_count = lax.axis_size("seq")
    unit_count = micro * HEADS
    head_parallel = unit_count % seq_count == 0
    per_device = unit_count // seq_count
    dp_count = lax.axis_size("dp")
    count = dp_count * seq_count
    me = lax.axis_index("dp") * seq_count + lax.axis_index("seq")
    orders = route_orders(dp_count, seq_count)
    steps = len(orders[0])
    ln1_g, ln1_b, w_qkv, b_q, b_v, w_out, b_out, ln2_g, ln2_b, w_up, b_up, w_down, b_down = shards
    shard_rows = w_qkv.shape[0]
    ratio = ff // width
    vec_sizes = [1] * 8 + [ratio]
    vecs_local = vector_block(
        [ln1_g, ln1_b, b_q, b_v, b_out, ln2_g, ln2_b, b_down, b_up], shard_rows, jnp.bfloat16
    )
    mlp_pack = jnp.concatenate(
        [
            w_out.reshape(shard_rows * ratio, width // ratio),
            w_up.reshape(shard_rows * ratio, ff // ratio),
            w_down,
        ],
        axis=1,
    )
    qkv_cols = thirds(w_qkv.shape[1])
    qkv_parts = split_cols(w_qkv, qkv_cols)
    gathered = gather_routes(
        [qkv_parts[0], qkv_parts[1], jnp.concatenate([qkv_parts[2], vecs_local], axis=1)],
        orders,
        count,
        me,
    )
    last_qkv, vecs_all = split_cols(gathered[2], [qkv_cols[2], vecs_local.shape[1]])
    qkv_weights = [gathered[0], gathered[1], last_qkv]
    (
        gain_one,
        shift_one,
        bias_query,
        bias_value,
        bias_out,
        gain_two,
        shift_two,
        bias_down,
        bias_up,
    ) = vector_unblock(vecs_all, vec_sizes)

    seq_in = inputs[:, 0].reshape(rows, width).astype(jnp.float32)
    normed_f, norm_one_back = jax.vjp(
        layer_norm, seq_in, gain_one.astype(jnp.float32), shift_one.astype(jnp.float32)
    )
    normed = normed_f.astype(jnp.bfloat16)
    if qkv_cols == [width] * 3:
        proj_q, proj_k, proj_v = [
            jnp.dot(normed, w, preferred_element_type=jnp.float32) for w in qkv_weights
        ]
    else:
        projected = jnp.dot(
            normed, jnp.concatenate(qkv_weights, axis=1), preferred_element_type=jnp.float32
        )
        proj_q, proj_k, proj_v = split_cols(projected, [width] * 3)
    queries = (proj_q + bias_query.astype(jnp.float32)).astype(jnp.bfloat16)
    keys_now = proj_k.astype(jnp.bfloat16)
    values_now = (proj_v + bias_value.astype(jnp.float32)).astype(jnp.bfloat16)

    if head_parallel:
        qkv_rows = jnp.concatenate([queries, keys_now, values_now], axis=1)
        qkv_units = rows_to_units(
            qkv_rows.reshape(micro, row_count, 3, HEADS, HEAD), seq_count, per_device, 3
        )
        uq, uk, uv = qkv_units[:, :, 0], qkv_units[:, :, 1], qkv_units[:, :, 2]
        allowed = unit_masks(unit_bounds(bounds, unit_count, per_device), seq_count * row_count)
        weights, totals, attended_u = unit_forward(uq, uk, uv, allowed)
        attended_b = units_to_rows(
            attended_u.astype(jnp.bfloat16)[:, :, None], seq_count, micro, 1
        )
        forward_anchors = [normed, qkv_units, weights, attended_u, attended_u]
    else:
        attended, saved = fallback_attention(queries, keys_now, values_now, bounds, row_count)
        attended_b = attended.astype(jnp.bfloat16)
        forward_anchors = [queries] + [attended] * (steps - 1)

    out_view, up_view, proj_down = split_cols(
        lax.all_gather(mlp_pack, ALL, axis=0, tiled=True), [width // ratio, ff // ratio, width]
    )
    full_rows = count * shard_rows
    out3 = out_view.reshape(full_rows, ratio, width // ratio)
    up3 = up_view.reshape(full_rows, ratio, ff // ratio)

    branch = jnp.einsum(
        "nr,rck->nck", attended_b, out3, preferred_element_type=jnp.float32
    ).reshape(rows, width) + bias_out.astype(jnp.float32)
    middle = seq_in + branch
    normed_two_f, norm_two_back = jax.vjp(
        layer_norm, middle, gain_two.astype(jnp.float32), shift_two.astype(jnp.float32)
    )
    normed_two = normed_two_f.astype(jnp.bfloat16)
    hidden = jnp.einsum(
        "nr,rck->nck", normed_two, up3, preferred_element_type=jnp.float32
    ).reshape(rows, ff) + bias_up.astype(jnp.float32)
    activated_f, gelu_back = jax.vjp(partial(jax.nn.gelu, approximate=False), hidden)
    activated = activated_f.astype(jnp.bfloat16)
    mlp_out = jnp.dot(activated, proj_down, preferred_element_type=jnp.float32) + bias_down.astype(
        jnp.float32
    )
    outputs = (middle + mlp_out).astype(jnp.bfloat16)

    out_grad = cotangent[:, 0].reshape(rows, width)
    out_grad_f = out_grad.astype(jnp.float32)
    grad_down = outer_rows(activated, out_grad)
    grad_bias_down = jnp.sum(out_grad_f, axis=0)
    act_grad = times_transposed(out_grad, proj_down)
    (hidden_grad,) = gelu_back(act_grad)
    hidden_grad_b = hidden_grad.astype(jnp.bfloat16)
    grad_up = outer_rows(normed_two, hidden_grad_b)
    grad_bias_up = jnp.sum(hidden_grad_b.astype(jnp.float32), axis=0)
    normed_two_grad = jnp.einsum(
        "nck,rck->nr", hidden_grad_b.reshape(rows, ratio, ff // ratio), up3,
        preferred_element_type=jnp.float32,
    )
    middle_ln_grad, grad_gain_two, grad_shift_two = norm_two_back(normed_two_grad)
    middle_grad = out_grad_f + middle_ln_grad
    branch_grad = middle_grad.astype(jnp.bfloat16)
    grad_out = outer_rows(attended_b, branch_grad)
    grad_bias_out = jnp.sum(branch_grad.astype(jnp.float32), axis=0)
    attended_grad = jnp.einsum(
        "nck,rck->nr", branch_grad.reshape(rows, ratio, width // ratio), out3,
        preferred_element_type=jnp.float32,
    ).astype(jnp.bfloat16)

    if head_parallel:
        grad_units = rows_to_units(
            attended_grad.reshape(micro, row_count, 1, HEADS, HEAD), seq_count, per_device, 1
        )[:, :, 0]
        qkv_grad_u = unit_backward(uq, uk, uv, weights, totals, attended_u, grad_units)
        proj_grad = units_to_rows(qkv_grad_u, seq_count, micro, 3)
        backward_anchors = [None, grad_units, qkv_grad_u, proj_grad, proj_grad]
    else:
        proj_grad = fallback_attention_backward(saved, attended_grad, row_count)
        backward_anchors = [None] + [proj_grad] * (steps - 1)

    vec_one = vector_block(
        [grad_bias_up, grad_bias_down, grad_gain_two, grad_shift_two], full_rows, jnp.float32
    )
    red_up, red_down, red_mixed = reduce_routes(
        [grad_up, grad_down, jnp.concatenate([grad_out, vec_one], axis=1)],
        orders,
        count,
        me,
        backward_anchors[:steps],
    )
    red_out, red_vec_one = split_cols(red_mixed, [width, vec_one.shape[1]])

    grad_bias_query = jnp.sum(proj_grad[:, :width].astype(jnp.float32), axis=0)
    grad_bias_value = jnp.sum(proj_grad[:, 2 * width :].astype(jnp.float32), axis=0)
    grad_parts = split_cols(proj_grad, qkv_cols)
    grad_qkv = [outer_rows(normed, g) for g in grad_parts]
    normed_grad = times_transposed(grad_parts[0], qkv_weights[0])
    for g, w in zip(grad_parts[1:], qkv_weights[1:]):
        normed_grad = normed_grad + times_transposed(g, w)
    input_ln_grad, grad_gain_one, grad_shift_one = norm_one_back(normed_grad)
    input_grads = (middle_grad + input_ln_grad).astype(jnp.bfloat16)

    vec_two = vector_block(
        [grad_gain_one, grad_shift_one, grad_bias_query, grad_bias_value, grad_bias_out],
        full_rows,
        jnp.float32,
    )
    red = reduce_routes(
        [grad_qkv[0], grad_qkv[1], jnp.concatenate([grad_qkv[2], vec_two], axis=1)],
        orders,
        count,
        me,
    )
    red_last, red_vec_two = split_cols(red[2], [qkv_cols[2], vec_two.shape[1]])
    red_qkv = jnp.concatenate([red[0], red[1], red_last], axis=1)
    r_bias_up, r_bias_down, r_gain_two, r_shift_two = vector_unblock(red_vec_one, [ratio, 1, 1, 1])
    r_gain_one, r_shift_one, r_bias_query, r_bias_value, r_bias_out = vector_unblock(
        red_vec_two, [1] * 5
    )
    reduced = (
        r_gain_one,
        r_shift_one,
        red_qkv,
        r_bias_query,
        r_bias_value,
        red_out,
        r_bias_out,
        r_gain_two,
        r_shift_two,
        red_up,
        r_bias_up,
        red_down,
        r_bias_down,
    )
    return (
        outputs.reshape(micro, 1, row_count, width),
        input_grads.reshape(micro, 1, row_count, width),
    ) + reduced


def solution(mesh):
    vec = P(ALL)
    mat = P(ALL, None)
    param_specs = (vec, vec, mat, vec, vec, mat, vec, vec, vec, mat, vec, mat, vec)
    return jax.shard_map(
        body,
        mesh=mesh,
        in_specs=(P(None, "dp", "seq", None), P(None, "dp", "seq", None), P(None, "dp", None, None))
        + param_specs,
        out_specs=(P(None, "dp", "seq", None), P(None, "dp", "seq", None)) + param_specs,
        check_vma=False,
    )
```

```python
from functools import partial

import jax
import jax.numpy as jnp
from jax import lax
from jax.sharding import PartitionSpec as P

HEADS = 12
HEAD = 64
EPSILON = 1e-05
ALL = ("dp", "seq")


def layer_norm(values, ln_gain, ln_shift):
    center = jnp.mean(values, axis=-1, keepdims=True)
    centered = values - center
    spread = jnp.mean(centered * centered, axis=-1, keepdims=True)
    return centered * lax.rsqrt(spread + EPSILON) * ln_gain + ln_shift


def piece_label(positions, bounds):
    inside = (positions[:, None] >= bounds[None, :, 0]) & (positions[:, None] < bounds[None, :, 1])
    labels = jnp.arange(1, bounds.shape[0] + 1, dtype=jnp.int32)
    return jnp.sum(jnp.where(inside, labels[None, :], 0), axis=1) - 1


def allowed_mask(query_pos, key_pos, bounds):
    query_label = piece_label(query_pos, bounds)
    key_label = piece_label(key_pos, bounds)
    causal = key_pos[None, :] <= query_pos[:, None]
    same_piece = (query_label[:, None] == key_label[None, :]) & (query_label[:, None] >= 0)
    return causal | same_piece


def outer_rows(left, right):
    return lax.dot_general(
        left, right, (((0,), (0,)), ((), ())), preferred_element_type=jnp.float32
    )


def times_transposed(left, right):
    return lax.dot_general(
        left, right, (((1,), (1,)), ((), ())), preferred_element_type=jnp.float32
    )


def route_orders(dp_size, seq_size):
    nbits = (dp_size * seq_size).bit_length() - 1
    if (dp_size, seq_size) == (4, 8):
        return [(3, 4, 0, 1, 2), (3, 0, 1, 4, 2), (3, 1, 4, 0, 2)]
    core = (seq_size.bit_length() - 1) if dp_size > 1 else None
    others = [b for b in range(nbits) if b != core]
    head = [core] if core is not None else []
    return [tuple(head + others[i:] + others[:i]) for i in range(3)]


def partner_pairs(count, bit):
    return [(i, i ^ (1 << bit)) for i in range(count)]


def tie(values, anchor):
    if anchor is None:
        return values
    values, _ = lax.optimization_barrier((values, anchor))
    return values


def gather_routes(routes, orders, count, me, anchors=None):
    nbits = count.bit_length() - 1
    idx = jnp.arange(count, dtype=jnp.int32)
    out = []
    for x, order in zip(routes, orders):
        rows, cols = x.shape
        for step, b in enumerate(reversed(order)):
            if anchors is not None:
                x = tie(x, anchors[step])
            got = lax.ppermute(x, ALL, partner_pairs(count, b))
            x = jnp.stack([x, got])
        rel = jnp.zeros((count,), jnp.int32)
        for j, b in enumerate(order):
            rel = rel + ((((idx >> b) & 1) ^ ((me >> b) & 1)) << (nbits - 1 - j))
        x = jnp.take(x.reshape(count, rows, cols), rel, axis=0)
        out.append(x.reshape(count * rows, cols))
    return out


def reduce_routes(routes, orders, count, me, anchors=None):
    nbits = count.bit_length() - 1
    out = []
    for x, order in zip(routes, orders):
        rows = x.shape[0] // count
        cols = x.shape[1]
        x = x.reshape([2] * nbits + [rows, cols])
        remaining = list(range(nbits - 1, -1, -1))
        for step, b in enumerate(order):
            if anchors is not None:
                x = tie(x, anchors[step])
            axis = remaining.index(b)
            mine = (me >> b) & 1
            keep = lax.dynamic_index_in_dim(x, mine, axis, keepdims=False)
            send = lax.dynamic_index_in_dim(x, 1 - mine, axis, keepdims=False).astype(jnp.bfloat16)
            got = lax.ppermute(send, ALL, partner_pairs(count, b))
            x = keep + got.astype(jnp.float32)
            remaining.pop(axis)
        out.append(x.reshape(rows, cols))
    return out


def split_cols(x, widths):
    out, at = [], 0
    for w in widths:
        out.append(x[:, at : at + w])
        at += w
    return out


def thirds(width, grain=128):
    first = -(-width // (3 * grain)) * grain
    return [first, first, width - 2 * first]


def vector_block(vectors, rows, dtype):
    cols = [v.reshape(rows, -1).astype(dtype) for v in vectors]
    used = sum(c.shape[1] for c in cols)
    pad = -(-used // 128) * 128 - used
    if pad:
        cols.append(jnp.zeros((rows, pad), dtype))
    return jnp.concatenate(cols, axis=1)


def vector_unblock(block, sizes):
    out, at = [], 0
    rows = block.shape[0]
    for s in sizes:
        out.append(block[:, at : at + s].reshape(rows * s))
        at += s
    return out


def unit_bounds(bounds, unit_count, per_device):
    first = lax.axis_index("seq") * per_device
    micro = (first + jnp.arange(per_device, dtype=jnp.int32)) // HEADS
    return bounds[:, 0][micro]


def unit_masks(ubounds, length):
    pos = jnp.arange(length, dtype=jnp.int32)
    return jax.vmap(lambda b: allowed_mask(pos, pos, b))(ubounds)


def rows_to_units(x, seq_count, per_device, parts):
    micro, rows = x.shape[0], x.shape[1]
    x = jnp.transpose(x, (0, 3, 1, 2, 4)).reshape(seq_count, per_device, rows, parts, HEAD)
    x = lax.all_to_all(x, "seq", 0, 0, tiled=True)
    x = jnp.transpose(x, (1, 0, 2, 3, 4))
    return x.reshape(per_device, seq_count * rows, parts, HEAD)


def units_to_rows(x, seq_count, micro, parts):
    per_device, length = x.shape[0], x.shape[1]
    rows = length // seq_count
    x = x.reshape(per_device, seq_count, rows, parts, HEAD)
    x = jnp.transpose(x, (1, 0, 2, 3, 4))
    x = lax.all_to_all(x, "seq", 0, 0, tiled=True)
    x = x.reshape(micro, HEADS, rows, parts, HEAD)
    x = jnp.transpose(x, (0, 2, 3, 1, 4))
    return x.reshape(micro * rows, parts * HEADS * HEAD)


def unit_forward(q, k, v, allowed):
    factor = q.shape[-1] ** (-0.5)
    scores = jnp.einsum("uqd,ukd->uqk", q, k, preferred_element_type=jnp.float32) * factor
    weights = jnp.where(allowed, jnp.exp(scores), 0.0)
    totals = jnp.sum(weights, axis=-1)
    summed = jnp.einsum(
        "uqk,ukd->uqd", weights.astype(jnp.bfloat16), v, preferred_element_type=jnp.float32
    )
    return weights, totals, summed / totals[:, :, None]


def unit_backward(q, k, v, weights, totals, attended, attended_grad):
    factor = q.shape[-1] ** (-0.5)
    grad_f = attended_grad.astype(jnp.float32)
    delta = jnp.sum(grad_f * attended, axis=-1) / totals
    summed_grad = (grad_f / totals[:, :, None]).astype(jnp.bfloat16)
    products = jnp.einsum("uqd,ukd->uqk", summed_grad, v, preferred_element_type=jnp.float32)
    score_grad = (weights * (products - delta[:, :, None])).astype(jnp.bfloat16)
    q_grad = jnp.einsum("uqk,ukd->uqd", score_grad, k, preferred_element_type=jnp.float32) * factor
    k_grad = jnp.einsum("uqk,uqd->ukd", score_grad, q, preferred_element_type=jnp.float32) * factor
    v_grad = jnp.einsum(
        "uqk,uqd->ukd", weights.astype(jnp.bfloat16), summed_grad, preferred_element_type=jnp.float32
    )
    return jnp.stack([q_grad, k_grad, v_grad], axis=2).astype(jnp.bfloat16)


def fallback_attention(queries, keys, values, bounds, row_count):
    micro = bounds.shape[0]
    seq_count = lax.axis_size("seq")
    total_len = row_count * seq_count
    query_pos = lax.axis_index("seq") * row_count + jnp.arange(row_count, dtype=jnp.int32)
    key_pos = jnp.arange(total_len, dtype=jnp.int32)
    saved = []
    attended_all = []
    for m in range(micro):
        sl = slice(m * row_count, (m + 1) * row_count)
        qh = queries[sl].reshape(row_count, HEADS, HEAD)
        k_all = lax.all_gather(keys[sl], "seq", axis=0, tiled=True).reshape(total_len, HEADS, HEAD)
        v_all = lax.all_gather(values[sl], "seq", axis=0, tiled=True).reshape(total_len, HEADS, HEAD)
        allowed = allowed_mask(query_pos, key_pos, bounds[m, 0])
        scores = jnp.einsum("rhd,khd->hrk", qh, k_all, preferred_element_type=jnp.float32) * HEAD ** (-0.5)
        weights = jnp.where(allowed[None], jnp.exp(scores), 0.0)
        totals = jnp.sum(weights, axis=-1)
        summed = jnp.einsum(
            "hrk,khd->rhd", weights.astype(jnp.bfloat16), v_all, preferred_element_type=jnp.float32
        )
        attended = summed / totals.T[:, :, None]
        saved.append((qh, k_all, v_all, weights, totals, attended))
        attended_all.append(attended.reshape(row_count, HEADS * HEAD))
    return jnp.concatenate(attended_all, axis=0), saved


def fallback_attention_backward(saved, attended_grad, row_count):
    factor = HEAD ** (-0.5)
    proj = []
    for m, (qh, k_all, v_all, weights, totals, attended) in enumerate(saved):
        grad = attended_grad[m * row_count : (m + 1) * row_count].astype(jnp.float32)
        grad = grad.reshape(row_count, HEADS, HEAD)
        delta = jnp.sum(grad * attended, axis=-1).T / totals
        grad_heads = (grad / totals.T[:, :, None]).astype(jnp.bfloat16)
        products = jnp.einsum("rhd,khd->hrk", grad_heads, v_all, preferred_element_type=jnp.float32)
        score_grad = (weights * (products - delta[:, :, None])).astype(jnp.bfloat16)
        q_grad = jnp.einsum("hrk,khd->rhd", score_grad, k_all, preferred_element_type=jnp.float32) * factor
        k_rows = jnp.einsum("hrk,rhd->khd", score_grad, qh, preferred_element_type=jnp.float32) * factor
        v_rows = jnp.einsum(
            "hrk,rhd->khd", weights.astype(jnp.bfloat16), grad_heads, preferred_element_type=jnp.float32
        )
        width = HEADS * HEAD
        k_own = lax.psum_scatter(
            k_rows.reshape(-1, width).astype(jnp.bfloat16), "seq", scatter_dimension=0, tiled=True
        )
        v_own = lax.psum_scatter(
            v_rows.reshape(-1, width).astype(jnp.bfloat16), "seq", scatter_dimension=0, tiled=True
        )
        proj.append(
            jnp.concatenate(
                [q_grad.reshape(row_count, width).astype(jnp.bfloat16), k_own, v_own], axis=1
            )
        )
    return jnp.concatenate(proj, axis=0)


def body(inputs, cotangent, bounds, *shards):
    micro = inputs.shape[0]
    row_count = inputs.shape[2]
    width = inputs.shape[3]
    ff = shards[9].shape[1]
    rows = micro * row_count
    seq_count = lax.axis_size("seq")
    unit_count = micro * HEADS
    head_parallel = unit_count % seq_count == 0
    per_device = unit_count // seq_count
    dp_count = lax.axis_size("dp")
    count = dp_count * seq_count
    me = lax.axis_index("dp") * seq_count + lax.axis_index("seq")
    orders = route_orders(dp_count, seq_count)
    steps = len(orders[0])
    ln1_g, ln1_b, w_qkv, b_q, b_v, w_out, b_out, ln2_g, ln2_b, w_up, b_up, w_down, b_down = shards
    shard_rows = w_qkv.shape[0]
    ratio = ff // width
    vec_sizes = [1] * 8 + [ratio]
    vecs_local = vector_block(
        [ln1_g, ln1_b, b_q, b_v, b_out, ln2_g, ln2_b, b_down, b_up], shard_rows, jnp.bfloat16
    )
    mlp_pack = jnp.concatenate([w_out, w_up, w_down.reshape(shard_rows, ratio * width)], axis=1)
    qkv_cols = thirds(w_qkv.shape[1])
    qkv_parts = split_cols(w_qkv, qkv_cols)
    gathered = gather_routes(
        [qkv_parts[0], qkv_parts[1], jnp.concatenate([qkv_parts[2], vecs_local], axis=1)],
        orders,
        count,
        me,
    )
    last_qkv, vecs_all = split_cols(gathered[2], [qkv_cols[2], vecs_local.shape[1]])
    qkv_weights = [gathered[0], gathered[1], last_qkv]
    (
        gain_one,
        shift_one,
        bias_query,
        bias_value,
        bias_out,
        gain_two,
        shift_two,
        bias_down,
        bias_up,
    ) = vector_unblock(vecs_all, vec_sizes)

    seq_in = inputs[:, 0].reshape(rows, width).astype(jnp.float32)
    normed_f, norm_one_back = jax.vjp(
        layer_norm, seq_in, gain_one.astype(jnp.float32), shift_one.astype(jnp.float32)
    )
    normed = normed_f.astype(jnp.bfloat16)
    if qkv_cols == [width] * 3:
        proj_q, proj_k, proj_v = [
            jnp.dot(normed, w, preferred_element_type=jnp.float32) for w in qkv_weights
        ]
    else:
        projected = jnp.dot(
            normed, jnp.concatenate(qkv_weights, axis=1), preferred_element_type=jnp.float32
        )
        proj_q, proj_k, proj_v = split_cols(projected, [width] * 3)
    queries = (proj_q + bias_query.astype(jnp.float32)).astype(jnp.bfloat16)
    keys_now = proj_k.astype(jnp.bfloat16)
    values_now = (proj_v + bias_value.astype(jnp.float32)).astype(jnp.bfloat16)

    if head_parallel:
        qkv_rows = jnp.concatenate([queries, keys_now, values_now], axis=1)
        qkv_units = rows_to_units(
            qkv_rows.reshape(micro, row_count, 3, HEADS, HEAD), seq_count, per_device, 3
        )
        uq, uk, uv = qkv_units[:, :, 0], qkv_units[:, :, 1], qkv_units[:, :, 2]
        allowed = unit_masks(unit_bounds(bounds, unit_count, per_device), seq_count * row_count)
        weights, totals, attended_u = unit_forward(uq, uk, uv, allowed)
        attended_b = units_to_rows(
            attended_u.astype(jnp.bfloat16)[:, :, None], seq_count, micro, 1
        )
        forward_anchors = [normed, qkv_units, weights, attended_u, attended_u]
    else:
        attended, saved = fallback_attention(queries, keys_now, values_now, bounds, row_count)
        attended_b = attended.astype(jnp.bfloat16)
        forward_anchors = [queries] + [attended] * (steps - 1)

    proj_out, proj_up, down_view = split_cols(
        lax.all_gather(mlp_pack, ALL, axis=0, tiled=True), [width, ff, ff]
    )
    proj_down = down_view.reshape(count * shard_rows * ratio, width)

    branch = jnp.dot(attended_b, proj_out, preferred_element_type=jnp.float32) + bias_out.astype(
        jnp.float32
    )
    middle = seq_in + branch
    normed_two_f, norm_two_back = jax.vjp(
        layer_norm, middle, gain_two.astype(jnp.float32), shift_two.astype(jnp.float32)
    )
    normed_two = normed_two_f.astype(jnp.bfloat16)
    hidden = jnp.dot(normed_two, proj_up, preferred_element_type=jnp.float32) + bias_up.astype(
        jnp.float32
    )
    activated_f, gelu_back = jax.vjp(partial(jax.nn.gelu, approximate=False), hidden)
    activated = activated_f.astype(jnp.bfloat16)
    mlp_out = jnp.dot(activated, proj_down, preferred_element_type=jnp.float32) + bias_down.astype(
        jnp.float32
    )
    outputs = (middle + mlp_out).astype(jnp.bfloat16)

    out_grad = cotangent[:, 0].reshape(rows, width)
    out_grad_f = out_grad.astype(jnp.float32)
    grad_down = outer_rows(activated, out_grad)
    grad_bias_down = jnp.sum(out_grad_f, axis=0)
    act_grad = times_transposed(out_grad, proj_down)
    (hidden_grad,) = gelu_back(act_grad)
    hidden_grad_b = hidden_grad.astype(jnp.bfloat16)
    grad_up = outer_rows(normed_two, hidden_grad_b)
    grad_bias_up = jnp.sum(hidden_grad_b.astype(jnp.float32), axis=0)
    normed_two_grad = times_transposed(hidden_grad_b, proj_up)
    middle_ln_grad, grad_gain_two, grad_shift_two = norm_two_back(normed_two_grad)
    middle_grad = out_grad_f + middle_ln_grad
    branch_grad = middle_grad.astype(jnp.bfloat16)
    grad_out = outer_rows(attended_b, branch_grad)
    grad_bias_out = jnp.sum(branch_grad.astype(jnp.float32), axis=0)
    attended_grad = times_transposed(branch_grad, proj_out).astype(jnp.bfloat16)

    if head_parallel:
        grad_units = rows_to_units(
            attended_grad.reshape(micro, row_count, 1, HEADS, HEAD), seq_count, per_device, 1
        )[:, :, 0]
        qkv_grad_u = unit_backward(uq, uk, uv, weights, totals, attended_u, grad_units)
        proj_grad = units_to_rows(qkv_grad_u, seq_count, micro, 3)
        backward_anchors = [None, grad_units, qkv_grad_u, qkv_grad_u, qkv_grad_u]
    else:
        proj_grad = fallback_attention_backward(saved, attended_grad, row_count)
        backward_anchors = [None] + [proj_grad] * (steps - 1)

    full_rows = count * shard_rows
    vec_one = vector_block(
        [grad_bias_up, grad_bias_down, grad_gain_two, grad_shift_two], full_rows, jnp.float32
    )
    red_up, red_down, red_mixed = reduce_routes(
        [grad_up, grad_down, jnp.concatenate([grad_out, vec_one], axis=1)],
        orders,
        count,
        me,
        backward_anchors[:steps],
    )
    red_out, red_vec_one = split_cols(red_mixed, [width, vec_one.shape[1]])

    grad_bias_query = jnp.sum(proj_grad[:, :width].astype(jnp.float32), axis=0)
    grad_bias_value = jnp.sum(proj_grad[:, 2 * width :].astype(jnp.float32), axis=0)
    grad_parts = split_cols(proj_grad, qkv_cols)
    grad_qkv = [outer_rows(normed, g) for g in grad_parts]
    normed_grad = times_transposed(grad_parts[0], qkv_weights[0])
    for g, w in zip(grad_parts[1:], qkv_weights[1:]):
        normed_grad = normed_grad + times_transposed(g, w)
    input_ln_grad, grad_gain_one, grad_shift_one = norm_one_back(normed_grad)
    input_grads = (middle_grad + input_ln_grad).astype(jnp.bfloat16)

    vec_two = vector_block(
        [grad_gain_one, grad_shift_one, grad_bias_query, grad_bias_value, grad_bias_out],
        full_rows,
        jnp.float32,
    )
    red = reduce_routes(
        [grad_qkv[0], grad_qkv[1], jnp.concatenate([grad_qkv[2], vec_two], axis=1)],
        orders,
        count,
        me,
        [(red_up, red_down, red_mixed)] + [None] * (steps - 1),
    )
    red_last, red_vec_two = split_cols(red[2], [qkv_cols[2], vec_two.shape[1]])
    red_qkv = jnp.concatenate([red[0], red[1], red_last], axis=1)
    r_bias_up, r_bias_down, r_gain_two, r_shift_two = vector_unblock(red_vec_one, [ratio, 1, 1, 1])
    r_gain_one, r_shift_one, r_bias_query, r_bias_value, r_bias_out = vector_unblock(
        red_vec_two, [1] * 5
    )
    reduced = (
        r_gain_one,
        r_shift_one,
        red_qkv,
        r_bias_query,
        r_bias_value,
        red_out,
        r_bias_out,
        r_gain_two,
        r_shift_two,
        red_up,
        r_bias_up,
        red_down,
        r_bias_down,
    )
    return (
        outputs.reshape(micro, 1, row_count, width),
        input_grads.reshape(micro, 1, row_count, width),
    ) + reduced


def solution(mesh):
    vec = P(ALL)
    mat = P(ALL, None)
    param_specs = (vec, vec, mat, vec, vec, mat, vec, vec, vec, mat, vec, mat, vec)
    return jax.shard_map(
        body,
        mesh=mesh,
        in_specs=(P(None, "dp", "seq", None), P(None, "dp", "seq", None), P(None, "dp", None, None))
        + param_specs,
        out_specs=(P(None, "dp", "seq", None), P(None, "dp", "seq", None)) + param_specs,
        check_vma=False,
    )
```

```python
from functools import partial

import jax
import jax.numpy as jnp
from jax import lax
from jax.sharding import PartitionSpec as P

HEADS = 12
HEAD = 64
EPSILON = 1e-05
ALL = ("dp", "seq")


def layer_norm(values, ln_gain, ln_shift):
    center = jnp.mean(values, axis=-1, keepdims=True)
    centered = values - center
    spread = jnp.mean(centered * centered, axis=-1, keepdims=True)
    return centered * lax.rsqrt(spread + EPSILON) * ln_gain + ln_shift


def piece_label(positions, bounds):
    inside = (positions[:, None] >= bounds[None, :, 0]) & (positions[:, None] < bounds[None, :, 1])
    labels = jnp.arange(1, bounds.shape[0] + 1, dtype=jnp.int32)
    return jnp.sum(jnp.where(inside, labels[None, :], 0), axis=1) - 1


def allowed_mask(query_pos, key_pos, bounds):
    query_label = piece_label(query_pos, bounds)
    key_label = piece_label(key_pos, bounds)
    causal = key_pos[None, :] <= query_pos[:, None]
    same_piece = (query_label[:, None] == key_label[None, :]) & (query_label[:, None] >= 0)
    return causal | same_piece


def outer_rows(left, right):
    return lax.dot_general(
        left, right, (((0,), (0,)), ((), ())), preferred_element_type=jnp.float32
    )


def times_transposed(left, right):
    return lax.dot_general(
        left, right, (((1,), (1,)), ((), ())), preferred_element_type=jnp.float32
    )


def route_orders(dp_size, seq_size):
    nbits = (dp_size * seq_size).bit_length() - 1
    if (dp_size, seq_size) == (4, 8):
        return [(3, 4, 0, 1, 2), (3, 0, 1, 4, 2), (3, 1, 4, 0, 2)]
    core = (seq_size.bit_length() - 1) if dp_size > 1 else None
    others = [b for b in range(nbits) if b != core]
    head = [core] if core is not None else []
    return [tuple(head + others[i:] + others[:i]) for i in range(3)]


def partner_pairs(count, bit):
    return [(i, i ^ (1 << bit)) for i in range(count)]


def tie(values, anchor):
    if anchor is None:
        return values
    values, _ = lax.optimization_barrier((values, anchor))
    return values


def gather_routes(routes, orders, count, me, anchors=None):
    nbits = count.bit_length() - 1
    idx = jnp.arange(count, dtype=jnp.int32)
    out = []
    for x, order in zip(routes, orders):
        rows, cols = x.shape
        for step, b in enumerate(reversed(order)):
            if anchors is not None:
                x = tie(x, anchors[step])
            got = lax.ppermute(x, ALL, partner_pairs(count, b))
            x = jnp.stack([x, got])
        rel = jnp.zeros((count,), jnp.int32)
        for j, b in enumerate(order):
            rel = rel + ((((idx >> b) & 1) ^ ((me >> b) & 1)) << (nbits - 1 - j))
        x = jnp.take(x.reshape(count, rows, cols), rel, axis=0)
        out.append(x.reshape(count * rows, cols))
    return out


def reduce_routes(routes, orders, count, me, anchors=None):
    nbits = count.bit_length() - 1
    out = []
    for x, order in zip(routes, orders):
        rows = x.shape[0] // count
        cols = x.shape[1]
        x = x.reshape([2] * nbits + [rows, cols])
        remaining = list(range(nbits - 1, -1, -1))
        for step, b in enumerate(order):
            if anchors is not None:
                x = tie(x, anchors[step])
            axis = remaining.index(b)
            mine = (me >> b) & 1
            keep = lax.dynamic_index_in_dim(x, mine, axis, keepdims=False)
            send = lax.dynamic_index_in_dim(x, 1 - mine, axis, keepdims=False).astype(jnp.bfloat16)
            got = lax.ppermute(send, ALL, partner_pairs(count, b))
            x = keep + got.astype(jnp.float32)
            remaining.pop(axis)
        out.append(x.reshape(rows, cols))
    return out


def split_cols(x, widths):
    out, at = [], 0
    for w in widths:
        out.append(x[:, at : at + w])
        at += w
    return out


def thirds(width, grain=128):
    first = -(-width // (3 * grain)) * grain
    return [first, first, width - 2 * first]


def vector_block(vectors, rows, dtype):
    cols = [v.reshape(rows, -1).astype(dtype) for v in vectors]
    used = sum(c.shape[1] for c in cols)
    pad = -(-used // 128) * 128 - used
    if pad:
        cols.append(jnp.zeros((rows, pad), dtype))
    return jnp.concatenate(cols, axis=1)


def vector_unblock(block, sizes):
    out, at = [], 0
    rows = block.shape[0]
    for s in sizes:
        out.append(block[:, at : at + s].reshape(rows * s))
        at += s
    return out


def unit_bounds(bounds, unit_count, per_device):
    first = lax.axis_index("seq") * per_device
    micro = (first + jnp.arange(per_device, dtype=jnp.int32)) // HEADS
    return bounds[:, 0][micro]


def unit_masks(ubounds, length):
    pos = jnp.arange(length, dtype=jnp.int32)
    return jax.vmap(lambda b: allowed_mask(pos, pos, b))(ubounds)


def rows_to_units(x, seq_count, per_device, parts):
    micro, rows = x.shape[0], x.shape[1]
    x = jnp.transpose(x, (0, 3, 1, 2, 4)).reshape(seq_count, per_device, rows, parts, HEAD)
    x = lax.all_to_all(x, "seq", 0, 0, tiled=True)
    x = jnp.transpose(x, (1, 0, 2, 3, 4))
    return x.reshape(per_device, seq_count * rows, parts, HEAD)


def units_to_rows(x, seq_count, micro, parts):
    per_device, length = x.shape[0], x.shape[1]
    rows = length // seq_count
    x = x.reshape(per_device, seq_count, rows, parts, HEAD)
    x = jnp.transpose(x, (1, 0, 2, 3, 4))
    x = lax.all_to_all(x, "seq", 0, 0, tiled=True)
    x = x.reshape(micro, HEADS, rows, parts, HEAD)
    x = jnp.transpose(x, (0, 2, 3, 1, 4))
    return x.reshape(micro * rows, parts * HEADS * HEAD)


def unit_forward(q, k, v, allowed):
    factor = q.shape[-1] ** (-0.5)
    scores = jnp.einsum("uqd,ukd->uqk", q, k, preferred_element_type=jnp.float32) * factor
    weights = jnp.where(allowed, jnp.exp(scores), 0.0)
    totals = jnp.sum(weights, axis=-1)
    summed = jnp.einsum(
        "uqk,ukd->uqd", weights.astype(jnp.bfloat16), v, preferred_element_type=jnp.float32
    )
    return weights, totals, summed / totals[:, :, None]


def unit_backward(q, k, v, weights, totals, attended, attended_grad):
    factor = q.shape[-1] ** (-0.5)
    grad_f = attended_grad.astype(jnp.float32)
    delta = jnp.sum(grad_f * attended, axis=-1) / totals
    summed_grad = (grad_f / totals[:, :, None]).astype(jnp.bfloat16)
    products = jnp.einsum("uqd,ukd->uqk", summed_grad, v, preferred_element_type=jnp.float32)
    score_grad = (weights * (products - delta[:, :, None])).astype(jnp.bfloat16)
    q_grad = jnp.einsum("uqk,ukd->uqd", score_grad, k, preferred_element_type=jnp.float32) * factor
    k_grad = jnp.einsum("uqk,uqd->ukd", score_grad, q, preferred_element_type=jnp.float32) * factor
    v_grad = jnp.einsum(
        "uqk,uqd->ukd", weights.astype(jnp.bfloat16), summed_grad, preferred_element_type=jnp.float32
    )
    return jnp.stack([q_grad, k_grad, v_grad], axis=2).astype(jnp.bfloat16)


def fallback_attention(queries, keys, values, bounds, row_count):
    micro = bounds.shape[0]
    seq_count = lax.axis_size("seq")
    total_len = row_count * seq_count
    query_pos = lax.axis_index("seq") * row_count + jnp.arange(row_count, dtype=jnp.int32)
    key_pos = jnp.arange(total_len, dtype=jnp.int32)
    saved = []
    attended_all = []
    for m in range(micro):
        sl = slice(m * row_count, (m + 1) * row_count)
        qh = queries[sl].reshape(row_count, HEADS, HEAD)
        k_all = lax.all_gather(keys[sl], "seq", axis=0, tiled=True).reshape(total_len, HEADS, HEAD)
        v_all = lax.all_gather(values[sl], "seq", axis=0, tiled=True).reshape(total_len, HEADS, HEAD)
        allowed = allowed_mask(query_pos, key_pos, bounds[m, 0])
        scores = jnp.einsum("rhd,khd->hrk", qh, k_all, preferred_element_type=jnp.float32) * HEAD ** (-0.5)
        weights = jnp.where(allowed[None], jnp.exp(scores), 0.0)
        totals = jnp.sum(weights, axis=-1)
        summed = jnp.einsum(
            "hrk,khd->rhd", weights.astype(jnp.bfloat16), v_all, preferred_element_type=jnp.float32
        )
        attended = summed / totals.T[:, :, None]
        saved.append((qh, k_all, v_all, weights, totals, attended))
        attended_all.append(attended.reshape(row_count, HEADS * HEAD))
    return jnp.concatenate(attended_all, axis=0), saved


def fallback_attention_backward(saved, attended_grad, row_count):
    factor = HEAD ** (-0.5)
    proj = []
    for m, (qh, k_all, v_all, weights, totals, attended) in enumerate(saved):
        grad = attended_grad[m * row_count : (m + 1) * row_count].astype(jnp.float32)
        grad = grad.reshape(row_count, HEADS, HEAD)
        delta = jnp.sum(grad * attended, axis=-1).T / totals
        grad_heads = (grad / totals.T[:, :, None]).astype(jnp.bfloat16)
        products = jnp.einsum("rhd,khd->hrk", grad_heads, v_all, preferred_element_type=jnp.float32)
        score_grad = (weights * (products - delta[:, :, None])).astype(jnp.bfloat16)
        q_grad = jnp.einsum("hrk,khd->rhd", score_grad, k_all, preferred_element_type=jnp.float32) * factor
        k_rows = jnp.einsum("hrk,rhd->khd", score_grad, qh, preferred_element_type=jnp.float32) * factor
        v_rows = jnp.einsum(
            "hrk,rhd->khd", weights.astype(jnp.bfloat16), grad_heads, preferred_element_type=jnp.float32
        )
        width = HEADS * HEAD
        k_own = lax.psum_scatter(
            k_rows.reshape(-1, width).astype(jnp.bfloat16), "seq", scatter_dimension=0, tiled=True
        )
        v_own = lax.psum_scatter(
            v_rows.reshape(-1, width).astype(jnp.bfloat16), "seq", scatter_dimension=0, tiled=True
        )
        proj.append(
            jnp.concatenate(
                [q_grad.reshape(row_count, width).astype(jnp.bfloat16), k_own, v_own], axis=1
            )
        )
    return jnp.concatenate(proj, axis=0)


def body(inputs, cotangent, bounds, *shards):
    micro = inputs.shape[0]
    row_count = inputs.shape[2]
    width = inputs.shape[3]
    ff = shards[9].shape[1]
    rows = micro * row_count
    seq_count = lax.axis_size("seq")
    unit_count = micro * HEADS
    head_parallel = unit_count % seq_count == 0
    per_device = unit_count // seq_count
    dp_count = lax.axis_size("dp")
    count = dp_count * seq_count
    me = lax.axis_index("dp") * seq_count + lax.axis_index("seq")
    orders = route_orders(dp_count, seq_count)
    steps = len(orders[0])
    ln1_g, ln1_b, w_qkv, b_q, b_v, w_out, b_out, ln2_g, ln2_b, w_up, b_up, w_down, b_down = shards
    shard_rows = w_qkv.shape[0]
    ratio = ff // width
    vec_sizes = [1] * 8 + [ratio]
    vecs_local = vector_block(
        [ln1_g, ln1_b, b_q, b_v, b_out, ln2_g, ln2_b, b_down, b_up], shard_rows, jnp.bfloat16
    )
    mlp_pack = jnp.concatenate([w_out, w_up, w_down.reshape(shard_rows, ratio * width)], axis=1)
    qkv_cols = thirds(w_qkv.shape[1])
    qkv_parts = split_cols(w_qkv, qkv_cols)
    gathered = gather_routes(
        [qkv_parts[0], qkv_parts[1], jnp.concatenate([qkv_parts[2], vecs_local], axis=1)],
        orders,
        count,
        me,
    )
    last_qkv, vecs_all = split_cols(gathered[2], [qkv_cols[2], vecs_local.shape[1]])
    qkv_weights = [gathered[0], gathered[1], last_qkv]
    (
        gain_one,
        shift_one,
        bias_query,
        bias_value,
        bias_out,
        gain_two,
        shift_two,
        bias_down,
        bias_up,
    ) = vector_unblock(vecs_all, vec_sizes)

    seq_in = inputs[:, 0].reshape(rows, width).astype(jnp.float32)
    normed_f, norm_one_back = jax.vjp(
        layer_norm, seq_in, gain_one.astype(jnp.float32), shift_one.astype(jnp.float32)
    )
    normed = normed_f.astype(jnp.bfloat16)
    if qkv_cols == [width] * 3:
        proj_q, proj_k, proj_v = [
            jnp.dot(normed, w, preferred_element_type=jnp.float32) for w in qkv_weights
        ]
    else:
        projected = jnp.dot(
            normed, jnp.concatenate(qkv_weights, axis=1), preferred_element_type=jnp.float32
        )
        proj_q, proj_k, proj_v = split_cols(projected, [width] * 3)
    queries = (proj_q + bias_query.astype(jnp.float32)).astype(jnp.bfloat16)
    keys_now = proj_k.astype(jnp.bfloat16)
    values_now = (proj_v + bias_value.astype(jnp.float32)).astype(jnp.bfloat16)

    if head_parallel:
        qkv_rows = jnp.concatenate([queries, keys_now, values_now], axis=1)
        qkv_units = rows_to_units(
            qkv_rows.reshape(micro, row_count, 3, HEADS, HEAD), seq_count, per_device, 3
        )
        uq, uk, uv = qkv_units[:, :, 0], qkv_units[:, :, 1], qkv_units[:, :, 2]
        allowed = unit_masks(unit_bounds(bounds, unit_count, per_device), seq_count * row_count)
        weights, totals, attended_u = unit_forward(uq, uk, uv, allowed)
        attended_b = units_to_rows(
            attended_u.astype(jnp.bfloat16)[:, :, None], seq_count, micro, 1
        )
        forward_anchors = [normed, qkv_units, weights, attended_u, attended_u]
    else:
        attended, saved = fallback_attention(queries, keys_now, values_now, bounds, row_count)
        attended_b = attended.astype(jnp.bfloat16)
        forward_anchors = [queries] + [attended] * (steps - 1)

    proj_out, proj_up, down_view = split_cols(
        lax.all_gather(mlp_pack, ALL, axis=0, tiled=True), [width, ff, ff]
    )
    proj_down = down_view.reshape(count * shard_rows * ratio, width)

    branch = jnp.dot(attended_b, proj_out, preferred_element_type=jnp.float32) + bias_out.astype(
        jnp.float32
    )
    middle = seq_in + branch
    normed_two_f, norm_two_back = jax.vjp(
        layer_norm, middle, gain_two.astype(jnp.float32), shift_two.astype(jnp.float32)
    )
    normed_two = normed_two_f.astype(jnp.bfloat16)
    hidden = jnp.dot(normed_two, proj_up, preferred_element_type=jnp.float32) + bias_up.astype(
        jnp.float32
    )
    activated_f, gelu_back = jax.vjp(partial(jax.nn.gelu, approximate=False), hidden)
    activated = activated_f.astype(jnp.bfloat16)
    mlp_out = jnp.dot(activated, proj_down, preferred_element_type=jnp.float32) + bias_down.astype(
        jnp.float32
    )
    outputs = (middle + mlp_out).astype(jnp.bfloat16)

    out_grad = cotangent[:, 0].reshape(rows, width)
    out_grad_f = out_grad.astype(jnp.float32)
    grad_down = outer_rows(activated, out_grad)
    grad_bias_down = jnp.sum(out_grad_f, axis=0)
    act_grad = times_transposed(out_grad, proj_down)
    (hidden_grad,) = gelu_back(act_grad)
    hidden_grad_b = hidden_grad.astype(jnp.bfloat16)
    grad_up = outer_rows(normed_two, hidden_grad_b)
    grad_bias_up = jnp.sum(hidden_grad_b.astype(jnp.float32), axis=0)
    normed_two_grad = times_transposed(hidden_grad_b, proj_up)
    middle_ln_grad, grad_gain_two, grad_shift_two = norm_two_back(normed_two_grad)
    middle_grad = out_grad_f + middle_ln_grad
    branch_grad = middle_grad.astype(jnp.bfloat16)
    grad_out = outer_rows(attended_b, branch_grad)
    grad_bias_out = jnp.sum(branch_grad.astype(jnp.float32), axis=0)
    attended_grad = times_transposed(branch_grad, proj_out).astype(jnp.bfloat16)

    if head_parallel:
        grad_units = rows_to_units(
            attended_grad.reshape(micro, row_count, 1, HEADS, HEAD), seq_count, per_device, 1
        )[:, :, 0]
        qkv_grad_u = unit_backward(uq, uk, uv, weights, totals, attended_u, grad_units)
        proj_grad = units_to_rows(qkv_grad_u, seq_count, micro, 3)
        backward_anchors = [None, grad_units, qkv_grad_u, proj_grad, proj_grad]
    else:
        proj_grad = fallback_attention_backward(saved, attended_grad, row_count)
        backward_anchors = [None] + [proj_grad] * (steps - 1)

    full_rows = count * shard_rows
    vec_one = vector_block(
        [grad_bias_up, grad_bias_down, grad_gain_two, grad_shift_two], full_rows, jnp.float32
    )
    red_up, red_down, red_mixed = reduce_routes(
        [grad_up, grad_down, jnp.concatenate([grad_out, vec_one], axis=1)],
        orders,
        count,
        me,
        backward_anchors[:steps],
    )
    red_out, red_vec_one = split_cols(red_mixed, [width, vec_one.shape[1]])

    grad_bias_query = jnp.sum(proj_grad[:, :width].astype(jnp.float32), axis=0)
    grad_bias_value = jnp.sum(proj_grad[:, 2 * width :].astype(jnp.float32), axis=0)
    grad_parts = split_cols(proj_grad, qkv_cols)
    grad_qkv = [outer_rows(normed, g) for g in grad_parts]
    normed_grad = times_transposed(grad_parts[0], qkv_weights[0])
    for g, w in zip(grad_parts[1:], qkv_weights[1:]):
        normed_grad = normed_grad + times_transposed(g, w)
    input_ln_grad, grad_gain_one, grad_shift_one = norm_one_back(normed_grad)
    input_grads = (middle_grad + input_ln_grad).astype(jnp.bfloat16)

    vec_two = vector_block(
        [grad_gain_one, grad_shift_one, grad_bias_query, grad_bias_value, grad_bias_out],
        full_rows,
        jnp.float32,
    )
    half = qkv_cols[1] // 2
    red = reduce_routes(
        [
            jnp.concatenate([grad_qkv[0], grad_qkv[1][:, :half]], axis=1),
            jnp.concatenate([grad_qkv[1][:, half:], grad_qkv[2], vec_two], axis=1),
        ],
        orders[:2],
        count,
        me,
    )
    red_last, red_vec_two = split_cols(
        red[1], [qkv_cols[1] - half + qkv_cols[2], vec_two.shape[1]]
    )
    red_qkv = jnp.concatenate([red[0], red_last], axis=1)
    r_bias_up, r_bias_down, r_gain_two, r_shift_two = vector_unblock(red_vec_one, [ratio, 1, 1, 1])
    r_gain_one, r_shift_one, r_bias_query, r_bias_value, r_bias_out = vector_unblock(
        red_vec_two, [1] * 5
    )
    reduced = (
        r_gain_one,
        r_shift_one,
        red_qkv,
        r_bias_query,
        r_bias_value,
        red_out,
        r_bias_out,
        r_gain_two,
        r_shift_two,
        red_up,
        r_bias_up,
        red_down,
        r_bias_down,
    )
    return (
        outputs.reshape(micro, 1, row_count, width),
        input_grads.reshape(micro, 1, row_count, width),
    ) + reduced


def solution(mesh):
    vec = P(ALL)
    mat = P(ALL, None)
    param_specs = (vec, vec, mat, vec, vec, mat, vec, vec, vec, mat, vec, mat, vec)
    return jax.shard_map(
        body,
        mesh=mesh,
        in_specs=(P(None, "dp", "seq", None), P(None, "dp", "seq", None), P(None, "dp", None, None))
        + param_specs,
        out_specs=(P(None, "dp", "seq", None), P(None, "dp", "seq", None)) + param_specs,
        check_vma=False,
    )
```

```python
from functools import partial

import jax
import jax.numpy as jnp
from jax import lax
from jax.sharding import PartitionSpec as P

HEADS = 12
HEAD = 64
EPSILON = 1e-05
ALL = ("dp", "seq")


def layer_norm(values, ln_gain, ln_shift):
    center = jnp.mean(values, axis=-1, keepdims=True)
    centered = values - center
    spread = jnp.mean(centered * centered, axis=-1, keepdims=True)
    return centered * lax.rsqrt(spread + EPSILON) * ln_gain + ln_shift


def piece_label(positions, bounds):
    inside = (positions[:, None] >= bounds[None, :, 0]) & (positions[:, None] < bounds[None, :, 1])
    labels = jnp.arange(1, bounds.shape[0] + 1, dtype=jnp.int32)
    return jnp.sum(jnp.where(inside, labels[None, :], 0), axis=1) - 1


def allowed_mask(query_pos, key_pos, bounds):
    query_label = piece_label(query_pos, bounds)
    key_label = piece_label(key_pos, bounds)
    causal = key_pos[None, :] <= query_pos[:, None]
    same_piece = (query_label[:, None] == key_label[None, :]) & (query_label[:, None] >= 0)
    return causal | same_piece


def outer_rows(left, right):
    return lax.dot_general(
        left, right, (((0,), (0,)), ((), ())), preferred_element_type=jnp.float32
    )


def times_transposed(left, right):
    return lax.dot_general(
        left, right, (((1,), (1,)), ((), ())), preferred_element_type=jnp.float32
    )


def route_orders(dp_size, seq_size):
    nbits = (dp_size * seq_size).bit_length() - 1
    if (dp_size, seq_size) == (4, 8):
        return [(3, 4, 0, 1, 2), (3, 0, 1, 4, 2), (3, 1, 4, 0, 2)]
    core = (seq_size.bit_length() - 1) if dp_size > 1 else None
    others = [b for b in range(nbits) if b != core]
    head = [core] if core is not None else []
    return [tuple(head + others[i:] + others[:i]) for i in range(3)]


def partner_pairs(count, bit):
    return [(i, i ^ (1 << bit)) for i in range(count)]


def tie(values, anchor):
    if anchor is None:
        return values
    values, _ = lax.optimization_barrier((values, anchor))
    return values


def gather_routes(routes, orders, count, me, anchors=None):
    nbits = count.bit_length() - 1
    idx = jnp.arange(count, dtype=jnp.int32)
    out = []
    for x, order in zip(routes, orders):
        rows, cols = x.shape
        for step, b in enumerate(reversed(order)):
            if anchors is not None:
                x = tie(x, anchors[step])
            got = lax.ppermute(x, ALL, partner_pairs(count, b))
            x = jnp.stack([x, got])
        rel = jnp.zeros((count,), jnp.int32)
        for j, b in enumerate(order):
            rel = rel + ((((idx >> b) & 1) ^ ((me >> b) & 1)) << (nbits - 1 - j))
        x = jnp.take(x.reshape(count, rows, cols), rel, axis=0)
        out.append(x.reshape(count * rows, cols))
    return out


def reduce_routes(routes, orders, count, me, anchors=None):
    nbits = count.bit_length() - 1
    out = []
    for x, order in zip(routes, orders):
        rows = x.shape[0] // count
        cols = x.shape[1]
        x = x.reshape([2] * nbits + [rows, cols])
        remaining = list(range(nbits - 1, -1, -1))
        for step, b in enumerate(order):
            if anchors is not None:
                x = tie(x, anchors[step])
            axis = remaining.index(b)
            mine = (me >> b) & 1
            keep = lax.dynamic_index_in_dim(x, mine, axis, keepdims=False)
            send = lax.dynamic_index_in_dim(x, 1 - mine, axis, keepdims=False).astype(jnp.bfloat16)
            got = lax.ppermute(send, ALL, partner_pairs(count, b))
            x = keep + got.astype(jnp.float32)
            remaining.pop(axis)
        out.append(x.reshape(rows, cols))
    return out


def split_cols(x, widths):
    out, at = [], 0
    for w in widths:
        out.append(x[:, at : at + w])
        at += w
    return out


def thirds(width, grain=128):
    first = -(-width // (3 * grain)) * grain
    return [first, first, width - 2 * first]


def vector_block(vectors, rows, dtype):
    cols = [v.reshape(rows, -1).astype(dtype) for v in vectors]
    used = sum(c.shape[1] for c in cols)
    pad = -(-used // 128) * 128 - used
    if pad:
        cols.append(jnp.zeros((rows, pad), dtype))
    return jnp.concatenate(cols, axis=1)


def vector_unblock(block, sizes):
    out, at = [], 0
    rows = block.shape[0]
    for s in sizes:
        out.append(block[:, at : at + s].reshape(rows * s))
        at += s
    return out


def unit_bounds(bounds, unit_count, per_device):
    first = lax.axis_index("seq") * per_device
    micro = (first + jnp.arange(per_device, dtype=jnp.int32)) // HEADS
    return bounds[:, 0][micro]


def unit_masks(ubounds, length):
    pos = jnp.arange(length, dtype=jnp.int32)
    return jax.vmap(lambda b: allowed_mask(pos, pos, b))(ubounds)


def rows_to_units(x, seq_count, per_device, parts):
    micro, rows = x.shape[0], x.shape[1]
    x = jnp.transpose(x, (0, 3, 1, 2, 4)).reshape(seq_count, per_device, rows, parts, HEAD)
    x = lax.all_to_all(x, "seq", 0, 0, tiled=True)
    x = jnp.transpose(x, (1, 0, 2, 3, 4))
    return x.reshape(per_device, seq_count * rows, parts, HEAD)


def units_to_rows(x, seq_count, micro, parts):
    per_device, length = x.shape[0], x.shape[1]
    rows = length // seq_count
    x = x.reshape(per_device, seq_count, rows, parts, HEAD)
    x = jnp.transpose(x, (1, 0, 2, 3, 4))
    x = lax.all_to_all(x, "seq", 0, 0, tiled=True)
    x = x.reshape(micro, HEADS, rows, parts, HEAD)
    x = jnp.transpose(x, (0, 2, 3, 1, 4))
    return x.reshape(micro * rows, parts * HEADS * HEAD)


def unit_forward(q, k, v, allowed):
    factor = q.shape[-1] ** (-0.5)
    scores = jnp.einsum("uqd,ukd->uqk", q, k, preferred_element_type=jnp.float32) * factor
    weights = jnp.where(allowed, jnp.exp(scores), 0.0)
    totals = jnp.sum(weights, axis=-1)
    summed = jnp.einsum(
        "uqk,ukd->uqd", weights.astype(jnp.bfloat16), v, preferred_element_type=jnp.float32
    )
    return weights, totals, summed / totals[:, :, None]


def unit_backward(q, k, v, weights, totals, attended, attended_grad):
    factor = q.shape[-1] ** (-0.5)
    grad_f = attended_grad.astype(jnp.float32)
    delta = jnp.sum(grad_f * attended, axis=-1) / totals
    summed_grad = (grad_f / totals[:, :, None]).astype(jnp.bfloat16)
    products = jnp.einsum("uqd,ukd->uqk", summed_grad, v, preferred_element_type=jnp.float32)
    score_grad = (weights * (products - delta[:, :, None])).astype(jnp.bfloat16)
    q_grad = jnp.einsum("uqk,ukd->uqd", score_grad, k, preferred_element_type=jnp.float32) * factor
    k_grad = jnp.einsum("uqk,uqd->ukd", score_grad, q, preferred_element_type=jnp.float32) * factor
    v_grad = jnp.einsum(
        "uqk,uqd->ukd", weights.astype(jnp.bfloat16), summed_grad, preferred_element_type=jnp.float32
    )
    return jnp.stack([q_grad, k_grad, v_grad], axis=2).astype(jnp.bfloat16)


def fallback_attention(queries, keys, values, bounds, row_count):
    micro = bounds.shape[0]
    seq_count = lax.axis_size("seq")
    total_len = row_count * seq_count
    query_pos = lax.axis_index("seq") * row_count + jnp.arange(row_count, dtype=jnp.int32)
    key_pos = jnp.arange(total_len, dtype=jnp.int32)
    saved = []
    attended_all = []
    for m in range(micro):
        sl = slice(m * row_count, (m + 1) * row_count)
        qh = queries[sl].reshape(row_count, HEADS, HEAD)
        k_all = lax.all_gather(keys[sl], "seq", axis=0, tiled=True).reshape(total_len, HEADS, HEAD)
        v_all = lax.all_gather(values[sl], "seq", axis=0, tiled=True).reshape(total_len, HEADS, HEAD)
        allowed = allowed_mask(query_pos, key_pos, bounds[m, 0])
        scores = jnp.einsum("rhd,khd->hrk", qh, k_all, preferred_element_type=jnp.float32) * HEAD ** (-0.5)
        weights = jnp.where(allowed[None], jnp.exp(scores), 0.0)
        totals = jnp.sum(weights, axis=-1)
        summed = jnp.einsum(
            "hrk,khd->rhd", weights.astype(jnp.bfloat16), v_all, preferred_element_type=jnp.float32
        )
        attended = summed / totals.T[:, :, None]
        saved.append((qh, k_all, v_all, weights, totals, attended))
        attended_all.append(attended.reshape(row_count, HEADS * HEAD))
    return jnp.concatenate(attended_all, axis=0), saved


def fallback_attention_backward(saved, attended_grad, row_count):
    factor = HEAD ** (-0.5)
    proj = []
    for m, (qh, k_all, v_all, weights, totals, attended) in enumerate(saved):
        grad = attended_grad[m * row_count : (m + 1) * row_count].astype(jnp.float32)
        grad = grad.reshape(row_count, HEADS, HEAD)
        delta = jnp.sum(grad * attended, axis=-1).T / totals
        grad_heads = (grad / totals.T[:, :, None]).astype(jnp.bfloat16)
        products = jnp.einsum("rhd,khd->hrk", grad_heads, v_all, preferred_element_type=jnp.float32)
        score_grad = (weights * (products - delta[:, :, None])).astype(jnp.bfloat16)
        q_grad = jnp.einsum("hrk,khd->rhd", score_grad, k_all, preferred_element_type=jnp.float32) * factor
        k_rows = jnp.einsum("hrk,rhd->khd", score_grad, qh, preferred_element_type=jnp.float32) * factor
        v_rows = jnp.einsum(
            "hrk,rhd->khd", weights.astype(jnp.bfloat16), grad_heads, preferred_element_type=jnp.float32
        )
        width = HEADS * HEAD
        k_own = lax.psum_scatter(
            k_rows.reshape(-1, width).astype(jnp.bfloat16), "seq", scatter_dimension=0, tiled=True
        )
        v_own = lax.psum_scatter(
            v_rows.reshape(-1, width).astype(jnp.bfloat16), "seq", scatter_dimension=0, tiled=True
        )
        proj.append(
            jnp.concatenate(
                [q_grad.reshape(row_count, width).astype(jnp.bfloat16), k_own, v_own], axis=1
            )
        )
    return jnp.concatenate(proj, axis=0)


def body(inputs, cotangent, bounds, *shards):
    micro = inputs.shape[0]
    row_count = inputs.shape[2]
    width = inputs.shape[3]
    ff = shards[9].shape[1]
    rows = micro * row_count
    seq_count = lax.axis_size("seq")
    unit_count = micro * HEADS
    head_parallel = unit_count % seq_count == 0
    per_device = unit_count // seq_count
    dp_count = lax.axis_size("dp")
    count = dp_count * seq_count
    me = lax.axis_index("dp") * seq_count + lax.axis_index("seq")
    orders = route_orders(dp_count, seq_count)
    steps = len(orders[0])
    ln1_g, ln1_b, w_qkv, b_q, b_v, w_out, b_out, ln2_g, ln2_b, w_up, b_up, w_down, b_down = shards
    shard_rows = w_qkv.shape[0]
    ratio = ff // width
    vec_sizes = [1] * 8 + [ratio]
    vecs_local = vector_block(
        [ln1_g, ln1_b, b_q, b_v, b_out, ln2_g, ln2_b, b_down, b_up], shard_rows, jnp.bfloat16
    )
    mlp_pack = jnp.concatenate([w_out, w_up, w_down.reshape(shard_rows, ratio * width)], axis=1)
    qkv_total = w_qkv.shape[1]
    split_at = qkv_total // 2
    gathered = gather_routes(
        [w_qkv[:, :split_at], jnp.concatenate([w_qkv[:, split_at:], vecs_local], axis=1)],
        orders[:2],
        count,
        me,
    )
    qkv_second, vecs_all = split_cols(gathered[1], [qkv_total - split_at, vecs_local.shape[1]])
    qkv_weights = [gathered[0], qkv_second]
    (
        gain_one,
        shift_one,
        bias_query,
        bias_value,
        bias_out,
        gain_two,
        shift_two,
        bias_down,
        bias_up,
    ) = vector_unblock(vecs_all, vec_sizes)

    seq_in = inputs[:, 0].reshape(rows, width).astype(jnp.float32)
    normed_f, norm_one_back = jax.vjp(
        layer_norm, seq_in, gain_one.astype(jnp.float32), shift_one.astype(jnp.float32)
    )
    normed = normed_f.astype(jnp.bfloat16)
    projected = jnp.concatenate(
        [jnp.dot(normed, w, preferred_element_type=jnp.float32) for w in qkv_weights], axis=1
    )
    proj_q, proj_k, proj_v = split_cols(projected, [width] * 3)
    queries = (proj_q + bias_query.astype(jnp.float32)).astype(jnp.bfloat16)
    keys_now = proj_k.astype(jnp.bfloat16)
    values_now = (proj_v + bias_value.astype(jnp.float32)).astype(jnp.bfloat16)

    if head_parallel:
        qkv_rows = jnp.concatenate([queries, keys_now, values_now], axis=1)
        qkv_units = rows_to_units(
            qkv_rows.reshape(micro, row_count, 3, HEADS, HEAD), seq_count, per_device, 3
        )
        uq, uk, uv = qkv_units[:, :, 0], qkv_units[:, :, 1], qkv_units[:, :, 2]
        allowed = unit_masks(unit_bounds(bounds, unit_count, per_device), seq_count * row_count)
        weights, totals, attended_u = unit_forward(uq, uk, uv, allowed)
        attended_b = units_to_rows(
            attended_u.astype(jnp.bfloat16)[:, :, None], seq_count, micro, 1
        )
        forward_anchors = [normed, qkv_units, weights, attended_u, attended_u]
    else:
        attended, saved = fallback_attention(queries, keys_now, values_now, bounds, row_count)
        attended_b = attended.astype(jnp.bfloat16)
        forward_anchors = [queries] + [attended] * (steps - 1)

    proj_out, proj_up, down_view = split_cols(
        lax.all_gather(mlp_pack, ALL, axis=0, tiled=True), [width, ff, ff]
    )
    proj_down = down_view.reshape(count * shard_rows * ratio, width)

    branch = jnp.dot(attended_b, proj_out, preferred_element_type=jnp.float32) + bias_out.astype(
        jnp.float32
    )
    middle = seq_in + branch
    normed_two_f, norm_two_back = jax.vjp(
        layer_norm, middle, gain_two.astype(jnp.float32), shift_two.astype(jnp.float32)
    )
    normed_two = normed_two_f.astype(jnp.bfloat16)
    hidden = jnp.dot(normed_two, proj_up, preferred_element_type=jnp.float32) + bias_up.astype(
        jnp.float32
    )
    activated_f, gelu_back = jax.vjp(partial(jax.nn.gelu, approximate=False), hidden)
    activated = activated_f.astype(jnp.bfloat16)
    mlp_out = jnp.dot(activated, proj_down, preferred_element_type=jnp.float32) + bias_down.astype(
        jnp.float32
    )
    outputs = (middle + mlp_out).astype(jnp.bfloat16)

    out_grad = cotangent[:, 0].reshape(rows, width)
    out_grad_f = out_grad.astype(jnp.float32)
    grad_down = outer_rows(activated, out_grad)
    grad_bias_down = jnp.sum(out_grad_f, axis=0)
    act_grad = times_transposed(out_grad, proj_down)
    (hidden_grad,) = gelu_back(act_grad)
    hidden_grad_b = hidden_grad.astype(jnp.bfloat16)
    grad_up = outer_rows(normed_two, hidden_grad_b)
    grad_bias_up = jnp.sum(hidden_grad_b.astype(jnp.float32), axis=0)
    normed_two_grad = times_transposed(hidden_grad_b, proj_up)
    middle_ln_grad, grad_gain_two, grad_shift_two = norm_two_back(normed_two_grad)
    middle_grad = out_grad_f + middle_ln_grad
    branch_grad = middle_grad.astype(jnp.bfloat16)
    grad_out = outer_rows(attended_b, branch_grad)
    grad_bias_out = jnp.sum(branch_grad.astype(jnp.float32), axis=0)
    attended_grad = times_transposed(branch_grad, proj_out).astype(jnp.bfloat16)

    if head_parallel:
        grad_units = rows_to_units(
            attended_grad.reshape(micro, row_count, 1, HEADS, HEAD), seq_count, per_device, 1
        )[:, :, 0]
        qkv_grad_u = unit_backward(uq, uk, uv, weights, totals, attended_u, grad_units)
        proj_grad = units_to_rows(qkv_grad_u, seq_count, micro, 3)
        backward_anchors = [None, grad_units, qkv_grad_u, proj_grad, proj_grad]
    else:
        proj_grad = fallback_attention_backward(saved, attended_grad, row_count)
        backward_anchors = [None] + [proj_grad] * (steps - 1)

    full_rows = count * shard_rows
    vec_one = vector_block(
        [grad_bias_up, grad_bias_down, grad_gain_two, grad_shift_two], full_rows, jnp.float32
    )
    red_up, red_down, red_mixed = reduce_routes(
        [grad_up, grad_down, jnp.concatenate([grad_out, vec_one], axis=1)],
        orders,
        count,
        me,
        backward_anchors[:steps],
    )
    red_out, red_vec_one = split_cols(red_mixed, [width, vec_one.shape[1]])

    grad_bias_query = jnp.sum(proj_grad[:, :width].astype(jnp.float32), axis=0)
    grad_bias_value = jnp.sum(proj_grad[:, 2 * width :].astype(jnp.float32), axis=0)
    grad_parts = split_cols(proj_grad, [split_at, qkv_total - split_at])
    grad_qkv = [outer_rows(normed, g) for g in grad_parts]
    normed_grad = times_transposed(grad_parts[0], qkv_weights[0]) + times_transposed(
        grad_parts[1], qkv_weights[1]
    )
    input_ln_grad, grad_gain_one, grad_shift_one = norm_one_back(normed_grad)
    input_grads = (middle_grad + input_ln_grad).astype(jnp.bfloat16)

    vec_two = vector_block(
        [grad_gain_one, grad_shift_one, grad_bias_query, grad_bias_value, grad_bias_out],
        full_rows,
        jnp.float32,
    )
    red = reduce_routes(
        [grad_qkv[0], jnp.concatenate([grad_qkv[1], vec_two], axis=1)],
        orders[:2],
        count,
        me,
    )
    red_last, red_vec_two = split_cols(red[1], [qkv_total - split_at, vec_two.shape[1]])
    red_qkv = jnp.concatenate([red[0], red_last], axis=1)
    r_bias_up, r_bias_down, r_gain_two, r_shift_two = vector_unblock(red_vec_one, [ratio, 1, 1, 1])
    r_gain_one, r_shift_one, r_bias_query, r_bias_value, r_bias_out = vector_unblock(
        red_vec_two, [1] * 5
    )
    reduced = (
        r_gain_one,
        r_shift_one,
        red_qkv,
        r_bias_query,
        r_bias_value,
        red_out,
        r_bias_out,
        r_gain_two,
        r_shift_two,
        red_up,
        r_bias_up,
        red_down,
        r_bias_down,
    )
    return (
        outputs.reshape(micro, 1, row_count, width),
        input_grads.reshape(micro, 1, row_count, width),
    ) + reduced


def solution(mesh):
    vec = P(ALL)
    mat = P(ALL, None)
    param_specs = (vec, vec, mat, vec, vec, mat, vec, vec, vec, mat, vec, mat, vec)
    return jax.shard_map(
        body,
        mesh=mesh,
        in_specs=(P(None, "dp", "seq", None), P(None, "dp", "seq", None), P(None, "dp", None, None))
        + param_specs,
        out_specs=(P(None, "dp", "seq", None), P(None, "dp", "seq", None)) + param_specs,
        check_vma=False,
    )
```

```python
from functools import partial

import jax
import jax.numpy as jnp
from jax import lax
from jax.sharding import PartitionSpec as P

HEADS = 12
HEAD = 64
EPSILON = 1e-05
ALL = ("dp", "seq")


def layer_norm(values, ln_gain, ln_shift):
    center = jnp.mean(values, axis=-1, keepdims=True)
    centered = values - center
    spread = jnp.mean(centered * centered, axis=-1, keepdims=True)
    return centered * lax.rsqrt(spread + EPSILON) * ln_gain + ln_shift


def piece_label(positions, bounds):
    inside = (positions[:, None] >= bounds[None, :, 0]) & (positions[:, None] < bounds[None, :, 1])
    labels = jnp.arange(1, bounds.shape[0] + 1, dtype=jnp.int32)
    return jnp.sum(jnp.where(inside, labels[None, :], 0), axis=1) - 1


def allowed_mask(query_pos, key_pos, bounds):
    query_label = piece_label(query_pos, bounds)
    key_label = piece_label(key_pos, bounds)
    causal = key_pos[None, :] <= query_pos[:, None]
    same_piece = (query_label[:, None] == key_label[None, :]) & (query_label[:, None] >= 0)
    return causal | same_piece


def outer_rows(left, right):
    return lax.dot_general(
        left, right, (((0,), (0,)), ((), ())), preferred_element_type=jnp.float32
    )


def times_transposed(left, right):
    return lax.dot_general(
        left, right, (((1,), (1,)), ((), ())), preferred_element_type=jnp.float32
    )


def route_orders(dp_size, seq_size):
    nbits = (dp_size * seq_size).bit_length() - 1
    if (dp_size, seq_size) == (4, 8):
        return [(3, 4, 0, 1, 2), (3, 0, 1, 4, 2), (3, 1, 4, 0, 2)]
    core = (seq_size.bit_length() - 1) if dp_size > 1 else None
    others = [b for b in range(nbits) if b != core]
    head = [core] if core is not None else []
    return [tuple(head + others[i:] + others[:i]) for i in range(3)]


def partner_pairs(count, bit):
    return [(i, i ^ (1 << bit)) for i in range(count)]


def tie(values, anchor):
    if anchor is None:
        return values
    values, _ = lax.optimization_barrier((values, anchor))
    return values


def gather_routes(routes, orders, count, me, anchors=None):
    nbits = count.bit_length() - 1
    idx = jnp.arange(count, dtype=jnp.int32)
    out = []
    for x, order in zip(routes, orders):
        rows, cols = x.shape
        for step, b in enumerate(reversed(order)):
            if anchors is not None:
                x = tie(x, anchors[step])
            got = lax.ppermute(x, ALL, partner_pairs(count, b))
            x = jnp.stack([x, got])
        rel = jnp.zeros((count,), jnp.int32)
        for j, b in enumerate(order):
            rel = rel + ((((idx >> b) & 1) ^ ((me >> b) & 1)) << (nbits - 1 - j))
        x = jnp.take(x.reshape(count, rows, cols), rel, axis=0)
        out.append(x.reshape(count * rows, cols))
    return out


def reduce_routes(routes, orders, count, me, anchors=None):
    nbits = count.bit_length() - 1
    out = []
    for x, order in zip(routes, orders):
        rows = x.shape[0] // count
        cols = x.shape[1]
        x = x.reshape([2] * nbits + [rows, cols])
        remaining = list(range(nbits - 1, -1, -1))
        for step, b in enumerate(order):
            if anchors is not None:
                x = tie(x, anchors[step])
            axis = remaining.index(b)
            mine = (me >> b) & 1
            keep = lax.dynamic_index_in_dim(x, mine, axis, keepdims=False)
            send = lax.dynamic_index_in_dim(x, 1 - mine, axis, keepdims=False).astype(jnp.bfloat16)
            got = lax.ppermute(send, ALL, partner_pairs(count, b))
            x = keep + got.astype(jnp.float32)
            remaining.pop(axis)
        out.append(x.reshape(rows, cols))
    return out


def split_cols(x, widths):
    out, at = [], 0
    for w in widths:
        out.append(x[:, at : at + w])
        at += w
    return out


def thirds(width, grain=128):
    first = -(-width // (3 * grain)) * grain
    return [first, first, width - 2 * first]


def vector_block(vectors, rows, dtype):
    cols = [v.reshape(rows, -1).astype(dtype) for v in vectors]
    used = sum(c.shape[1] for c in cols)
    pad = -(-used // 128) * 128 - used
    if pad:
        cols.append(jnp.zeros((rows, pad), dtype))
    return jnp.concatenate(cols, axis=1)


def vector_unblock(block, sizes):
    out, at = [], 0
    rows = block.shape[0]
    for s in sizes:
        out.append(block[:, at : at + s].reshape(rows * s))
        at += s
    return out


def unit_bounds(bounds, unit_count, per_device):
    first = lax.axis_index("seq") * per_device
    micro = (first + jnp.arange(per_device, dtype=jnp.int32)) // HEADS
    return bounds[:, 0][micro]


def unit_masks(ubounds, length):
    pos = jnp.arange(length, dtype=jnp.int32)
    return jax.vmap(lambda b: allowed_mask(pos, pos, b))(ubounds)


def rows_to_units(x, seq_count, per_device, parts):
    micro, rows = x.shape[0], x.shape[1]
    x = jnp.transpose(x, (0, 3, 1, 2, 4)).reshape(seq_count, per_device, rows, parts, HEAD)
    x = lax.all_to_all(x, "seq", 0, 0, tiled=True)
    x = jnp.transpose(x, (1, 0, 2, 3, 4))
    return x.reshape(per_device, seq_count * rows, parts, HEAD)


def units_to_rows(x, seq_count, micro, parts):
    per_device, length = x.shape[0], x.shape[1]
    rows = length // seq_count
    x = x.reshape(per_device, seq_count, rows, parts, HEAD)
    x = jnp.transpose(x, (1, 0, 2, 3, 4))
    x = lax.all_to_all(x, "seq", 0, 0, tiled=True)
    x = x.reshape(micro, HEADS, rows, parts, HEAD)
    x = jnp.transpose(x, (0, 2, 3, 1, 4))
    return x.reshape(micro * rows, parts * HEADS * HEAD)


def unit_forward(q, k, v, allowed):
    factor = q.shape[-1] ** (-0.5)
    scores = jnp.einsum("uqd,ukd->uqk", q, k, preferred_element_type=jnp.float32) * factor
    weights = jnp.where(allowed, jnp.exp(scores), 0.0)
    totals = jnp.sum(weights, axis=-1)
    summed = jnp.einsum(
        "uqk,ukd->uqd", weights.astype(jnp.bfloat16), v, preferred_element_type=jnp.float32
    )
    return weights, totals, summed / totals[:, :, None]


def unit_backward(q, k, v, weights, totals, attended, attended_grad):
    factor = q.shape[-1] ** (-0.5)
    grad_f = attended_grad.astype(jnp.float32)
    delta = jnp.sum(grad_f * attended, axis=-1) / totals
    summed_grad = (grad_f / totals[:, :, None]).astype(jnp.bfloat16)
    products = jnp.einsum("uqd,ukd->uqk", summed_grad, v, preferred_element_type=jnp.float32)
    score_grad = (weights * (products - delta[:, :, None])).astype(jnp.bfloat16)
    q_grad = jnp.einsum("uqk,ukd->uqd", score_grad, k, preferred_element_type=jnp.float32) * factor
    k_grad = jnp.einsum("uqk,uqd->ukd", score_grad, q, preferred_element_type=jnp.float32) * factor
    v_grad = jnp.einsum(
        "uqk,uqd->ukd", weights.astype(jnp.bfloat16), summed_grad, preferred_element_type=jnp.float32
    )
    return jnp.stack([q_grad, k_grad, v_grad], axis=2).astype(jnp.bfloat16)


def fallback_attention(queries, keys, values, bounds, row_count):
    micro = bounds.shape[0]
    seq_count = lax.axis_size("seq")
    total_len = row_count * seq_count
    query_pos = lax.axis_index("seq") * row_count + jnp.arange(row_count, dtype=jnp.int32)
    key_pos = jnp.arange(total_len, dtype=jnp.int32)
    saved = []
    attended_all = []
    for m in range(micro):
        sl = slice(m * row_count, (m + 1) * row_count)
        qh = queries[sl].reshape(row_count, HEADS, HEAD)
        k_all = lax.all_gather(keys[sl], "seq", axis=0, tiled=True).reshape(total_len, HEADS, HEAD)
        v_all = lax.all_gather(values[sl], "seq", axis=0, tiled=True).reshape(total_len, HEADS, HEAD)
        allowed = allowed_mask(query_pos, key_pos, bounds[m, 0])
        scores = jnp.einsum("rhd,khd->hrk", qh, k_all, preferred_element_type=jnp.float32) * HEAD ** (-0.5)
        weights = jnp.where(allowed[None], jnp.exp(scores), 0.0)
        totals = jnp.sum(weights, axis=-1)
        summed = jnp.einsum(
            "hrk,khd->rhd", weights.astype(jnp.bfloat16), v_all, preferred_element_type=jnp.float32
        )
        attended = summed / totals.T[:, :, None]
        saved.append((qh, k_all, v_all, weights, totals, attended))
        attended_all.append(attended.reshape(row_count, HEADS * HEAD))
    return jnp.concatenate(attended_all, axis=0), saved


def fallback_attention_backward(saved, attended_grad, row_count):
    factor = HEAD ** (-0.5)
    proj = []
    for m, (qh, k_all, v_all, weights, totals, attended) in enumerate(saved):
        grad = attended_grad[m * row_count : (m + 1) * row_count].astype(jnp.float32)
        grad = grad.reshape(row_count, HEADS, HEAD)
        delta = jnp.sum(grad * attended, axis=-1).T / totals
        grad_heads = (grad / totals.T[:, :, None]).astype(jnp.bfloat16)
        products = jnp.einsum("rhd,khd->hrk", grad_heads, v_all, preferred_element_type=jnp.float32)
        score_grad = (weights * (products - delta[:, :, None])).astype(jnp.bfloat16)
        q_grad = jnp.einsum("hrk,khd->rhd", score_grad, k_all, preferred_element_type=jnp.float32) * factor
        k_rows = jnp.einsum("hrk,rhd->khd", score_grad, qh, preferred_element_type=jnp.float32) * factor
        v_rows = jnp.einsum(
            "hrk,rhd->khd", weights.astype(jnp.bfloat16), grad_heads, preferred_element_type=jnp.float32
        )
        width = HEADS * HEAD
        k_own = lax.psum_scatter(
            k_rows.reshape(-1, width).astype(jnp.bfloat16), "seq", scatter_dimension=0, tiled=True
        )
        v_own = lax.psum_scatter(
            v_rows.reshape(-1, width).astype(jnp.bfloat16), "seq", scatter_dimension=0, tiled=True
        )
        proj.append(
            jnp.concatenate(
                [q_grad.reshape(row_count, width).astype(jnp.bfloat16), k_own, v_own], axis=1
            )
        )
    return jnp.concatenate(proj, axis=0)


def body(inputs, cotangent, bounds, *shards):
    micro = inputs.shape[0]
    row_count = inputs.shape[2]
    width = inputs.shape[3]
    ff = shards[9].shape[1]
    rows = micro * row_count
    seq_count = lax.axis_size("seq")
    unit_count = micro * HEADS
    head_parallel = unit_count % seq_count == 0
    per_device = unit_count // seq_count
    dp_count = lax.axis_size("dp")
    count = dp_count * seq_count
    me = lax.axis_index("dp") * seq_count + lax.axis_index("seq")
    orders = route_orders(dp_count, seq_count)
    steps = len(orders[0])
    ln1_g, ln1_b, w_qkv, b_q, b_v, w_out, b_out, ln2_g, ln2_b, w_up, b_up, w_down, b_down = shards
    shard_rows = w_qkv.shape[0]
    ratio = ff // width
    vec_sizes = [1] * 8 + [ratio]
    vecs_local = vector_block(
        [ln1_g, ln1_b, b_q, b_v, b_out, ln2_g, ln2_b, b_down, b_up], shard_rows, jnp.bfloat16
    )
    mlp_pack = jnp.concatenate([w_out, w_up, w_down.reshape(shard_rows, ratio * width)], axis=1)
    qkv_total = w_qkv.shape[1]
    split_at = qkv_total // 2
    gathered = gather_routes(
        [w_qkv[:, :split_at], jnp.concatenate([w_qkv[:, split_at:], vecs_local], axis=1)],
        orders[:2],
        count,
        me,
    )
    qkv_second, vecs_all = split_cols(gathered[1], [qkv_total - split_at, vecs_local.shape[1]])
    qkv_weights = [gathered[0], qkv_second]
    (
        gain_one,
        shift_one,
        bias_query,
        bias_value,
        bias_out,
        gain_two,
        shift_two,
        bias_down,
        bias_up,
    ) = vector_unblock(vecs_all, vec_sizes)

    seq_in = inputs[:, 0].reshape(rows, width).astype(jnp.float32)
    normed_f, norm_one_back = jax.vjp(
        layer_norm, seq_in, gain_one.astype(jnp.float32), shift_one.astype(jnp.float32)
    )
    normed = normed_f.astype(jnp.bfloat16)
    projected = jnp.concatenate(
        [jnp.dot(normed, w, preferred_element_type=jnp.float32) for w in qkv_weights], axis=1
    )
    proj_q, proj_k, proj_v = split_cols(projected, [width] * 3)
    queries = (proj_q + bias_query.astype(jnp.float32)).astype(jnp.bfloat16)
    keys_now = proj_k.astype(jnp.bfloat16)
    values_now = (proj_v + bias_value.astype(jnp.float32)).astype(jnp.bfloat16)

    if head_parallel:
        qkv_rows = jnp.concatenate([queries, keys_now, values_now], axis=1)
        qkv_units = rows_to_units(
            qkv_rows.reshape(micro, row_count, 3, HEADS, HEAD), seq_count, per_device, 3
        )
        uq, uk, uv = qkv_units[:, :, 0], qkv_units[:, :, 1], qkv_units[:, :, 2]
        allowed = unit_masks(unit_bounds(bounds, unit_count, per_device), seq_count * row_count)
        weights, totals, attended_u = unit_forward(uq, uk, uv, allowed)
        attended_b = units_to_rows(
            attended_u.astype(jnp.bfloat16)[:, :, None], seq_count, micro, 1
        )
        forward_anchors = [normed, qkv_units, weights, attended_u, attended_u]
    else:
        attended, saved = fallback_attention(queries, keys_now, values_now, bounds, row_count)
        attended_b = attended.astype(jnp.bfloat16)
        forward_anchors = [queries] + [attended] * (steps - 1)

    proj_out, proj_up, down_view = split_cols(
        lax.all_gather(mlp_pack, ALL, axis=0, tiled=True), [width, ff, ff]
    )
    proj_down = down_view.reshape(count * shard_rows * ratio, width)

    branch = jnp.dot(attended_b, proj_out, preferred_element_type=jnp.float32) + bias_out.astype(
        jnp.float32
    )
    middle = seq_in + branch
    normed_two_f, norm_two_back = jax.vjp(
        layer_norm, middle, gain_two.astype(jnp.float32), shift_two.astype(jnp.float32)
    )
    normed_two = normed_two_f.astype(jnp.bfloat16)
    hidden = jnp.dot(normed_two, proj_up, preferred_element_type=jnp.float32) + bias_up.astype(
        jnp.float32
    )
    activated_f, gelu_back = jax.vjp(partial(jax.nn.gelu, approximate=False), hidden)
    activated = activated_f.astype(jnp.bfloat16)
    mlp_out = jnp.dot(activated, proj_down, preferred_element_type=jnp.float32) + bias_down.astype(
        jnp.float32
    )
    outputs = (middle + mlp_out).astype(jnp.bfloat16)

    out_grad = cotangent[:, 0].reshape(rows, width)
    out_grad_f = out_grad.astype(jnp.float32)
    grad_down = outer_rows(activated, out_grad)
    grad_bias_down = jnp.sum(out_grad_f, axis=0)
    act_grad = times_transposed(out_grad, proj_down)
    (hidden_grad,) = gelu_back(act_grad)
    hidden_grad_b = hidden_grad.astype(jnp.bfloat16)
    grad_up = outer_rows(normed_two, hidden_grad_b)
    grad_bias_up = jnp.sum(hidden_grad_b.astype(jnp.float32), axis=0)
    normed_two_grad = times_transposed(hidden_grad_b, proj_up)
    middle_ln_grad, grad_gain_two, grad_shift_two = norm_two_back(normed_two_grad)
    middle_grad = out_grad_f + middle_ln_grad
    branch_grad = middle_grad.astype(jnp.bfloat16)
    grad_out = outer_rows(attended_b, branch_grad)
    grad_bias_out = jnp.sum(branch_grad.astype(jnp.float32), axis=0)
    attended_grad = times_transposed(branch_grad, proj_out).astype(jnp.bfloat16)

    if head_parallel:
        grad_units = rows_to_units(
            attended_grad.reshape(micro, row_count, 1, HEADS, HEAD), seq_count, per_device, 1
        )[:, :, 0]
        qkv_grad_u = unit_backward(uq, uk, uv, weights, totals, attended_u, grad_units)
        proj_grad = units_to_rows(qkv_grad_u, seq_count, micro, 3)
        backward_anchors = [None, grad_units, qkv_grad_u, proj_grad, proj_grad]
    else:
        proj_grad = fallback_attention_backward(saved, attended_grad, row_count)
        backward_anchors = [None] + [proj_grad] * (steps - 1)

    full_rows = count * shard_rows
    vec_one = vector_block(
        [grad_bias_up, grad_bias_down, grad_gain_two, grad_shift_two], full_rows, jnp.float32
    )
    up_keep = ff - ff // 4
    red_up_a, red_down, red_mixed = reduce_routes(
        [grad_up[:, :up_keep], grad_down, jnp.concatenate([grad_out, vec_one, grad_up[:, up_keep:]], axis=1)],
        orders,
        count,
        me,
        backward_anchors[:steps],
    )
    red_out, red_vec_one, red_up_b = split_cols(red_mixed, [width, vec_one.shape[1], ff - up_keep])
    red_up = jnp.concatenate([red_up_a, red_up_b], axis=1)

    grad_bias_query = jnp.sum(proj_grad[:, :width].astype(jnp.float32), axis=0)
    grad_bias_value = jnp.sum(proj_grad[:, 2 * width :].astype(jnp.float32), axis=0)
    grad_parts = split_cols(proj_grad, [split_at, qkv_total - split_at])
    grad_qkv = [outer_rows(normed, g) for g in grad_parts]
    normed_grad = times_transposed(grad_parts[0], qkv_weights[0]) + times_transposed(
        grad_parts[1], qkv_weights[1]
    )
    input_ln_grad, grad_gain_one, grad_shift_one = norm_one_back(normed_grad)
    input_grads = (middle_grad + input_ln_grad).astype(jnp.bfloat16)

    vec_two = vector_block(
        [grad_gain_one, grad_shift_one, grad_bias_query, grad_bias_value, grad_bias_out],
        full_rows,
        jnp.float32,
    )
    red = reduce_routes(
        [grad_qkv[0], jnp.concatenate([grad_qkv[1], vec_two], axis=1)],
        orders[:2],
        count,
        me,
    )
    red_last, red_vec_two = split_cols(red[1], [qkv_total - split_at, vec_two.shape[1]])
    red_qkv = jnp.concatenate([red[0], red_last], axis=1)
    r_bias_up, r_bias_down, r_gain_two, r_shift_two = vector_unblock(red_vec_one, [ratio, 1, 1, 1])
    r_gain_one, r_shift_one, r_bias_query, r_bias_value, r_bias_out = vector_unblock(
        red_vec_two, [1] * 5
    )
    reduced = (
        r_gain_one,
        r_shift_one,
        red_qkv,
        r_bias_query,
        r_bias_value,
        red_out,
        r_bias_out,
        r_gain_two,
        r_shift_two,
        red_up,
        r_bias_up,
        red_down,
        r_bias_down,
    )
    return (
        outputs.reshape(micro, 1, row_count, width),
        input_grads.reshape(micro, 1, row_count, width),
    ) + reduced


def solution(mesh):
    vec = P(ALL)
    mat = P(ALL, None)
    param_specs = (vec, vec, mat, vec, vec, mat, vec, vec, vec, mat, vec, mat, vec)
    return jax.shard_map(
        body,
        mesh=mesh,
        in_specs=(P(None, "dp", "seq", None), P(None, "dp", "seq", None), P(None, "dp", None, None))
        + param_specs,
        out_specs=(P(None, "dp", "seq", None), P(None, "dp", "seq", None)) + param_specs,
        check_vma=False,
    )
```
